32 devices in a mesh: band: 2 (over y), domain: 16 (over z, x, core).
Axes of the slice: x: 2, y: 2, z: 4, core: 2. Of those that a mesh axis runs over, the one named last changes fastest.
Arguments:
- orbitals: bfloat16 [128, 16, 32, 256], P('domain', None, None, 'band'), may hold values from -12 to 12
- potential: float32 [128, 16, 32], P('domain'), may hold values from -2 to 0
Outputs:
- filtered: bfloat16 [128, 16, 32, 256], P('domain', None, None, 'band')
- correlation: float32 [256, 256], P('band')
- projected: float32 [256, 256], P('band')
The draws below stay inside these ranges and needn't reach their ends.
All inputs are finite; a program needn't handle non-finite values.
Results may differ from the reference program's by a relative error of at most 0.005.
Values may be sent and summed in bfloat16 or wider, within the bound.
No kernel may reach another device: no remote copies, remote signals or barrier semaphores. Data moves between devices by JAX's collectives and lax.ppermute only.
A program may use at most 64 MiB of HBM per device.

```python
from functools import partial
import jax
import jax.numpy as jnp
from jax import lax

RADIUS = 4
NY = 16
NZ = 32
NX = 128
NORB = 256


def with_spikes(entries, rng, source, target, shards_of, factor):
    owner, partner = [(jnp.arange(entries.shape[position]) // (entries.shape[position] // shards_of)).reshape([-1 if axis == position else 1 for axis in range(entries.ndim)]) for position in (source, target)]
    chosen = jax.random.permutation(rng, shards_of)[partner]
    strong = (owner == chosen) | (owner == (partner + shards_of // 2) % shards_of)
    return jnp.where(strong, factor * entries, entries)


def level_of(stream_key, shape, split, smallest, high):
    def one(dim, parts):
        steps = jax.random.uniform(jax.random.fold_in(jax.random.fold_in(stream_key, 6), dim), (parts,), jnp.float32, smallest / len(split), high / len(split))
        return jnp.repeat(jnp.exp(steps), shape[dim] // parts).reshape((-1,) + (1,) * (len(shape) - dim - 1))

    gain = one(*split[0])
    for cut in split[1:]:
        gain = gain * one(*cut)
    return gain


def heavy_noise(key, dims, width, reach, shards, heavy, dtype=jnp.bfloat16):
    drawn = width * jax.random.normal(key, dims, jnp.float32)
    if shards:
        drawn = drawn * level_of(key, dims, shards, -0.22, 0.18)
    return jnp.clip(with_spikes(drawn, jax.random.fold_in(key, 3), *heavy), -reach, reach).astype(dtype)


def setup_inputs(seed: int = 0) -> dict:
    key_list = jax.random.split(jax.random.key(seed), 3)
    orbitals = heavy_noise(key_list[0], (NX, NY, NZ, NORB), 2.0, 12.0, ((0, 16), (3, 2)), (0, 3, 16, 2.0))
    potential = jnp.clip(-2.0 + 2.0 * jax.random.uniform(key_list[1], (NX, NY, NZ), jnp.float32) ** level_of(key_list[1], (NX, NY, NZ), ((0, 16),), -0.2, 0.2), -2.0, 0.0)
    return {"orbitals": orbitals, "potential": potential}


stencil_weights = (-205.0 / 72.0, 8.0 / 5.0, -1.0 / 5.0, 8.0 / 315.0, -1.0 / 560.0)
spectrum_centre = 6.0
first_factor = -0.125
second_factor = -1.0 / 7.0
memory_factor = -1.0 / 7.0


def hamiltonian(values, potential):
    summed = (3.0 * stencil_weights[0]) * values
    for offset in range(1, RADIUS + 1):
        for axis_id in range(3):
            summed = summed + stencil_weights[offset] * (jnp.roll(values, offset, axis=axis_id) + jnp.roll(values, -offset, axis=axis_id))
    return -0.5 * summed + potential[:, :, :, None] * values


def filter_group(member, potential):
    initial = member.astype(jnp.float32)
    first = ((hamiltonian(initial, potential) - spectrum_centre * initial) * first_factor).astype(jnp.bfloat16)
    first_f32 = first.astype(jnp.float32)
    filtered = ((hamiltonian(first_f32, potential) - spectrum_centre * first_f32) * second_factor + memory_factor * initial).astype(jnp.bfloat16)
    applied = hamiltonian(filtered.astype(jnp.float32), potential).astype(jnp.bfloat16)
    return filtered, applied


def accumulate(totals, plane_pair):
    plane_rows, images = plane_pair
    correlation_new = totals[0] + jnp.dot(plane_rows.T, plane_rows, preferred_element_type=jnp.float32)
    projected_new = totals[1] + jnp.dot(images.T, plane_rows, preferred_element_type=jnp.float32)
    return (correlation_new, projected_new), None


def reference(orbitals, potential):
    group_width = 16
    groups = NORB // group_width
    stacked = jnp.moveaxis(orbitals.reshape(NX, NY, NZ, groups, group_width), 3, 0)
    filtered, applied = lax.map(partial(filter_group, potential=potential), stacked)
    filtered = jnp.moveaxis(filtered, 0, 3).reshape(NX, NY, NZ, NORB)
    applied = jnp.moveaxis(applied, 0, 3).reshape(NX, NY * NZ, NORB)
    plane_rows = filtered.reshape(NX, NY * NZ, NORB)
    empty_sum = jnp.zeros((NORB, NORB), jnp.float32)
    totals, unused = lax.scan(accumulate, (empty_sum, empty_sum), (plane_rows, applied))
    cell_weight = 1.0 / (NX * NY * NZ)
    return filtered, totals[0] * cell_weight, totals[1] * cell_weight
```

```python
import jax
import jax.numpy as jnp
from jax import lax
from jax.sharding import PartitionSpec as P

RADIUS = 4


stencil_weights = (-205.0 / 72.0, 8.0 / 5.0, -1.0 / 5.0, 8.0 / 315.0, -1.0 / 560.0)
spectrum_centre = 6.0
first_factor = -0.125
second_factor = -1.0 / 7.0
memory_factor = -1.0 / 7.0


def padded(block, sides, width):
    for axis, dim in sides:
        count = lax.axis_size(axis)
        forward = [(i, i + 1) for i in range(count - 1)]
        forward.append((count - 1, 0))
        backward = [(target, source) for source, target in forward]
        low = lax.ppermute(
            lax.slice_in_dim(block, block.shape[dim] - width, None, axis=dim), axis, forward
        )
        high = lax.ppermute(lax.slice_in_dim(block, 0, width, axis=dim), axis, backward)
        block = jnp.concatenate([low, block, high], axis=dim)
    return block


def planes_of(extended, first_plane, planes):
    return lax.slice_in_dim(extended, first_plane, first_plane + planes, axis=0)


def hamiltonian(extended, potential, planes):
    middle = planes_of(extended, RADIUS, planes)
    summed = 3.0 * stencil_weights[0] * middle
    for offset in range(1, RADIUS + 1):
        beside = planes_of(extended, RADIUS + offset, planes) + planes_of(
            extended, RADIUS - offset, planes
        )
        beside = beside + jnp.roll(middle, offset, axis=1) + jnp.roll(middle, -offset, axis=1)
        beside = beside + jnp.roll(middle, offset, axis=2) + jnp.roll(middle, -offset, axis=2)
        summed = summed + stencil_weights[offset] * beside
    return -0.5 * summed + potential[:, :, :, None] * middle


def widened(values):
    return padded(values, (("domain", 0),), RADIUS)


def energy_block(filtered, potential, cell_count):
    extended = padded(filtered, (("domain", 0),), RADIUS).astype(jnp.float32)
    applied = hamiltonian(extended, potential, filtered.shape[0]).astype(jnp.bfloat16)
    return applied.reshape(cell_count, filtered.shape[3])


def shards(orbitals, potential):
    planes = orbitals.shape[0]
    initial = orbitals.astype(jnp.float32)
    extended = widened(orbitals).astype(jnp.float32)
    first = (
        (hamiltonian(extended, potential, planes) - spectrum_centre * initial) * first_factor
    ).astype(jnp.bfloat16)
    first_wide = widened(first).astype(jnp.float32)
    first_own = planes_of(first_wide, RADIUS, planes)
    filtered = (
        (hamiltonian(first_wide, potential, planes) - spectrum_centre * first_own) * second_factor
        + memory_factor * initial
    ).astype(jnp.bfloat16)
    cell_count = planes * filtered.shape[1] * filtered.shape[2]
    cell_weight = 1.0 / (cell_count * lax.axis_size("domain"))
    own_block = filtered.reshape(cell_count, filtered.shape[3])
    applied = energy_block(filtered, potential, cell_count)
    piece = lax.all_gather(own_block, "band", axis=1, tiled=True)
    correlation_piece = jnp.einsum(
        "cb,ck->bk", own_block, piece, preferred_element_type=jnp.float32
    )
    energy_piece = jnp.einsum("cb,ck->bk", applied, piece, preferred_element_type=jnp.float32)
    partial_terms = jnp.stack((correlation_piece, energy_piece))
    summed = butterfly_sum(partial_terms, "domain") * cell_weight
    correlation = summed[0]
    projected = summed[1]
    return (filtered, correlation, projected)


def butterfly_sum(values, axis):
    count = lax.axis_size(axis)
    bit = 1
    while bit < count:
        pairs = [(i, i ^ bit) for i in range(count)]
        values = values + lax.ppermute(values, axis, pairs)
        bit *= 2
    return values


def solution(mesh):
    placed = (P("domain", None, None, "band"), P("domain", None, None))
    return jax.shard_map(
        shards,
        mesh=mesh,
        in_specs=placed,
        out_specs=(P("domain", None, None, "band"), P("band", None), P("band", None)),
        check_vma=False,
    )
```

```python
import jax
import jax.numpy as jnp
from jax import lax
from jax.experimental import pallas as pl
from jax.experimental.pallas import tpu as pltpu
from jax.sharding import PartitionSpec as P

RADIUS = 4


stencil_weights = (-205.0 / 72.0, 8.0 / 5.0, -1.0 / 5.0, 8.0 / 315.0, -1.0 / 560.0)
spectrum_centre = 6.0
first_factor = -0.125
second_factor = -1.0 / 7.0
memory_factor = -1.0 / 7.0


def halos(block, axis, width):
    count = lax.axis_size(axis)
    forward = [(i, (i + 1) % count) for i in range(count)]
    backward = [(target, source) for source, target in forward]
    low = lax.ppermute(lax.slice_in_dim(block, block.shape[0] - width, None, axis=0), axis, forward)
    high = lax.ppermute(lax.slice_in_dim(block, 0, width, axis=0), axis, backward)
    return low, high


def stencil_kernel(stage, planes, ny, nz):
    def kernel(*refs):
        if stage == "filtered":
            low, own, high, pot, initial, out = refs
        else:
            low, own, high, pot, out = refs

        def plane_ref(p):
            if p < 0:
                return low, p + RADIUS
            if p >= planes:
                return high, p - planes
            return own, p

        for x in range(planes):
            def row(y, carry, x=x):
                centre = own[x, y].astype(jnp.float32)
                summed = (3.0 * stencil_weights[0]) * centre
                for k in range(1, RADIUS + 1):
                    above, ia = plane_ref(x + k)
                    below, ib = plane_ref(x - k)
                    beside = above[ia, y].astype(jnp.float32) + below[ib, y].astype(jnp.float32)
                    beside = beside + own[x, (y + k) % ny].astype(jnp.float32)
                    beside = beside + own[x, (y + ny - k) % ny].astype(jnp.float32)
                    beside = beside + (
                        pltpu.roll(centre, k, 0) + pltpu.roll(centre, nz - k, 0)
                    )
                    summed = summed + stencil_weights[k] * beside
                applied = -0.5 * summed + pot[x, y] * centre
                if stage == "first":
                    result = (applied - spectrum_centre * centre) * first_factor
                elif stage == "filtered":
                    result = (applied - spectrum_centre * centre) * second_factor + (
                        memory_factor * initial[x, y].astype(jnp.float32)
                    )
                else:
                    result = applied
                out[x, y] = result.astype(out.dtype)
                return carry

            lax.fori_loop(0, ny, row, 0)

    return kernel


def stencil_stage(stage, block, potential_wide, initial=None):
    planes, ny, nz, nb = block.shape
    low, high = halos(block, "domain", RADIUS)
    operands = [low, block, high, potential_wide]
    if initial is not None:
        operands.append(initial)
    return pl.pallas_call(
        stencil_kernel(stage, planes, ny, nz),
        out_shape=jax.ShapeDtypeStruct(block.shape, jnp.bfloat16),
        name=f"stencil_{stage}",
    )(*operands)


def butterfly_sum(values, axis):
    count = lax.axis_size(axis)
    bit = 1
    while bit < count:
        pairs = [(i, i ^ bit) for i in range(count)]
        values = values + lax.ppermute(values, axis, pairs)
        bit *= 2
    return values


def shards(orbitals, potential):
    planes, ny, nz, nb = orbitals.shape
    potential_wide = jnp.broadcast_to(potential[:, :, :, None], (planes, ny, nz, nb))
    first = stencil_stage("first", orbitals, potential_wide)
    filtered = stencil_stage("filtered", first, potential_wide, orbitals)
    applied_grid = stencil_stage("applied", filtered, potential_wide)
    cell_count = planes * ny * nz
    cell_weight = 1.0 / (cell_count * lax.axis_size("domain"))
    own_block = filtered.reshape(cell_count, nb)
    applied = applied_grid.reshape(cell_count, nb)
    piece = lax.all_gather(own_block, "band", axis=1, tiled=True)
    correlation_piece = jnp.einsum(
        "cb,ck->bk", own_block, piece, preferred_element_type=jnp.float32
    )
    energy_piece = jnp.einsum("cb,ck->bk", applied, piece, preferred_element_type=jnp.float32)
    partial_terms = jnp.stack((correlation_piece, energy_piece))
    summed = butterfly_sum(partial_terms, "domain") * cell_weight
    correlation = summed[0]
    projected = summed[1]
    return (filtered, correlation, projected)


def solution(mesh):
    placed = (P("domain", None, None, "band"), P("domain", None, None))
    return jax.shard_map(
        shards,
        mesh=mesh,
        in_specs=placed,
        out_specs=(P("domain", None, None, "band"), P("band", None), P("band", None)),
        check_vma=False,
    )
```

```python
import jax
import jax.numpy as jnp
from jax import lax
from jax.experimental import pallas as pl
from jax.experimental.pallas import tpu as pltpu
from jax.sharding import PartitionSpec as P

RADIUS = 4


stencil_weights = (-205.0 / 72.0, 8.0 / 5.0, -1.0 / 5.0, 8.0 / 315.0, -1.0 / 560.0)
spectrum_centre = 6.0
first_factor = -0.125
second_factor = -1.0 / 7.0
memory_factor = -1.0 / 7.0


def halos(block, axis, width):
    count = lax.axis_size(axis)
    forward = [(i, (i + 1) % count) for i in range(count)]
    backward = [(target, source) for source, target in forward]
    low = lax.ppermute(lax.slice_in_dim(block, block.shape[0] - width, None, axis=0), axis, forward)
    high = lax.ppermute(lax.slice_in_dim(block, 0, width, axis=0), axis, backward)
    return low, high


def stencil_kernel(stage, planes, ny, nz):
    def kernel(*refs):
        if stage == "filtered":
            low, own, high, pot, initial, out = refs
        else:
            low, own, high, pot, out = refs

        def plane_ref(p):
            if p < 0:
                return low, p + RADIUS
            if p >= planes:
                return high, p - planes
            return own, p

        for x in range(planes):
            def row(y, carry, x=x):
                centre = own[x, y].astype(jnp.float32)
                summed = (3.0 * stencil_weights[0]) * centre
                for k in range(1, RADIUS + 1):
                    above, ia = plane_ref(x + k)
                    below, ib = plane_ref(x - k)
                    beside = above[ia, y].astype(jnp.float32) + below[ib, y].astype(jnp.float32)
                    beside = beside + own[x, (y + k) % ny].astype(jnp.float32)
                    beside = beside + own[x, (y + ny - k) % ny].astype(jnp.float32)
                    beside = beside + (
                        pltpu.roll(centre, k, 0) + pltpu.roll(centre, nz - k, 0)
                    )
                    summed = summed + stencil_weights[k] * beside
                applied = -0.5 * summed + pot[x, y] * centre
                if stage == "first":
                    result = (applied - spectrum_centre * centre) * first_factor
                elif stage == "filtered":
                    result = (applied - spectrum_centre * centre) * second_factor + (
                        memory_factor * initial[x, y].astype(jnp.float32)
                    )
                else:
                    result = applied
                out[x, y] = result.astype(out.dtype)
                return carry

            lax.fori_loop(0, ny, row, 0)

    return kernel


def stencil_stage(stage, block, potential_wide, initial=None):
    planes, ny, nz, nb = block.shape
    low, high = halos(block, "domain", RADIUS)
    operands = [low, block, high, potential_wide]
    if initial is not None:
        operands.append(initial)
    return pl.pallas_call(
        stencil_kernel(stage, planes, ny, nz),
        out_shape=jax.ShapeDtypeStruct(block.shape, jnp.bfloat16),
        name=f"stencil_{stage}",
    )(*operands)


def halving_sum(values, axis):
    count = lax.axis_size(axis)
    index = lax.axis_index(axis)
    bits = []
    bit = 1
    while bit < count:
        bits.append(bit)
        bit *= 2
    for bit in bits:
        pairs = [(i, i ^ bit) for i in range(count)]
        half = values.shape[1] // 2
        upper = (index // bit) % 2
        keep = lax.dynamic_slice_in_dim(values, upper * half, half, axis=1)
        send = lax.dynamic_slice_in_dim(values, (1 - upper) * half, half, axis=1)
        values = keep + lax.ppermute(send, axis, pairs)
    for bit in reversed(bits):
        pairs = [(i, i ^ bit) for i in range(count)]
        upper = (index // bit) % 2
        other = lax.ppermute(values, axis, pairs)
        values = jnp.where(
            upper == 0,
            jnp.concatenate([values, other], axis=1),
            jnp.concatenate([other, values], axis=1),
        )
    return values


def shards(orbitals, potential):
    planes, ny, nz, nb = orbitals.shape
    potential_wide = jnp.broadcast_to(potential[:, :, :, None], (planes, ny, nz, nb))
    first = stencil_stage("first", orbitals, potential_wide)
    filtered = stencil_stage("filtered", first, potential_wide, orbitals)
    applied_grid = stencil_stage("applied", filtered, potential_wide)
    cell_count = planes * ny * nz
    cell_weight = 1.0 / (cell_count * lax.axis_size("domain"))
    own_block = filtered.reshape(cell_count, nb)
    applied = applied_grid.reshape(cell_count, nb)
    band = lax.axis_index("band")
    partner = lax.ppermute(own_block, "band", [(0, 1), (1, 0)])
    gram = lambda rows, cols: jnp.einsum(
        "cb,ck->bk", rows, cols, preferred_element_type=jnp.float32
    )
    placed = lambda mine, theirs: jnp.where(
        band == 0,
        jnp.concatenate([mine, theirs], axis=1),
        jnp.concatenate([theirs, mine], axis=1),
    )
    correlation_piece = placed(gram(own_block, own_block), gram(own_block, partner))
    energy_piece = placed(gram(applied, own_block), gram(applied, partner))
    partial_terms = jnp.stack((correlation_piece, energy_piece))
    summed = halving_sum(partial_terms, "domain") * cell_weight
    correlation = summed[0]
    projected = summed[1]
    return (filtered, correlation, projected)


def solution(mesh):
    placed = (P("domain", None, None, "band"), P("domain", None, None))
    return jax.shard_map(
        shards,
        mesh=mesh,
        in_specs=placed,
        out_specs=(P("domain", None, None, "band"), P("band", None), P("band", None)),
        check_vma=False,
    )
```

```python
import jax
import jax.numpy as jnp
from jax import lax
from jax.experimental import pallas as pl
from jax.experimental.pallas import tpu as pltpu
from jax.sharding import PartitionSpec as P

RADIUS = 4


stencil_weights = (-205.0 / 72.0, 8.0 / 5.0, -1.0 / 5.0, 8.0 / 315.0, -1.0 / 560.0)
spectrum_centre = 6.0
first_factor = -0.125
second_factor = -1.0 / 7.0
memory_factor = -1.0 / 7.0


def halos(block, axis, width):
    count = lax.axis_size(axis)
    forward = [(i, (i + 1) % count) for i in range(count)]
    backward = [(target, source) for source, target in forward]
    low = lax.ppermute(lax.slice_in_dim(block, block.shape[0] - width, None, axis=0), axis, forward)
    high = lax.ppermute(lax.slice_in_dim(block, 0, width, axis=0), axis, backward)
    return low, high


def stencil_kernel(stage, planes, ny, nz):
    def kernel(*refs):
        if stage == "filtered":
            low, own, high, pot, initial, out = refs
        else:
            low, own, high, pot, out = refs

        def plane_ref(p):
            if p < 0:
                return low, p + RADIUS
            if p >= planes:
                return high, p - planes
            return own, p

        for x in range(planes):
            def row(y, carry, x=x):
                centre = own[x, y].astype(jnp.float32)
                summed = (3.0 * stencil_weights[0]) * centre
                for k in range(1, RADIUS + 1):
                    above, ia = plane_ref(x + k)
                    below, ib = plane_ref(x - k)
                    beside = above[ia, y].astype(jnp.float32) + below[ib, y].astype(jnp.float32)
                    beside = beside + own[x, (y + k) % ny].astype(jnp.float32)
                    beside = beside + own[x, (y + ny - k) % ny].astype(jnp.float32)
                    beside = beside + (
                        pltpu.roll(centre, k, 0) + pltpu.roll(centre, nz - k, 0)
                    )
                    summed = summed + stencil_weights[k] * beside
                applied = -0.5 * summed + pot[x, y] * centre
                if stage == "first":
                    result = (applied - spectrum_centre * centre) * first_factor
                elif stage == "filtered":
                    result = (applied - spectrum_centre * centre) * second_factor + (
                        memory_factor * initial[x, y].astype(jnp.float32)
                    )
                else:
                    result = applied
                out[x, y] = result.astype(out.dtype)
                return carry

            lax.fori_loop(0, ny, row, 0)

    return kernel


def stencil_stage(stage, block, potential_wide, initial=None):
    planes, ny, nz, nb = block.shape
    low, high = halos(block, "domain", RADIUS)
    operands = [low, block, high, potential_wide]
    if initial is not None:
        operands.append(initial)
    return pl.pallas_call(
        stencil_kernel(stage, planes, ny, nz),
        out_shape=jax.ShapeDtypeStruct(block.shape, jnp.bfloat16),
        name=f"stencil_{stage}",
    )(*operands)


def butterfly_sum(values, axis):
    count = lax.axis_size(axis)
    bit = 1
    while bit < count:
        pairs = [(i, i ^ bit) for i in range(count)]
        values = values + lax.ppermute(values, axis, pairs)
        bit *= 2
    return values


def shards(orbitals, potential):
    planes, ny, nz, nb = orbitals.shape
    potential_wide = jnp.broadcast_to(potential[:, :, :, None], (planes, ny, nz, nb))
    cell_count = planes * ny * nz
    cell_weight = 1.0 / (cell_count * lax.axis_size("domain"))
    band = lax.axis_index("band")
    gram = lambda rows, cols: jnp.einsum(
        "cb,ck->bk", rows, cols, preferred_element_type=jnp.float32
    )
    placed = lambda mine, theirs: jnp.where(
        band == 0,
        jnp.concatenate([mine, theirs], axis=1),
        jnp.concatenate([theirs, mine], axis=1),
    )
    first = stencil_stage("first", orbitals, potential_wide)
    filtered = stencil_stage("filtered", first, potential_wide, orbitals)
    own_block = filtered.reshape(cell_count, nb)
    partner = lax.ppermute(own_block, "band", [(0, 1), (1, 0)])
    correlation_piece = placed(gram(own_block, own_block), gram(own_block, partner))
    correlation = butterfly_sum(correlation_piece, "domain") * cell_weight
    applied = stencil_stage("applied", filtered, potential_wide).reshape(cell_count, nb)
    energy_piece = placed(gram(applied, own_block), gram(applied, partner))
    projected = butterfly_sum(energy_piece, "domain") * cell_weight
    return (filtered, correlation, projected)


def solution(mesh):
    placed = (P("domain", None, None, "band"), P("domain", None, None))
    return jax.shard_map(
        shards,
        mesh=mesh,
        in_specs=placed,
        out_specs=(P("domain", None, None, "band"), P("band", None), P("band", None)),
        check_vma=False,
    )
```

```python
import jax
import jax.numpy as jnp
from jax import lax
from jax.experimental import pallas as pl
from jax.experimental.pallas import tpu as pltpu
from jax.sharding import PartitionSpec as P

RADIUS = 4


stencil_weights = (-205.0 / 72.0, 8.0 / 5.0, -1.0 / 5.0, 8.0 / 315.0, -1.0 / 560.0)
spectrum_centre = 6.0
first_factor = -0.125
second_factor = -1.0 / 7.0
memory_factor = -1.0 / 7.0


def halos(block, axis, width):
    count = lax.axis_size(axis)
    forward = [(i, (i + 1) % count) for i in range(count)]
    backward = [(target, source) for source, target in forward]
    low = lax.ppermute(lax.slice_in_dim(block, block.shape[0] - width, None, axis=0), axis, forward)
    high = lax.ppermute(lax.slice_in_dim(block, 0, width, axis=0), axis, backward)
    return low, high


def interior_kernel(planes, ny, nz):
    def kernel(own, out):
        for x in range(planes):
            def row(y, carry, x=x):
                centre = own[x, y].astype(jnp.float32)
                summed = (3.0 * stencil_weights[0]) * centre
                for k in range(1, RADIUS + 1):
                    beside = own[x, (y + k) % ny].astype(jnp.float32)
                    beside = beside + own[x, (y + ny - k) % ny].astype(jnp.float32)
                    beside = beside + (
                        pltpu.roll(centre, k, 0) + pltpu.roll(centre, nz - k, 0)
                    )
                    if x + k < planes:
                        beside = beside + own[x + k, y].astype(jnp.float32)
                    if x - k >= 0:
                        beside = beside + own[x - k, y].astype(jnp.float32)
                    summed = summed + stencil_weights[k] * beside
                out[x, y] = summed
                return carry

            lax.fori_loop(0, ny, row, 0)

    return kernel


def finish_kernel(stage, planes, ny):
    def kernel(*refs):
        if stage == "filtered":
            low, high, own, partial, pot, initial, out = refs
        else:
            low, high, own, partial, pot, out = refs
        for x in range(planes):
            def row(y, carry, x=x):
                summed = partial[x, y]
                for k in range(1, RADIUS + 1):
                    outside = []
                    if x + k >= planes:
                        outside.append(high[x + k - planes, y].astype(jnp.float32))
                    if x - k < 0:
                        outside.append(low[x - k + RADIUS, y].astype(jnp.float32))
                    if outside:
                        term = outside[0] if len(outside) == 1 else outside[0] + outside[1]
                        summed = summed + stencil_weights[k] * term
                centre = own[x, y].astype(jnp.float32)
                applied = -0.5 * summed + pot[x, y] * centre
                if stage == "first":
                    result = (applied - spectrum_centre * centre) * first_factor
                elif stage == "filtered":
                    result = (applied - spectrum_centre * centre) * second_factor + (
                        memory_factor * initial[x, y].astype(jnp.float32)
                    )
                else:
                    result = applied
                out[x, y] = result.astype(out.dtype)
                return carry

            lax.fori_loop(0, ny, row, 0)

    return kernel


def stencil_stage(stage, block, potential_wide, initial=None):
    planes, ny, nz, nb = block.shape
    low, high = halos(block, "domain", RADIUS)
    partial = pl.pallas_call(
        interior_kernel(planes, ny, nz),
        out_shape=jax.ShapeDtypeStruct(block.shape, jnp.float32),
        name=f"interior_{stage}",
    )(block)
    operands = [low, high, block, partial, potential_wide]
    if initial is not None:
        operands.append(initial)
    return pl.pallas_call(
        finish_kernel(stage, planes, ny),
        out_shape=jax.ShapeDtypeStruct(block.shape, jnp.bfloat16),
        name=f"finish_{stage}",
    )(*operands)


def butterfly_sum(values, axis):
    count = lax.axis_size(axis)
    bit = 1
    while bit < count:
        pairs = [(i, i ^ bit) for i in range(count)]
        values = values + lax.ppermute(values, axis, pairs)
        bit *= 2
    return values


def shards(orbitals, potential):
    planes, ny, nz, nb = orbitals.shape
    potential_wide = jnp.broadcast_to(potential[:, :, :, None], (planes, ny, nz, nb))
    cell_count = planes * ny * nz
    cell_weight = 1.0 / (cell_count * lax.axis_size("domain"))
    band = lax.axis_index("band")
    gram = lambda rows, cols: jnp.einsum(
        "cb,ck->bk", rows, cols, preferred_element_type=jnp.float32
    )
    placed = lambda mine, theirs: jnp.where(
        band == 0,
        jnp.concatenate([mine, theirs], axis=1),
        jnp.concatenate([theirs, mine], axis=1),
    )
    first = stencil_stage("first", orbitals, potential_wide)
    filtered = stencil_stage("filtered", first, potential_wide, orbitals)
    own_block = filtered.reshape(cell_count, nb)
    partner = lax.ppermute(own_block, "band", [(0, 1), (1, 0)])
    correlation_piece = placed(gram(own_block, own_block), gram(own_block, partner))
    correlation = butterfly_sum(correlation_piece, "domain") * cell_weight
    applied = stencil_stage("applied", filtered, potential_wide).reshape(cell_count, nb)
    energy_piece = placed(gram(applied, own_block), gram(applied, partner))
    projected = butterfly_sum(energy_piece, "domain") * cell_weight
    return (filtered, correlation, projected)


def solution(mesh):
    placed = (P("domain", None, None, "band"), P("domain", None, None))
    return jax.shard_map(
        shards,
        mesh=mesh,
        in_specs=placed,
        out_specs=(P("domain", None, None, "band"), P("band", None), P("band", None)),
        check_vma=False,
    )
```

```python
import jax
import jax.numpy as jnp
from jax import lax
from jax.experimental import pallas as pl
from jax.experimental.pallas import tpu as pltpu
from jax.sharding import PartitionSpec as P

RADIUS = 4


stencil_weights = (-205.0 / 72.0, 8.0 / 5.0, -1.0 / 5.0, 8.0 / 315.0, -1.0 / 560.0)
spectrum_centre = 6.0
first_factor = -0.125
second_factor = -1.0 / 7.0
memory_factor = -1.0 / 7.0


def interior_kernel(stage, planes, ny, nz):
    shift = 0.0 if stage == "applied" else spectrum_centre

    def kernel(own, pot, out):
        for x in range(planes):
            def row(y, carry, x=x):
                centre = own[x, y].astype(jnp.float32)
                summed = (3.0 * stencil_weights[0]) * centre
                for k in range(1, RADIUS + 1):
                    beside = own[x, (y + k) % ny].astype(jnp.float32)
                    beside = beside + own[x, (y + ny - k) % ny].astype(jnp.float32)
                    beside = beside + (
                        pltpu.roll(centre, k, 0) + pltpu.roll(centre, nz - k, 0)
                    )
                    if x + k < planes:
                        beside = beside + own[x + k, y].astype(jnp.float32)
                    if x - k >= 0:
                        beside = beside + own[x - k, y].astype(jnp.float32)
                    summed = summed + stencil_weights[k] * beside
                applied = -0.5 * summed + pot[x, y] * centre
                if shift:
                    applied = applied - shift * centre
                out[x, y] = applied
                return carry

            lax.fori_loop(0, ny, row, 0)

    return kernel


def finish_kernel(stage, planes, ny):
    def kernel(*refs):
        refs = list(refs)
        low, high, partial = refs[:3]
        initial = refs[3] if stage == "filtered" else None
        outs = refs[4:] if stage == "filtered" else refs[3:]
        out = outs[0]
        for x in range(planes):
            def row(y, carry, x=x):
                summed = partial[x, y]
                for k in range(1, RADIUS + 1):
                    outside = []
                    if x + k >= planes:
                        outside.append(high[x + k - planes, y].astype(jnp.float32))
                    if x - k < 0:
                        outside.append(low[x - k + RADIUS, y].astype(jnp.float32))
                    if outside:
                        term = outside[0] if len(outside) == 1 else outside[0] + outside[1]
                        summed = summed + (-0.5 * stencil_weights[k]) * term
                if stage == "first":
                    result = summed * first_factor
                elif stage == "filtered":
                    result = summed * second_factor + (
                        memory_factor * initial[x, y].astype(jnp.float32)
                    )
                else:
                    result = summed
                result = result.astype(out.dtype)
                out[x, y] = result
                if len(outs) == 3:
                    if x >= planes - RADIUS:
                        outs[1][x - planes + RADIUS, y] = result
                    if x < RADIUS:
                        outs[2][x, y] = result
                return carry

            lax.fori_loop(0, ny, row, 0)

    return kernel


def stencil_stage(stage, block, sends, potential_wide, initial=None, keep_sends=True):
    planes, ny, nz, nb = block.shape
    low, high = exchange(sends, "domain")
    partial = pl.pallas_call(
        interior_kernel(stage, planes, ny, nz),
        out_shape=jax.ShapeDtypeStruct(block.shape, jnp.float32),
        name=f"interior_{stage}",
    )(block, potential_wide)
    operands = [low, high, partial]
    if initial is not None:
        operands.append(initial)
    shapes = [jax.ShapeDtypeStruct(block.shape, jnp.bfloat16)]
    if keep_sends:
        edge = jax.ShapeDtypeStruct((RADIUS, ny, nz, nb), jnp.bfloat16)
        shapes += [edge, edge]
    return pl.pallas_call(
        finish_kernel(stage, planes, ny),
        out_shape=tuple(shapes),
        name=f"finish_{stage}",
    )(*operands)


def exchange(sends, axis):
    count = lax.axis_size(axis)
    forward = [(i, (i + 1) % count) for i in range(count)]
    backward = [(target, source) for source, target in forward]
    return lax.ppermute(sends[0], axis, forward), lax.ppermute(sends[1], axis, backward)


def butterfly_sum(values, axis):
    count = lax.axis_size(axis)
    bit = 1
    while bit < count:
        pairs = [(i, i ^ bit) for i in range(count)]
        values = values + lax.ppermute(values, axis, pairs)
        bit *= 2
    return values


def shards(orbitals, potential):
    planes, ny, nz, nb = orbitals.shape
    potential_wide = jnp.broadcast_to(potential[:, :, :, None], (planes, ny, nz, nb))
    cell_count = planes * ny * nz
    cell_weight = 1.0 / (cell_count * lax.axis_size("domain"))
    band = lax.axis_index("band")
    gram = lambda rows, cols: jnp.einsum(
        "cb,ck->bk", rows, cols, preferred_element_type=jnp.float32
    )
    placed = lambda mine, theirs: jnp.where(
        band == 0,
        jnp.concatenate([mine, theirs], axis=1),
        jnp.concatenate([theirs, mine], axis=1),
    )
    planes_sent = (
        lax.slice_in_dim(orbitals, planes - RADIUS, None, axis=0),
        lax.slice_in_dim(orbitals, 0, RADIUS, axis=0),
    )
    first, *first_sent = stencil_stage("first", orbitals, planes_sent, potential_wide)
    filtered, *filtered_sent = stencil_stage(
        "filtered", first, first_sent, potential_wide, orbitals
    )
    own_block = filtered.reshape(cell_count, nb)
    partner = lax.ppermute(own_block, "band", [(0, 1), (1, 0)])
    correlation_piece = placed(gram(own_block, own_block), gram(own_block, partner))
    correlation = butterfly_sum(correlation_piece, "domain") * cell_weight
    (applied_grid,) = stencil_stage(
        "applied", filtered, filtered_sent, potential_wide, keep_sends=False
    )
    applied = applied_grid.reshape(cell_count, nb)
    energy_piece = placed(gram(applied, own_block), gram(applied, partner))
    projected = butterfly_sum(energy_piece, "domain") * cell_weight
    return (filtered, correlation, projected)


def solution(mesh):
    placed = (P("domain", None, None, "band"), P("domain", None, None))
    return jax.shard_map(
        shards,
        mesh=mesh,
        in_specs=placed,
        out_specs=(P("domain", None, None, "band"), P("band", None), P("band", None)),
        check_vma=False,
    )
```

```python
import jax
import jax.numpy as jnp
from jax import lax
from jax.experimental import pallas as pl
from jax.experimental.pallas import tpu as pltpu
from jax.sharding import PartitionSpec as P

RADIUS = 4


stencil_weights = (-205.0 / 72.0, 8.0 / 5.0, -1.0 / 5.0, 8.0 / 315.0, -1.0 / 560.0)
spectrum_centre = 6.0
first_factor = -0.125
second_factor = -1.0 / 7.0
memory_factor = -1.0 / 7.0


def interior_kernel(stage, planes, ny, nz):
    shift = 0.0 if stage == "applied" else spectrum_centre

    def kernel(own_narrow, pot, out, own):
        for x in range(planes):
            own[x] = own_narrow[x].astype(jnp.float32)
        for x in range(planes):
            def row(y, carry, x=x):
                centre = own[x, y]
                summed = (3.0 * stencil_weights[0]) * centre
                for k in range(1, RADIUS + 1):
                    beside = own[x, (y + k) % ny] + own[x, (y + ny - k) % ny]
                    beside = beside + (
                        pltpu.roll(centre, k, 0) + pltpu.roll(centre, nz - k, 0)
                    )
                    if x + k < planes:
                        beside = beside + own[x + k, y]
                    if x - k >= 0:
                        beside = beside + own[x - k, y]
                    summed = summed + stencil_weights[k] * beside
                applied = -0.5 * summed + pot[x, y] * centre
                if shift:
                    applied = applied - shift * centre
                out[x, y] = applied
                return carry

            lax.fori_loop(0, ny, row, 0)

    return kernel


def finish_kernel(stage, planes, ny):
    def kernel(*refs):
        refs = list(refs)
        low, high, partial = refs[:3]
        initial = refs[3] if stage == "filtered" else None
        outs = refs[4:] if stage == "filtered" else refs[3:]
        out = outs[0]
        for x in range(planes):
            def row(y, carry, x=x):
                summed = partial[x, y]
                for k in range(1, RADIUS + 1):
                    outside = []
                    if x + k >= planes:
                        outside.append(high[x + k - planes, y].astype(jnp.float32))
                    if x - k < 0:
                        outside.append(low[x - k + RADIUS, y].astype(jnp.float32))
                    if outside:
                        term = outside[0] if len(outside) == 1 else outside[0] + outside[1]
                        summed = summed + (-0.5 * stencil_weights[k]) * term
                if stage == "first":
                    result = summed * first_factor
                elif stage == "filtered":
                    result = summed * second_factor + (
                        memory_factor * initial[x, y].astype(jnp.float32)
                    )
                else:
                    result = summed
                result = result.astype(out.dtype)
                out[x, y] = result
                if len(outs) == 3:
                    if x >= planes - RADIUS:
                        outs[1][x - planes + RADIUS, y] = result
                    if x < RADIUS:
                        outs[2][x, y] = result
                return carry

            lax.fori_loop(0, ny, row, 0)

    return kernel


def stencil_stage(stage, block, sends, potential_wide, initial=None, keep_sends=True):
    planes, ny, nz, nb = block.shape
    low, high = exchange(sends, "domain")
    partial = pl.pallas_call(
        interior_kernel(stage, planes, ny, nz),
        out_shape=jax.ShapeDtypeStruct(block.shape, jnp.float32),
        scratch_shapes=[pltpu.VMEM(block.shape, jnp.float32)],
        name=f"interior_{stage}",
    )(block, potential_wide)
    operands = [low, high, partial]
    if initial is not None:
        operands.append(initial)
    shapes = [jax.ShapeDtypeStruct(block.shape, jnp.bfloat16)]
    if keep_sends:
        edge = jax.ShapeDtypeStruct((RADIUS, ny, nz, nb), jnp.bfloat16)
        shapes += [edge, edge]
    return pl.pallas_call(
        finish_kernel(stage, planes, ny),
        out_shape=tuple(shapes),
        name=f"finish_{stage}",
    )(*operands)


def exchange(sends, axis):
    count = lax.axis_size(axis)
    forward = [(i, (i + 1) % count) for i in range(count)]
    backward = [(target, source) for source, target in forward]
    return lax.ppermute(sends[0], axis, forward), lax.ppermute(sends[1], axis, backward)


def butterfly_sum(values, axis):
    count = lax.axis_size(axis)
    bit = 1
    while bit < count:
        pairs = [(i, i ^ bit) for i in range(count)]
        values = values + lax.ppermute(values, axis, pairs)
        bit *= 2
    return values


def shards(orbitals, potential):
    planes, ny, nz, nb = orbitals.shape
    potential_wide = jnp.broadcast_to(potential[:, :, :, None], (planes, ny, nz, nb))
    cell_count = planes * ny * nz
    cell_weight = 1.0 / (cell_count * lax.axis_size("domain"))
    band = lax.axis_index("band")
    gram = lambda rows, cols: jnp.einsum(
        "cb,ck->bk", rows, cols, preferred_element_type=jnp.float32
    )
    placed = lambda mine, theirs: jnp.where(
        band == 0,
        jnp.concatenate([mine, theirs], axis=1),
        jnp.concatenate([theirs, mine], axis=1),
    )
    planes_sent = (
        lax.slice_in_dim(orbitals, planes - RADIUS, None, axis=0),
        lax.slice_in_dim(orbitals, 0, RADIUS, axis=0),
    )
    first, *first_sent = stencil_stage("first", orbitals, planes_sent, potential_wide)
    filtered, *filtered_sent = stencil_stage(
        "filtered", first, first_sent, potential_wide, orbitals
    )
    own_block = filtered.reshape(cell_count, nb)
    partner = lax.ppermute(own_block, "band", [(0, 1), (1, 0)])
    correlation_piece = placed(gram(own_block, own_block), gram(own_block, partner))
    correlation = butterfly_sum(correlation_piece, "domain") * cell_weight
    (applied_grid,) = stencil_stage(
        "applied", filtered, filtered_sent, potential_wide, keep_sends=False
    )
    applied = applied_grid.reshape(cell_count, nb)
    energy_piece = placed(gram(applied, own_block), gram(applied, partner))
    projected = butterfly_sum(energy_piece, "domain") * cell_weight
    return (filtered, correlation, projected)


def solution(mesh):
    placed = (P("domain", None, None, "band"), P("domain", None, None))
    return jax.shard_map(
        shards,
        mesh=mesh,
        in_specs=placed,
        out_specs=(P("domain", None, None, "band"), P("band", None), P("band", None)),
        check_vma=False,
    )
```

```python
import jax
import jax.numpy as jnp
from jax import lax
from jax.experimental import pallas as pl
from jax.experimental.pallas import tpu as pltpu
from jax.sharding import PartitionSpec as P

RADIUS = 4


stencil_weights = (-205.0 / 72.0, 8.0 / 5.0, -1.0 / 5.0, 8.0 / 315.0, -1.0 / 560.0)
spectrum_centre = 6.0
first_factor = -0.125
second_factor = -1.0 / 7.0
memory_factor = -1.0 / 7.0


def interior_kernel(stage, planes, ny, nz):
    shift = 0.0 if stage == "applied" else spectrum_centre

    def kernel(own_narrow, pot, out, own):
        for x in range(planes):
            own[x] = own_narrow[x].astype(jnp.float32)
        for x in range(planes):
            def row(y, carry, x=x):
                centre = own[x, y]
                summed = (3.0 * stencil_weights[0]) * centre
                for k in range(1, RADIUS + 1):
                    beside = own[x, (y + k) % ny] + own[x, (y + ny - k) % ny]
                    beside = beside + (
                        pltpu.roll(centre, k, 0) + pltpu.roll(centre, nz - k, 0)
                    )
                    if x + k < planes:
                        beside = beside + own[x + k, y]
                    if x - k >= 0:
                        beside = beside + own[x - k, y]
                    summed = summed + stencil_weights[k] * beside
                applied = -0.5 * summed + pot[x, y] * centre
                if shift:
                    applied = applied - shift * centre
                out[x, y] = applied
                return carry

            lax.fori_loop(0, ny, row, 0)

    return kernel


def finish_kernel(stage, planes, ny):
    def kernel(*refs):
        refs = list(refs)
        low, high, partial = refs[:3]
        initial = refs[3] if stage == "filtered" else None
        outs = refs[4:] if stage == "filtered" else refs[3:]
        out = outs[0]
        for x in range(planes):
            def row(y, carry, x=x):
                summed = partial[x, y]
                for k in range(1, RADIUS + 1):
                    outside = []
                    if x + k >= planes:
                        outside.append(high[x + k - planes, y].astype(jnp.float32))
                    if x - k < 0:
                        outside.append(low[x - k + RADIUS, y].astype(jnp.float32))
                    if outside:
                        term = outside[0] if len(outside) == 1 else outside[0] + outside[1]
                        summed = summed + (-0.5 * stencil_weights[k]) * term
                if stage == "first":
                    result = summed * first_factor
                elif stage == "filtered":
                    result = summed * second_factor + (
                        memory_factor * initial[x, y].astype(jnp.float32)
                    )
                else:
                    result = summed
                result = result.astype(out.dtype)
                out[x, y] = result
                if len(outs) == 3:
                    if x >= planes - RADIUS:
                        outs[1][x - planes + RADIUS, y] = result
                    if x < RADIUS:
                        outs[2][x, y] = result
                return carry

            lax.fori_loop(0, ny, row, 0)

    return kernel


def stencil_stage(stage, block, sends, potential_wide, initial=None, keep_sends=True):
    planes, ny, nz, nb = block.shape
    low, high = exchange(sends, "domain")
    partial = pl.pallas_call(
        interior_kernel(stage, planes, ny, nz),
        out_shape=jax.ShapeDtypeStruct(block.shape, jnp.float32),
        scratch_shapes=[pltpu.VMEM(block.shape, jnp.float32)],
        name=f"interior_{stage}",
    )(block, potential_wide)
    operands = [low, high, partial]
    if initial is not None:
        operands.append(initial)
    shapes = [jax.ShapeDtypeStruct(block.shape, jnp.bfloat16)]
    if keep_sends:
        edge = jax.ShapeDtypeStruct((RADIUS, ny, nz, nb), jnp.bfloat16)
        shapes += [edge, edge]
    return pl.pallas_call(
        finish_kernel(stage, planes, ny),
        out_shape=tuple(shapes),
        name=f"finish_{stage}",
    )(*operands)


def exchange(sends, axis):
    count = lax.axis_size(axis)
    forward = [(i, (i + 1) % count) for i in range(count)]
    backward = [(target, source) for source, target in forward]
    return lax.ppermute(sends[0], axis, forward), lax.ppermute(sends[1], axis, backward)


def butterfly_sum(values, axis):
    count = lax.axis_size(axis)
    index = lax.axis_index(axis)
    pairs_of = lambda bit: [(i, i ^ bit) for i in range(count)]
    half = values.shape[0] // 2
    upper = index % 2
    keep = lax.dynamic_slice_in_dim(values, upper * half, half, axis=0)
    send = lax.dynamic_slice_in_dim(values, (1 - upper) * half, half, axis=0)
    values = keep + lax.ppermute(send, axis, pairs_of(1))
    bit = 2
    while bit < count:
        values = values + lax.ppermute(values, axis, pairs_of(bit))
        bit *= 2
    other = lax.ppermute(values, axis, pairs_of(1))
    return jnp.where(
        upper == 0,
        jnp.concatenate([values, other], axis=0),
        jnp.concatenate([other, values], axis=0),
    )


def shards(orbitals, potential):
    planes, ny, nz, nb = orbitals.shape
    potential_wide = jnp.broadcast_to(potential[:, :, :, None], (planes, ny, nz, nb))
    cell_count = planes * ny * nz
    cell_weight = 1.0 / (cell_count * lax.axis_size("domain"))
    band = lax.axis_index("band")
    gram = lambda rows, cols: jnp.einsum(
        "cb,ck->bk", rows, cols, preferred_element_type=jnp.float32
    )
    placed = lambda mine, theirs: jnp.where(
        band == 0,
        jnp.concatenate([mine, theirs], axis=1),
        jnp.concatenate([theirs, mine], axis=1),
    )
    planes_sent = (
        lax.slice_in_dim(orbitals, planes - RADIUS, None, axis=0),
        lax.slice_in_dim(orbitals, 0, RADIUS, axis=0),
    )
    first, *first_sent = stencil_stage("first", orbitals, planes_sent, potential_wide)
    filtered, *filtered_sent = stencil_stage(
        "filtered", first, first_sent, potential_wide, orbitals
    )
    own_block = filtered.reshape(cell_count, nb)
    partner = lax.ppermute(own_block, "band", [(0, 1), (1, 0)])
    correlation_piece = placed(gram(own_block, own_block), gram(own_block, partner))
    correlation = butterfly_sum(correlation_piece, "domain") * cell_weight
    (applied_grid,) = stencil_stage(
        "applied", filtered, filtered_sent, potential_wide, keep_sends=False
    )
    applied = applied_grid.reshape(cell_count, nb)
    energy_piece = placed(gram(applied, own_block), gram(applied, partner))
    projected = butterfly_sum(energy_piece, "domain") * cell_weight
    return (filtered, correlation, projected)


def solution(mesh):
    placed = (P("domain", None, None, "band"), P("domain", None, None))
    return jax.shard_map(
        shards,
        mesh=mesh,
        in_specs=placed,
        out_specs=(P("domain", None, None, "band"), P("band", None), P("band", None)),
        check_vma=False,
    )
```

```python
import jax
import jax.numpy as jnp
from jax import lax
from jax.experimental import pallas as pl
from jax.experimental.pallas import tpu as pltpu
from jax.sharding import PartitionSpec as P

RADIUS = 4


stencil_weights = (-205.0 / 72.0, 8.0 / 5.0, -1.0 / 5.0, 8.0 / 315.0, -1.0 / 560.0)
spectrum_centre = 6.0
first_factor = -0.125
second_factor = -1.0 / 7.0
memory_factor = -1.0 / 7.0


def interior_kernel(stage, planes, ny, nz):
    shift = 0.0 if stage == "applied" else spectrum_centre

    def kernel(own_narrow, pot, out, own):
        for x in range(planes):
            own[x] = own_narrow[x].astype(jnp.float32)
        for x in range(planes):
            def row(y, carry, x=x):
                centre = own[x, y]
                summed = (3.0 * stencil_weights[0]) * centre
                for k in range(1, RADIUS + 1):
                    beside = own[x, (y + k) % ny] + own[x, (y + ny - k) % ny]
                    beside = beside + (
                        pltpu.roll(centre, k, 0) + pltpu.roll(centre, nz - k, 0)
                    )
                    if x + k < planes:
                        beside = beside + own[x + k, y]
                    if x - k >= 0:
                        beside = beside + own[x - k, y]
                    summed = summed + stencil_weights[k] * beside
                applied = -0.5 * summed + pot[x, y] * centre
                if shift:
                    applied = applied - shift * centre
                out[x, y] = applied
                return carry

            lax.fori_loop(0, ny, row, 0)

    return kernel


def finish_kernel(stage, planes, ny):
    def kernel(*refs):
        refs = list(refs)
        low, high, partial = refs[:3]
        initial = refs[3] if stage == "filtered" else None
        outs = refs[4:] if stage == "filtered" else refs[3:]
        out = outs[0]
        for x in range(planes):
            def row(y, carry, x=x):
                summed = partial[x, y]
                for k in range(1, RADIUS + 1):
                    outside = []
                    if x + k >= planes:
                        outside.append(high[x + k - planes, y].astype(jnp.float32))
                    if x - k < 0:
                        outside.append(low[x - k + RADIUS, y].astype(jnp.float32))
                    if outside:
                        term = outside[0] if len(outside) == 1 else outside[0] + outside[1]
                        summed = summed + (-0.5 * stencil_weights[k]) * term
                if stage == "first":
                    result = summed * first_factor
                elif stage == "filtered":
                    result = summed * second_factor + (
                        memory_factor * initial[x, y].astype(jnp.float32)
                    )
                else:
                    result = summed
                result = result.astype(out.dtype)
                out[x, y] = result
                if len(outs) == 3:
                    if x >= planes - RADIUS:
                        outs[1][x - planes + RADIUS, y] = result
                    if x < RADIUS:
                        outs[2][x, y] = result
                return carry

            lax.fori_loop(0, ny, row, 0)

    return kernel


def stencil_stage(stage, block, sends, potential_wide, initial=None, keep_sends=True):
    planes, ny, nz, nb = block.shape
    low, high = exchange(sends, "domain")
    partial = pl.pallas_call(
        interior_kernel(stage, planes, ny, nz),
        out_shape=jax.ShapeDtypeStruct(block.shape, jnp.float32),
        scratch_shapes=[pltpu.VMEM(block.shape, jnp.float32)],
        name=f"interior_{stage}",
    )(block, potential_wide)
    operands = [low, high, partial]
    if initial is not None:
        operands.append(initial)
    shapes = [jax.ShapeDtypeStruct(block.shape, jnp.bfloat16)]
    if keep_sends:
        edge = jax.ShapeDtypeStruct((RADIUS, ny, nz, nb), jnp.bfloat16)
        shapes += [edge, edge]
    return pl.pallas_call(
        finish_kernel(stage, planes, ny),
        out_shape=tuple(shapes),
        name=f"finish_{stage}",
    )(*operands)


def exchange(sends, axis):
    count = lax.axis_size(axis)
    forward = [(i, (i + 1) % count) for i in range(count)]
    backward = [(target, source) for source, target in forward]
    return lax.ppermute(sends[0], axis, forward), lax.ppermute(sends[1], axis, backward)


def butterfly_sum(values, axis):
    count = lax.axis_size(axis)
    index = lax.axis_index(axis)
    pairs_of = lambda bit: [(i, i ^ bit) for i in range(count)]
    half = values.shape[0] // 2
    upper = index % 2
    keep = lax.dynamic_slice_in_dim(values, upper * half, half, axis=0)
    send = lax.dynamic_slice_in_dim(values, (1 - upper) * half, half, axis=0)
    values = keep + lax.ppermute(send, axis, pairs_of(1))
    bits = []
    bit = 2
    while bit < count:
        bits.append(bit)
        bit *= 2
    while bits:
        if len(bits) == 1:
            values = values + lax.ppermute(values, axis, pairs_of(bits.pop(0)))
            continue
        a, b = bits.pop(0), bits.pop(0)
        near = lax.ppermute(values, axis, pairs_of(a))
        far = lax.ppermute(values, axis, pairs_of(b))
        across = lax.ppermute(values, axis, pairs_of(a | b))
        values = (values + near) + (far + across)
    other = lax.ppermute(values, axis, pairs_of(1))
    return jnp.where(
        upper == 0,
        jnp.concatenate([values, other], axis=0),
        jnp.concatenate([other, values], axis=0),
    )


def shards(orbitals, potential):
    planes, ny, nz, nb = orbitals.shape
    potential_wide = jnp.broadcast_to(potential[:, :, :, None], (planes, ny, nz, nb))
    cell_count = planes * ny * nz
    cell_weight = 1.0 / (cell_count * lax.axis_size("domain"))
    band = lax.axis_index("band")
    gram = lambda rows, cols: jnp.einsum(
        "cb,ck->bk", rows, cols, preferred_element_type=jnp.float32
    )
    placed = lambda mine, theirs: jnp.where(
        band == 0,
        jnp.concatenate([mine, theirs], axis=1),
        jnp.concatenate([theirs, mine], axis=1),
    )
    planes_sent = (
        lax.slice_in_dim(orbitals, planes - RADIUS, None, axis=0),
        lax.slice_in_dim(orbitals, 0, RADIUS, axis=0),
    )
    first, *first_sent = stencil_stage("first", orbitals, planes_sent, potential_wide)
    filtered, *filtered_sent = stencil_stage(
        "filtered", first, first_sent, potential_wide, orbitals
    )
    own_block = filtered.reshape(cell_count, nb)
    partner = lax.ppermute(own_block, "band", [(0, 1), (1, 0)])
    correlation_piece = placed(gram(own_block, own_block), gram(own_block, partner))
    correlation = butterfly_sum(correlation_piece, "domain") * cell_weight
    (applied_grid,) = stencil_stage(
        "applied", filtered, filtered_sent, potential_wide, keep_sends=False
    )
    applied = applied_grid.reshape(cell_count, nb)
    energy_piece = placed(gram(applied, own_block), gram(applied, partner))
    projected = butterfly_sum(energy_piece, "domain") * cell_weight
    return (filtered, correlation, projected)


def solution(mesh):
    placed = (P("domain", None, None, "band"), P("domain", None, None))
    return jax.shard_map(
        shards,
        mesh=mesh,
        in_specs=placed,
        out_specs=(P("domain", None, None, "band"), P("band", None), P("band", None)),
        check_vma=False,
    )
```

```python
import jax
import jax.numpy as jnp
from jax import lax
from jax.experimental import pallas as pl
from jax.experimental.pallas import tpu as pltpu
from jax.sharding import PartitionSpec as P

RADIUS = 4


stencil_weights = (-205.0 / 72.0, 8.0 / 5.0, -1.0 / 5.0, 8.0 / 315.0, -1.0 / 560.0)
spectrum_centre = 6.0
first_factor = -0.125
second_factor = -1.0 / 7.0
memory_factor = -1.0 / 7.0


def plane_blocks(planes):
    return (planes // RADIUS, RADIUS) if planes % RADIUS == 0 else (1, planes)


def interior_kernel(stage, planes, ny, nz):
    shift = 0.0 if stage == "applied" else spectrum_centre
    blocks, depth = plane_blocks(planes)

    def kernel(own_narrow, pot, out, own):
        step = pl.program_id(0)

        @pl.when(step == 0)
        def _():
            for x in range(planes):
                own[x] = own_narrow[x].astype(jnp.float32)

        for block in range(blocks):
            @pl.when(step == block)
            def _(block=block):
                for j in range(depth):
                    x = block * depth + j

                    def row(y, carry, x=x, j=j):
                        centre = own[x, y]
                        summed = (3.0 * stencil_weights[0]) * centre
                        for k in range(1, RADIUS + 1):
                            beside = own[x, (y + k) % ny] + own[x, (y + ny - k) % ny]
                            beside = beside + (
                                pltpu.roll(centre, k, 0) + pltpu.roll(centre, nz - k, 0)
                            )
                            if x + k < planes:
                                beside = beside + own[x + k, y]
                            if x - k >= 0:
                                beside = beside + own[x - k, y]
                            summed = summed + stencil_weights[k] * beside
                        applied = -0.5 * summed + pot[j, y] * centre
                        if shift:
                            applied = applied - shift * centre
                        out[j, y] = applied
                        return carry

                    lax.fori_loop(0, ny, row, 0)

    return kernel


def finish_kernel(stage, planes, ny):
    blocks, depth = plane_blocks(planes)

    def kernel(*refs):
        refs = list(refs)
        low, high, partial = refs[:3]
        initial = refs[3] if stage == "filtered" else None
        outs = refs[4:] if stage == "filtered" else refs[3:]
        out = outs[0]
        step = pl.program_id(0)
        for block in range(blocks):
            @pl.when(step == block)
            def _(block=block):
                for j in range(depth):
                    x = block * depth + j

                    def row(y, carry, x=x, j=j):
                        summed = partial[j, y]
                        for k in range(1, RADIUS + 1):
                            outside = []
                            if x + k >= planes:
                                outside.append(high[x + k - planes, y].astype(jnp.float32))
                            if x - k < 0:
                                outside.append(low[x - k + RADIUS, y].astype(jnp.float32))
                            if outside:
                                term = outside[0] if len(outside) == 1 else outside[0] + outside[1]
                                summed = summed + (-0.5 * stencil_weights[k]) * term
                        if stage == "first":
                            result = summed * first_factor
                        elif stage == "filtered":
                            result = summed * second_factor + (
                                memory_factor * initial[j, y].astype(jnp.float32)
                            )
                        else:
                            result = summed
                        result = result.astype(out.dtype)
                        out[j, y] = result
                        if len(outs) == 3:
                            if x >= planes - RADIUS:
                                outs[1][x - planes + RADIUS, y] = result
                            if x < RADIUS:
                                outs[2][x, y] = result
                        return carry

                    lax.fori_loop(0, ny, row, 0)

    return kernel


def stencil_stage(stage, block, sends, potential_wide, initial=None, keep_sends=True):
    planes, ny, nz, nb = block.shape
    blocks, depth = plane_blocks(planes)
    whole = pl.BlockSpec(block.shape, lambda i: (0, 0, 0, 0))
    edge = pl.BlockSpec((RADIUS, ny, nz, nb), lambda i: (0, 0, 0, 0))
    part = pl.BlockSpec((depth, ny, nz, nb), lambda i: (i, 0, 0, 0))
    low, high = exchange(sends, "domain")
    partial = pl.pallas_call(
        interior_kernel(stage, planes, ny, nz),
        grid=(blocks,),
        in_specs=[whole, part],
        out_specs=part,
        out_shape=jax.ShapeDtypeStruct(block.shape, jnp.float32),
        scratch_shapes=[pltpu.VMEM(block.shape, jnp.float32)],
        name=f"interior_{stage}",
    )(block, potential_wide)
    operands = [low, high, partial]
    in_specs = [edge, edge, part]
    if initial is not None:
        operands.append(initial)
        in_specs.append(part)
    shapes = [jax.ShapeDtypeStruct(block.shape, jnp.bfloat16)]
    out_specs = [part]
    if keep_sends:
        edge_shape = jax.ShapeDtypeStruct((RADIUS, ny, nz, nb), jnp.bfloat16)
        shapes += [edge_shape, edge_shape]
        out_specs += [edge, edge]
    return pl.pallas_call(
        finish_kernel(stage, planes, ny),
        grid=(blocks,),
        in_specs=in_specs,
        out_specs=tuple(out_specs),
        out_shape=tuple(shapes),
        name=f"finish_{stage}",
    )(*operands)


def exchange(sends, axis):
    count = lax.axis_size(axis)
    forward = [(i, (i + 1) % count) for i in range(count)]
    backward = [(target, source) for source, target in forward]
    return lax.ppermute(sends[0], axis, forward), lax.ppermute(sends[1], axis, backward)


def butterfly_sum(values, axis):
    count = lax.axis_size(axis)
    bit = 1
    while bit < count:
        pairs = [(i, i ^ bit) for i in range(count)]
        values = values + lax.ppermute(values, axis, pairs)
        bit *= 2
    return values


def shards(orbitals, potential):
    planes, ny, nz, nb = orbitals.shape
    potential_wide = jnp.broadcast_to(potential[:, :, :, None], (planes, ny, nz, nb))
    cell_count = planes * ny * nz
    cell_weight = 1.0 / (cell_count * lax.axis_size("domain"))
    band = lax.axis_index("band")
    gram = lambda rows, cols: jnp.einsum(
        "cb,ck->bk", rows, cols, preferred_element_type=jnp.float32
    )
    placed = lambda mine, theirs: jnp.where(
        band == 0,
        jnp.concatenate([mine, theirs], axis=1),
        jnp.concatenate([theirs, mine], axis=1),
    )
    planes_sent = (
        lax.slice_in_dim(orbitals, planes - RADIUS, None, axis=0),
        lax.slice_in_dim(orbitals, 0, RADIUS, axis=0),
    )
    first, *first_sent = stencil_stage("first", orbitals, planes_sent, potential_wide)
    filtered, *filtered_sent = stencil_stage(
        "filtered", first, first_sent, potential_wide, orbitals
    )
    own_block = filtered.reshape(cell_count, nb)
    partner = lax.ppermute(own_block, "band", [(0, 1), (1, 0)])
    correlation_piece = placed(gram(own_block, own_block), gram(own_block, partner))
    correlation = butterfly_sum(correlation_piece, "domain") * cell_weight
    (applied_grid,) = stencil_stage(
        "applied", filtered, filtered_sent, potential_wide, keep_sends=False
    )
    applied = applied_grid.reshape(cell_count, nb)
    energy_piece = placed(gram(applied, own_block), gram(applied, partner))
    projected = butterfly_sum(energy_piece, "domain") * cell_weight
    return (filtered, correlation, projected)


def solution(mesh):
    placed = (P("domain", None, None, "band"), P("domain", None, None))
    return jax.shard_map(
        shards,
        mesh=mesh,
        in_specs=placed,
        out_specs=(P("domain", None, None, "band"), P("band", None), P("band", None)),
        check_vma=False,
    )
```

```python
import jax
import jax.numpy as jnp
from jax import lax
from jax.experimental import pallas as pl
from jax.experimental.pallas import tpu as pltpu
from jax.sharding import PartitionSpec as P

RADIUS = 4


stencil_weights = (-205.0 / 72.0, 8.0 / 5.0, -1.0 / 5.0, 8.0 / 315.0, -1.0 / 560.0)
spectrum_centre = 6.0
first_factor = -0.125
second_factor = -1.0 / 7.0
memory_factor = -1.0 / 7.0


def plane_blocks(planes):
    return (planes // RADIUS, RADIUS) if planes % RADIUS == 0 else (1, planes)


def interior_kernel(stage, planes, ny, nz):
    shift = 0.0 if stage == "applied" else spectrum_centre
    blocks, depth = plane_blocks(planes)

    def kernel(own_narrow, pot, out, own):
        step = pl.program_id(0)

        @pl.when(step == 0)
        def _():
            for x in range(planes):
                own[x] = own_narrow[x].astype(jnp.float32)

        for block in range(blocks):
            @pl.when(step == block)
            def _(block=block):
                for j in range(depth):
                    x = block * depth + j

                    def row(y, carry, x=x, j=j):
                        centre = own[x, y]
                        summed = (3.0 * stencil_weights[0]) * centre
                        for k in range(1, RADIUS + 1):
                            beside = own[x, (y + k) % ny] + own[x, (y + ny - k) % ny]
                            beside = beside + (
                                pltpu.roll(centre, k, 0) + pltpu.roll(centre, nz - k, 0)
                            )
                            if x + k < planes:
                                beside = beside + own[x + k, y]
                            if x - k >= 0:
                                beside = beside + own[x - k, y]
                            summed = summed + stencil_weights[k] * beside
                        chosen = lax.broadcasted_iota(jnp.int32, (nz, ny), 1) == y
                        column = jnp.sum(
                            jnp.where(chosen, pot[x], 0.0), axis=1, keepdims=True
                        )
                        applied = -0.5 * summed + column * centre
                        if shift:
                            applied = applied - shift * centre
                        out[j, y] = applied
                        return carry

                    lax.fori_loop(0, ny, row, 0)

    return kernel


def finish_kernel(stage, planes, ny):
    blocks, depth = plane_blocks(planes)

    def kernel(*refs):
        refs = list(refs)
        low, high, partial = refs[:3]
        initial = refs[3] if stage == "filtered" else None
        outs = refs[4:] if stage == "filtered" else refs[3:]
        out = outs[0]
        step = pl.program_id(0)
        for block in range(blocks):
            @pl.when(step == block)
            def _(block=block):
                for j in range(depth):
                    x = block * depth + j

                    def row(y, carry, x=x, j=j):
                        summed = partial[j, y]
                        for k in range(1, RADIUS + 1):
                            outside = []
                            if x + k >= planes:
                                outside.append(high[x + k - planes, y].astype(jnp.float32))
                            if x - k < 0:
                                outside.append(low[x - k + RADIUS, y].astype(jnp.float32))
                            if outside:
                                term = outside[0] if len(outside) == 1 else outside[0] + outside[1]
                                summed = summed + (-0.5 * stencil_weights[k]) * term
                        if stage == "first":
                            result = summed * first_factor
                        elif stage == "filtered":
                            result = summed * second_factor + (
                                memory_factor * initial[j, y].astype(jnp.float32)
                            )
                        else:
                            result = summed
                        result = result.astype(out.dtype)
                        out[j, y] = result
                        if len(outs) == 3:
                            if x >= planes - RADIUS:
                                outs[1][x - planes + RADIUS, y] = result
                            if x < RADIUS:
                                outs[2][x, y] = result
                        return carry

                    lax.fori_loop(0, ny, row, 0)

    return kernel


def stencil_stage(stage, block, sends, potential_wide, initial=None, keep_sends=True):
    planes, ny, nz, nb = block.shape
    blocks, depth = plane_blocks(planes)
    whole = pl.BlockSpec(block.shape, lambda i: (0, 0, 0, 0))
    edge = pl.BlockSpec((RADIUS, ny, nz, nb), lambda i: (0, 0, 0, 0))
    part = pl.BlockSpec((depth, ny, nz, nb), lambda i: (i, 0, 0, 0))
    low, high = exchange(sends, "domain")
    potential_whole = pl.BlockSpec(potential_wide.shape, lambda i: (0, 0, 0))
    partial = pl.pallas_call(
        interior_kernel(stage, planes, ny, nz),
        grid=(blocks,),
        in_specs=[whole, potential_whole],
        out_specs=part,
        out_shape=jax.ShapeDtypeStruct(block.shape, jnp.float32),
        scratch_shapes=[pltpu.VMEM(block.shape, jnp.float32)],
        name=f"interior_{stage}",
    )(block, potential_wide)
    operands = [low, high, partial]
    in_specs = [edge, edge, part]
    if initial is not None:
        operands.append(initial)
        in_specs.append(part)
    shapes = [jax.ShapeDtypeStruct(block.shape, jnp.bfloat16)]
    out_specs = [part]
    if keep_sends:
        edge_shape = jax.ShapeDtypeStruct((RADIUS, ny, nz, nb), jnp.bfloat16)
        shapes += [edge_shape, edge_shape]
        out_specs += [edge, edge]
    return pl.pallas_call(
        finish_kernel(stage, planes, ny),
        grid=(blocks,),
        in_specs=in_specs,
        out_specs=tuple(out_specs),
        out_shape=tuple(shapes),
        name=f"finish_{stage}",
    )(*operands)


def exchange(sends, axis):
    count = lax.axis_size(axis)
    forward = [(i, (i + 1) % count) for i in range(count)]
    backward = [(target, source) for source, target in forward]
    return lax.ppermute(sends[0], axis, forward), lax.ppermute(sends[1], axis, backward)


def butterfly_sum(values, axis):
    count = lax.axis_size(axis)
    bit = 1
    while bit < count:
        pairs = [(i, i ^ bit) for i in range(count)]
        values = values + lax.ppermute(values, axis, pairs)
        bit *= 2
    return values


def shards(orbitals, potential):
    planes, ny, nz, nb = orbitals.shape
    potential_wide = jnp.swapaxes(potential, 1, 2)
    cell_count = planes * ny * nz
    cell_weight = 1.0 / (cell_count * lax.axis_size("domain"))
    band = lax.axis_index("band")
    gram = lambda rows, cols: jnp.einsum(
        "cb,ck->bk", rows, cols, preferred_element_type=jnp.float32
    )
    placed = lambda mine, theirs: jnp.where(
        band == 0,
        jnp.concatenate([mine, theirs], axis=1),
        jnp.concatenate([theirs, mine], axis=1),
    )
    planes_sent = (
        lax.slice_in_dim(orbitals, planes - RADIUS, None, axis=0),
        lax.slice_in_dim(orbitals, 0, RADIUS, axis=0),
    )
    first, *first_sent = stencil_stage("first", orbitals, planes_sent, potential_wide)
    filtered, *filtered_sent = stencil_stage(
        "filtered", first, first_sent, potential_wide, orbitals
    )
    own_block = filtered.reshape(cell_count, nb)
    partner = lax.ppermute(own_block, "band", [(0, 1), (1, 0)])
    correlation_piece = placed(gram(own_block, own_block), gram(own_block, partner))
    correlation = butterfly_sum(correlation_piece, "domain") * cell_weight
    (applied_grid,) = stencil_stage(
        "applied", filtered, filtered_sent, potential_wide, keep_sends=False
    )
    applied = applied_grid.reshape(cell_count, nb)
    energy_piece = placed(gram(applied, own_block), gram(applied, partner))
    projected = butterfly_sum(energy_piece, "domain") * cell_weight
    return (filtered, correlation, projected)


def solution(mesh):
    placed = (P("domain", None, None, "band"), P("domain", None, None))
    return jax.shard_map(
        shards,
        mesh=mesh,
        in_specs=placed,
        out_specs=(P("domain", None, None, "band"), P("band", None), P("band", None)),
        check_vma=False,
    )
```

```python
import jax
import jax.numpy as jnp
from jax import lax
from jax.experimental import pallas as pl
from jax.experimental.pallas import tpu as pltpu
from jax.sharding import PartitionSpec as P

RADIUS = 4


stencil_weights = (-205.0 / 72.0, 8.0 / 5.0, -1.0 / 5.0, 8.0 / 315.0, -1.0 / 560.0)
spectrum_centre = 6.0
first_factor = -0.125
second_factor = -1.0 / 7.0
memory_factor = -1.0 / 7.0


def plane_blocks(planes):
    return (planes // RADIUS, RADIUS) if planes % RADIUS == 0 else (1, planes)


def interior_kernel(stage, planes, ny, nz):
    shift = 0.0 if stage == "applied" else spectrum_centre
    blocks, depth = plane_blocks(planes)

    def kernel(own_narrow, pot, out, own):
        step = pl.program_id(0)

        @pl.when(step == 0)
        def _():
            for x in range(planes):
                own[x] = own_narrow[x].astype(jnp.float32)

        for block in range(blocks):
            @pl.when(step == block)
            def _(block=block):
                for j in range(depth):
                    x = block * depth + j

                    def row(y, carry, x=x, j=j):
                        centre = own[x, y]
                        summed = (3.0 * stencil_weights[0]) * centre
                        for k in range(1, RADIUS + 1):
                            beside = own[x, (y + k) % ny] + own[x, (y + ny - k) % ny]
                            beside = beside + (
                                pltpu.roll(centre, k, 0) + pltpu.roll(centre, nz - k, 0)
                            )
                            if x + k < planes:
                                beside = beside + own[x + k, y]
                            if x - k >= 0:
                                beside = beside + own[x - k, y]
                            summed = summed + stencil_weights[k] * beside
                        applied = -0.5 * summed + pot[j, y] * centre
                        if shift:
                            applied = applied - shift * centre
                        out[j, y] = applied
                        return carry

                    lax.fori_loop(0, ny, row, 0)

    return kernel


def finish_kernel(stage, planes, ny):
    blocks, depth = plane_blocks(planes)

    def kernel(*refs):
        refs = list(refs)
        low, high, partial = refs[:3]
        initial = refs[3] if stage == "filtered" else None
        outs = refs[4:] if stage == "filtered" else refs[3:]
        out = outs[0]
        step = pl.program_id(0)
        for block in range(blocks):
            @pl.when(step == block)
            def _(block=block):
                for j in range(depth):
                    x = block * depth + j

                    def row(y, carry, x=x, j=j):
                        summed = partial[j, y]
                        for k in range(1, RADIUS + 1):
                            outside = []
                            if x + k >= planes:
                                outside.append(high[x + k - planes, y].astype(jnp.float32))
                            if x - k < 0:
                                outside.append(low[x - k + RADIUS, y].astype(jnp.float32))
                            if outside:
                                term = outside[0] if len(outside) == 1 else outside[0] + outside[1]
                                summed = summed + (-0.5 * stencil_weights[k]) * term
                        if stage == "first":
                            result = summed * first_factor
                        elif stage == "filtered":
                            result = summed * second_factor + (
                                memory_factor * initial[j, y].astype(jnp.float32)
                            )
                        else:
                            result = summed
                        result = result.astype(out.dtype)
                        out[j, y] = result
                        if len(outs) == 3:
                            if x >= planes - RADIUS:
                                outs[1][x - planes + RADIUS, y] = result
                            if x < RADIUS:
                                outs[2][x, y] = result
                        return carry

                    lax.fori_loop(0, ny, row, 0)

    return kernel


def stencil_stage(stage, block, sends, potential_wide, initial=None, keep_sends=True):
    planes, ny, nz, nb = block.shape
    blocks, depth = plane_blocks(planes)
    whole = pl.BlockSpec(block.shape, lambda i: (0, 0, 0, 0))
    edge = pl.BlockSpec((RADIUS, ny, nz, nb), lambda i: (0, 0, 0, 0))
    part = pl.BlockSpec((depth, ny, nz, nb), lambda i: (i, 0, 0, 0))
    low, high = exchange(sends, "domain")
    partial = pl.pallas_call(
        interior_kernel(stage, planes, ny, nz),
        grid=(blocks,),
        in_specs=[whole, part],
        out_specs=part,
        out_shape=jax.ShapeDtypeStruct(block.shape, jnp.float32),
        scratch_shapes=[pltpu.VMEM(block.shape, jnp.float32)],
        name=f"interior_{stage}",
    )(block, potential_wide)
    operands = [low, high, partial]
    in_specs = [edge, edge, part]
    if initial is not None:
        operands.append(initial)
        in_specs.append(part)
    shapes = [jax.ShapeDtypeStruct(block.shape, jnp.bfloat16)]
    out_specs = [part]
    if keep_sends:
        edge_shape = jax.ShapeDtypeStruct((RADIUS, ny, nz, nb), jnp.bfloat16)
        shapes += [edge_shape, edge_shape]
        out_specs += [edge, edge]
    return pl.pallas_call(
        finish_kernel(stage, planes, ny),
        grid=(blocks,),
        in_specs=in_specs,
        out_specs=tuple(out_specs),
        out_shape=tuple(shapes),
        name=f"finish_{stage}",
    )(*operands)


def exchange(sends, axis):
    count = lax.axis_size(axis)
    forward = [(i, (i + 1) % count) for i in range(count)]
    backward = [(target, source) for source, target in forward]
    return lax.ppermute(sends[0], axis, forward), lax.ppermute(sends[1], axis, backward)


def interior_halves_kernel(stage, planes, ny, nz, parts):
    shift = 0.0 if stage == "applied" else spectrum_centre
    blocks, depth = plane_blocks(planes)

    def kernel(*refs):
        narrow = refs[:parts]
        pot, out, own = refs[parts:]
        step = pl.program_id(0)

        @pl.when(step == 0)
        def _():
            for x in range(planes):
                if parts == 1:
                    own[x] = narrow[0][x].astype(jnp.float32)
                else:
                    own[x] = narrow[x // depth][x % depth].astype(jnp.float32)

        for block in range(blocks):
            @pl.when(step == block)
            def _(block=block):
                for j in range(depth):
                    x = block * depth + j

                    def row(y, carry, x=x, j=j):
                        centre = own[x, y]
                        summed = (3.0 * stencil_weights[0]) * centre
                        for k in range(1, RADIUS + 1):
                            beside = own[x, (y + k) % ny] + own[x, (y + ny - k) % ny]
                            beside = beside + (
                                pltpu.roll(centre, k, 0) + pltpu.roll(centre, nz - k, 0)
                            )
                            if x + k < planes:
                                beside = beside + own[x + k, y]
                            if x - k >= 0:
                                beside = beside + own[x - k, y]
                            summed = summed + stencil_weights[k] * beside
                        applied = -0.5 * summed + pot[j, y] * centre
                        if shift:
                            applied = applied - shift * centre
                        out[j, y] = applied
                        return carry

                    lax.fori_loop(0, ny, row, 0)

    return kernel


def finish_half_kernel(stage, planes, ny, half):
    def kernel(*refs):
        halo, partial = refs[:2]
        initial = refs[2] if stage == "filtered" else None
        out = refs[-1]
        for j in range(RADIUS):
            x = half * RADIUS + j

            def row(y, carry, x=x, j=j):
                summed = partial[j, y]
                for k in range(1, RADIUS + 1):
                    if x + k >= planes:
                        summed = summed + (-0.5 * stencil_weights[k]) * halo[
                            x + k - planes, y
                        ].astype(jnp.float32)
                    if x - k < 0:
                        summed = summed + (-0.5 * stencil_weights[k]) * halo[
                            x - k + RADIUS, y
                        ].astype(jnp.float32)
                if stage == "first":
                    result = summed * first_factor
                elif stage == "filtered":
                    result = summed * second_factor + (
                        memory_factor * initial[j, y].astype(jnp.float32)
                    )
                else:
                    result = summed
                out[j, y] = result.astype(out.dtype)
                return carry

            lax.fori_loop(0, ny, row, 0)

    return kernel


def stencil_halves(stage, halves, potential_wide, initial=None):
    parts = len(halves)
    if parts == 1:
        planes, ny, nz, nb = halves[0].shape
        lower = lax.slice_in_dim(halves[0], 0, RADIUS, axis=0)
        upper = lax.slice_in_dim(halves[0], RADIUS, None, axis=0)
    else:
        lower, upper = halves
        ny, nz, nb = lower.shape[1:]
        planes = 2 * RADIUS
    blocks, depth = plane_blocks(planes)
    count = lax.axis_size("domain")
    forward = [(i, (i + 1) % count) for i in range(count)]
    backward = [(target, source) for source, target in forward]
    below = lax.ppermute(upper, "domain", forward)
    above = lax.ppermute(lower, "domain", backward)
    part = pl.BlockSpec((depth, ny, nz, nb), lambda i: (i, 0, 0, 0))
    narrow_specs = [pl.BlockSpec(h.shape, lambda i: (0, 0, 0, 0)) for h in halves]
    partial = pl.pallas_call(
        interior_halves_kernel(stage, planes, ny, nz, parts),
        grid=(blocks,),
        in_specs=narrow_specs + [part],
        out_specs=part,
        out_shape=jax.ShapeDtypeStruct((planes, ny, nz, nb), jnp.float32),
        scratch_shapes=[pltpu.VMEM((planes, ny, nz, nb), jnp.float32)],
        name=f"interior_{stage}",
    )(*halves, potential_wide)
    results = []
    for half, halo in ((0, below), (1, above)):
        chosen = pl.BlockSpec((RADIUS, ny, nz, nb), lambda i, half=half: (half, 0, 0, 0))
        edge = pl.BlockSpec((RADIUS, ny, nz, nb), lambda i: (0, 0, 0, 0))
        operands = [halo, partial]
        in_specs = [edge, chosen]
        if initial is not None:
            operands.append(initial)
            in_specs.append(chosen)
        results.append(
            pl.pallas_call(
                finish_half_kernel(stage, planes, ny, half),
                grid=(1,),
                in_specs=in_specs,
                out_specs=edge,
                out_shape=jax.ShapeDtypeStruct((RADIUS, ny, nz, nb), jnp.bfloat16),
                name=f"finish_{stage}_{half}",
            )(*operands)
        )
    return results


def butterfly_sum(values, axis):
    count = lax.axis_size(axis)
    bit = 1
    while bit < count:
        pairs = [(i, i ^ bit) for i in range(count)]
        values = values + lax.ppermute(values, axis, pairs)
        bit *= 2
    return values


def shards(orbitals, potential):
    planes, ny, nz, nb = orbitals.shape
    potential_wide = jnp.broadcast_to(potential[:, :, :, None], (planes, ny, nz, nb))
    cell_count = planes * ny * nz
    cell_weight = 1.0 / (cell_count * lax.axis_size("domain"))
    band = lax.axis_index("band")
    gram = lambda rows, cols: jnp.einsum(
        "cb,ck->bk", rows, cols, preferred_element_type=jnp.float32
    )
    placed = lambda mine, theirs: jnp.where(
        band == 0,
        jnp.concatenate([mine, theirs], axis=1),
        jnp.concatenate([theirs, mine], axis=1),
    )
    if planes == 2 * RADIUS:
        first_halves = stencil_halves("first", [orbitals], potential_wide)
        filtered_halves = stencil_halves("filtered", first_halves, potential_wide, orbitals)
        filtered = jnp.concatenate(filtered_halves, axis=0)
    else:
        planes_sent = (
            lax.slice_in_dim(orbitals, planes - RADIUS, None, axis=0),
            lax.slice_in_dim(orbitals, 0, RADIUS, axis=0),
        )
        first, *first_sent = stencil_stage("first", orbitals, planes_sent, potential_wide)
        filtered, *filtered_sent = stencil_stage(
            "filtered", first, first_sent, potential_wide, orbitals
        )
    own_block = filtered.reshape(cell_count, nb)
    partner = lax.ppermute(own_block, "band", [(0, 1), (1, 0)])
    correlation_piece = placed(gram(own_block, own_block), gram(own_block, partner))
    correlation = butterfly_sum(correlation_piece, "domain") * cell_weight
    if planes == 2 * RADIUS:
        applied_grid = jnp.concatenate(
            stencil_halves("applied", filtered_halves, potential_wide), axis=0
        )
    else:
        (applied_grid,) = stencil_stage(
            "applied", filtered, filtered_sent, potential_wide, keep_sends=False
        )
    applied = applied_grid.reshape(cell_count, nb)
    energy_piece = placed(gram(applied, own_block), gram(applied, partner))
    projected = butterfly_sum(energy_piece, "domain") * cell_weight
    return (filtered, correlation, projected)


def solution(mesh):
    placed = (P("domain", None, None, "band"), P("domain", None, None))
    return jax.shard_map(
        shards,
        mesh=mesh,
        in_specs=placed,
        out_specs=(P("domain", None, None, "band"), P("band", None), P("band", None)),
        check_vma=False,
    )
```

```python
import jax
import jax.numpy as jnp
from jax import lax
from jax.experimental import pallas as pl
from jax.experimental.pallas import tpu as pltpu
from jax.sharding import PartitionSpec as P

RADIUS = 4


stencil_weights = (-205.0 / 72.0, 8.0 / 5.0, -1.0 / 5.0, 8.0 / 315.0, -1.0 / 560.0)
spectrum_centre = 6.0
first_factor = -0.125
second_factor = -1.0 / 7.0
memory_factor = -1.0 / 7.0


def plane_blocks(planes):
    return (planes // RADIUS, RADIUS) if planes % RADIUS == 0 else (1, planes)


def interior_kernel(stage, planes, ny, nz):
    shift = 0.0 if stage == "applied" else spectrum_centre
    blocks, depth = plane_blocks(planes)

    def kernel(own_narrow, pot, out, own):
        step = pl.program_id(0)

        @pl.when(step == 0)
        def _():
            for x in range(planes):
                own[x] = own_narrow[x].astype(jnp.float32)

        for block in range(blocks):
            @pl.when(step == block)
            def _(block=block):
                for j in range(depth):
                    x = block * depth + j

                    def row(y, carry, x=x, j=j):
                        centre = own[x, y]
                        summed = (3.0 * stencil_weights[0]) * centre
                        for k in range(1, RADIUS + 1):
                            beside = own[x, (y + k) % ny] + own[x, (y + ny - k) % ny]
                            beside = beside + (
                                pltpu.roll(centre, k, 0) + pltpu.roll(centre, nz - k, 0)
                            )
                            if x + k < planes:
                                beside = beside + own[x + k, y]
                            if x - k >= 0:
                                beside = beside + own[x - k, y]
                            summed = summed + stencil_weights[k] * beside
                        applied = -0.5 * summed + pot[j, y] * centre
                        if shift:
                            applied = applied - shift * centre
                        out[j, y] = applied
                        return carry

                    lax.fori_loop(0, ny, row, 0)

    return kernel


def finish_kernel(stage, planes, ny):
    blocks, depth = plane_blocks(planes)

    def kernel(*refs):
        refs = list(refs)
        low, partial = refs[:2]
        high = low
        initial = refs[2] if stage == "filtered" else None
        outs = refs[3:] if stage == "filtered" else refs[2:]
        out = outs[0]
        step = pl.program_id(0)
        for block in range(blocks):
            @pl.when(step == block)
            def _(block=block):
                for j in range(depth):
                    x = block * depth + j

                    def row(y, carry, x=x, j=j):
                        summed = partial[j, y]
                        for k in range(1, RADIUS + 1):
                            outside = []
                            if x + k >= planes:
                                outside.append(high[x + k - planes, y].astype(jnp.float32))
                            if x - k < 0:
                                outside.append(low[x - k + RADIUS, y].astype(jnp.float32))
                            if outside:
                                term = outside[0] if len(outside) == 1 else outside[0] + outside[1]
                                summed = summed + (-0.5 * stencil_weights[k]) * term
                        if stage == "first":
                            result = summed * first_factor
                        elif stage == "filtered":
                            result = summed * second_factor + (
                                memory_factor * initial[j, y].astype(jnp.float32)
                            )
                        else:
                            result = summed
                        result = result.astype(out.dtype)
                        out[j, y] = result
                        if len(outs) == 3:
                            if x >= planes - RADIUS:
                                outs[1][x - planes + RADIUS, y] = result
                            if x < RADIUS:
                                outs[2][x, y] = result
                        return carry

                    lax.fori_loop(0, ny, row, 0)

    return kernel


def stencil_stage(stage, block, sends, potential_wide, initial=None, keep_sends=True):
    planes, ny, nz, nb = block.shape
    blocks, depth = plane_blocks(planes)
    if blocks < 2:
        return stencil_stage_whole(stage, block, sends, potential_wide, initial, keep_sends)
    whole = pl.BlockSpec(block.shape, lambda i: (0, 0, 0, 0))
    edge = pl.BlockSpec((RADIUS, ny, nz, nb), lambda i: (0, 0, 0, 0))
    part = pl.BlockSpec((depth, ny, nz, nb), lambda i: (i, 0, 0, 0))
    low, high = exchange(sends, "domain")
    partial = pl.pallas_call(
        interior_kernel(stage, planes, ny, nz),
        grid=(blocks,),
        in_specs=[whole, part],
        out_specs=part,
        out_shape=jax.ShapeDtypeStruct(block.shape, jnp.float32),
        scratch_shapes=[pltpu.VMEM(block.shape, jnp.float32)],
        name=f"interior_{stage}",
    )(block, potential_wide)
    halos = jnp.concatenate([low, high], axis=0)
    halo_block = pl.BlockSpec((RADIUS, ny, nz, nb), lambda i: (jnp.minimum(i, 1), 0, 0, 0))
    operands = [halos, partial]
    in_specs = [halo_block, part]
    if initial is not None:
        operands.append(initial)
        in_specs.append(part)
    shapes = [jax.ShapeDtypeStruct(block.shape, jnp.bfloat16)]
    out_specs = [part]
    if keep_sends:
        edge_shape = jax.ShapeDtypeStruct((RADIUS, ny, nz, nb), jnp.bfloat16)
        shapes += [edge_shape, edge_shape]
        out_specs += [edge, edge]
    return pl.pallas_call(
        finish_kernel(stage, planes, ny),
        grid=(blocks,),
        in_specs=in_specs,
        out_specs=tuple(out_specs),
        out_shape=tuple(shapes),
        name=f"finish_{stage}",
    )(*operands)


def finish_kernel_whole(stage, planes, ny):
    blocks, depth = plane_blocks(planes)

    def kernel(*refs):
        refs = list(refs)
        low, high, partial = refs[:3]
        initial = refs[3] if stage == "filtered" else None
        outs = refs[4:] if stage == "filtered" else refs[3:]
        out = outs[0]
        step = pl.program_id(0)
        for block in range(blocks):
            @pl.when(step == block)
            def _(block=block):
                for j in range(depth):
                    x = block * depth + j

                    def row(y, carry, x=x, j=j):
                        summed = partial[j, y]
                        for k in range(1, RADIUS + 1):
                            outside = []
                            if x + k >= planes:
                                outside.append(high[x + k - planes, y].astype(jnp.float32))
                            if x - k < 0:
                                outside.append(low[x - k + RADIUS, y].astype(jnp.float32))
                            if outside:
                                term = outside[0] if len(outside) == 1 else outside[0] + outside[1]
                                summed = summed + (-0.5 * stencil_weights[k]) * term
                        if stage == "first":
                            result = summed * first_factor
                        elif stage == "filtered":
                            result = summed * second_factor + (
                                memory_factor * initial[j, y].astype(jnp.float32)
                            )
                        else:
                            result = summed
                        result = result.astype(out.dtype)
                        out[j, y] = result
                        if len(outs) == 3:
                            if x >= planes - RADIUS:
                                outs[1][x - planes + RADIUS, y] = result
                            if x < RADIUS:
                                outs[2][x, y] = result
                        return carry

                    lax.fori_loop(0, ny, row, 0)

    return kernel


def stencil_stage_whole(stage, block, sends, potential_wide, initial=None, keep_sends=True):
    planes, ny, nz, nb = block.shape
    blocks, depth = plane_blocks(planes)
    whole = pl.BlockSpec(block.shape, lambda i: (0, 0, 0, 0))
    edge = pl.BlockSpec((RADIUS, ny, nz, nb), lambda i: (0, 0, 0, 0))
    part = pl.BlockSpec((depth, ny, nz, nb), lambda i: (i, 0, 0, 0))
    low, high = exchange(sends, "domain")
    partial = pl.pallas_call(
        interior_kernel(stage, planes, ny, nz),
        grid=(blocks,),
        in_specs=[whole, part],
        out_specs=part,
        out_shape=jax.ShapeDtypeStruct(block.shape, jnp.float32),
        scratch_shapes=[pltpu.VMEM(block.shape, jnp.float32)],
        name=f"interior_{stage}",
    )(block, potential_wide)
    operands = [low, high, partial]
    in_specs = [edge, edge, part]
    if initial is not None:
        operands.append(initial)
        in_specs.append(part)
    shapes = [jax.ShapeDtypeStruct(block.shape, jnp.bfloat16)]
    out_specs = [part]
    if keep_sends:
        edge_shape = jax.ShapeDtypeStruct((RADIUS, ny, nz, nb), jnp.bfloat16)
        shapes += [edge_shape, edge_shape]
        out_specs += [edge, edge]
    return pl.pallas_call(
        finish_kernel_whole(stage, planes, ny),
        grid=(blocks,),
        in_specs=in_specs,
        out_specs=tuple(out_specs),
        out_shape=tuple(shapes),
        name=f"finish_{stage}",
    )(*operands)


def exchange(sends, axis):
    count = lax.axis_size(axis)
    forward = [(i, (i + 1) % count) for i in range(count)]
    backward = [(target, source) for source, target in forward]
    return lax.ppermute(sends[0], axis, forward), lax.ppermute(sends[1], axis, backward)


def butterfly_sum(values, axis):
    count = lax.axis_size(axis)
    bit = 1
    while bit < count:
        pairs = [(i, i ^ bit) for i in range(count)]
        values = values + lax.ppermute(values, axis, pairs)
        bit *= 2
    return values


def shards(orbitals, potential):
    planes, ny, nz, nb = orbitals.shape
    potential_wide = jnp.broadcast_to(potential[:, :, :, None], (planes, ny, nz, nb))
    cell_count = planes * ny * nz
    cell_weight = 1.0 / (cell_count * lax.axis_size("domain"))
    band = lax.axis_index("band")
    gram = lambda rows, cols: jnp.einsum(
        "cb,ck->bk", rows, cols, preferred_element_type=jnp.float32
    )
    placed = lambda mine, theirs: jnp.where(
        band == 0,
        jnp.concatenate([mine, theirs], axis=1),
        jnp.concatenate([theirs, mine], axis=1),
    )
    planes_sent = (
        lax.slice_in_dim(orbitals, planes - RADIUS, None, axis=0),
        lax.slice_in_dim(orbitals, 0, RADIUS, axis=0),
    )
    first, *first_sent = stencil_stage("first", orbitals, planes_sent, potential_wide)
    filtered, *filtered_sent = stencil_stage(
        "filtered", first, first_sent, potential_wide, orbitals
    )
    own_block = filtered.reshape(cell_count, nb)
    partner = lax.ppermute(own_block, "band", [(0, 1), (1, 0)])
    correlation_piece = placed(gram(own_block, own_block), gram(own_block, partner))
    correlation = butterfly_sum(correlation_piece, "domain") * cell_weight
    (applied_grid,) = stencil_stage(
        "applied", filtered, filtered_sent, potential_wide, keep_sends=False
    )
    applied = applied_grid.reshape(cell_count, nb)
    energy_piece = placed(gram(applied, own_block), gram(applied, partner))
    projected = butterfly_sum(energy_piece, "domain") * cell_weight
    return (filtered, correlation, projected)


def solution(mesh):
    placed = (P("domain", None, None, "band"), P("domain", None, None))
    return jax.shard_map(
        shards,
        mesh=mesh,
        in_specs=placed,
        out_specs=(P("domain", None, None, "band"), P("band", None), P("band", None)),
        check_vma=False,
    )
```

```python
import jax
import jax.numpy as jnp
from jax import lax
from jax.experimental import pallas as pl
from jax.experimental.pallas import tpu as pltpu
from jax.experimental.layout import Layout, with_layout_constraint
from jax.sharding import PartitionSpec as P

RADIUS = 4


stencil_weights = (-205.0 / 72.0, 8.0 / 5.0, -1.0 / 5.0, 8.0 / 315.0, -1.0 / 560.0)
spectrum_centre = 6.0
first_factor = -0.125
second_factor = -1.0 / 7.0
memory_factor = -1.0 / 7.0


def plane_blocks(planes):
    return (planes // RADIUS, RADIUS) if planes % RADIUS == 0 else (1, planes)


def interior_kernel(stage, planes, ny, nz):
    shift = 0.0 if stage == "applied" else spectrum_centre
    blocks, depth = plane_blocks(planes)

    def kernel(own_narrow, pot, out, own):
        step = pl.program_id(0)

        @pl.when(step == 0)
        def _():
            for x in range(planes):
                own[x] = own_narrow[x].astype(jnp.float32)

        for block in range(blocks):
            @pl.when(step == block)
            def _(block=block):
                for j in range(depth):
                    x = block * depth + j

                    def row(y, carry, x=x, j=j):
                        centre = own[x, y]
                        summed = (3.0 * stencil_weights[0]) * centre
                        for k in range(1, RADIUS + 1):
                            beside = own[x, (y + k) % ny] + own[x, (y + ny - k) % ny]
                            beside = beside + (
                                pltpu.roll(centre, k, 0) + pltpu.roll(centre, nz - k, 0)
                            )
                            if x + k < planes:
                                beside = beside + own[x + k, y]
                            if x - k >= 0:
                                beside = beside + own[x - k, y]
                            summed = summed + stencil_weights[k] * beside
                        applied = -0.5 * summed + pot[j, y] * centre
                        if shift:
                            applied = applied - shift * centre
                        out[j, y] = applied
                        return carry

                    lax.fori_loop(0, ny, row, 0)

    return kernel


def finish_kernel(stage, planes, ny):
    blocks, depth = plane_blocks(planes)

    def kernel(*refs):
        refs = list(refs)
        low, partial = refs[:2]
        high = low
        initial = refs[2] if stage == "filtered" else None
        outs = refs[3:] if stage == "filtered" else refs[2:]
        out = outs[0]
        step = pl.program_id(0)
        for block in range(blocks):
            @pl.when(step == block)
            def _(block=block):
                for j in range(depth):
                    x = block * depth + j

                    def row(y, carry, x=x, j=j):
                        summed = partial[j, y]
                        for k in range(1, RADIUS + 1):
                            outside = []
                            if x + k >= planes:
                                outside.append(high[x + k - planes, y].astype(jnp.float32))
                            if x - k < 0:
                                outside.append(low[x - k + RADIUS, y].astype(jnp.float32))
                            if outside:
                                term = outside[0] if len(outside) == 1 else outside[0] + outside[1]
                                summed = summed + (-0.5 * stencil_weights[k]) * term
                        if stage == "first":
                            result = summed * first_factor
                        elif stage == "filtered":
                            result = summed * second_factor + (
                                memory_factor * initial[j, y].astype(jnp.float32)
                            )
                        else:
                            result = summed
                        result = result.astype(out.dtype)
                        out[j, y] = result
                        if len(outs) == 3:
                            if x >= planes - RADIUS:
                                outs[1][x - planes + RADIUS, y] = result
                            if x < RADIUS:
                                outs[2][x, y] = result
                        return carry

                    lax.fori_loop(0, ny, row, 0)

    return kernel


def stencil_stage(stage, block, sends, potential_wide, initial=None, keep_sends=True):
    planes, ny, nz, nb = block.shape
    blocks, depth = plane_blocks(planes)
    if blocks < 2:
        return stencil_stage_whole(stage, block, sends, potential_wide, initial, keep_sends)
    whole = pl.BlockSpec(block.shape, lambda i: (0, 0, 0, 0))
    edge = pl.BlockSpec((RADIUS, ny, nz, nb), lambda i: (0, 0, 0, 0))
    part = pl.BlockSpec((depth, ny, nz, nb), lambda i: (i, 0, 0, 0))
    low, high = exchange(sends, "domain")
    partial = pl.pallas_call(
        interior_kernel(stage, planes, ny, nz),
        grid=(blocks,),
        in_specs=[whole, part],
        out_specs=part,
        out_shape=jax.ShapeDtypeStruct(block.shape, jnp.float32),
        scratch_shapes=[pltpu.VMEM(block.shape, jnp.float32)],
        name=f"interior_{stage}",
    )(block, potential_wide)
    halos = jnp.concatenate([low, high], axis=0)
    halo_block = pl.BlockSpec((RADIUS, ny, nz, nb), lambda i: (jnp.minimum(i, 1), 0, 0, 0))
    operands = [halos, partial]
    in_specs = [halo_block, part]
    if initial is not None:
        operands.append(initial)
        in_specs.append(part)
    shapes = [jax.ShapeDtypeStruct(block.shape, jnp.bfloat16)]
    out_specs = [part]
    if keep_sends:
        edge_shape = jax.ShapeDtypeStruct((RADIUS, ny, nz, nb), jnp.bfloat16)
        shapes += [edge_shape, edge_shape]
        out_specs += [edge, edge]
    return pl.pallas_call(
        finish_kernel(stage, planes, ny),
        grid=(blocks,),
        in_specs=in_specs,
        out_specs=tuple(out_specs),
        out_shape=tuple(shapes),
        name=f"finish_{stage}",
    )(*operands)


def finish_kernel_whole(stage, planes, ny):
    blocks, depth = plane_blocks(planes)

    def kernel(*refs):
        refs = list(refs)
        low, high, partial = refs[:3]
        initial = refs[3] if stage == "filtered" else None
        outs = refs[4:] if stage == "filtered" else refs[3:]
        out = outs[0]
        step = pl.program_id(0)
        for block in range(blocks):
            @pl.when(step == block)
            def _(block=block):
                for j in range(depth):
                    x = block * depth + j

                    def row(y, carry, x=x, j=j):
                        summed = partial[j, y]
                        for k in range(1, RADIUS + 1):
                            outside = []
                            if x + k >= planes:
                                outside.append(high[x + k - planes, y].astype(jnp.float32))
                            if x - k < 0:
                                outside.append(low[x - k + RADIUS, y].astype(jnp.float32))
                            if outside:
                                term = outside[0] if len(outside) == 1 else outside[0] + outside[1]
                                summed = summed + (-0.5 * stencil_weights[k]) * term
                        if stage == "first":
                            result = summed * first_factor
                        elif stage == "filtered":
                            result = summed * second_factor + (
                                memory_factor * initial[j, y].astype(jnp.float32)
                            )
                        else:
                            result = summed
                        result = result.astype(out.dtype)
                        out[j, y] = result
                        if len(outs) == 3:
                            if x >= planes - RADIUS:
                                outs[1][x - planes + RADIUS, y] = result
                            if x < RADIUS:
                                outs[2][x, y] = result
                        return carry

                    lax.fori_loop(0, ny, row, 0)

    return kernel


def stencil_stage_whole(stage, block, sends, potential_wide, initial=None, keep_sends=True):
    planes, ny, nz, nb = block.shape
    blocks, depth = plane_blocks(planes)
    whole = pl.BlockSpec(block.shape, lambda i: (0, 0, 0, 0))
    edge = pl.BlockSpec((RADIUS, ny, nz, nb), lambda i: (0, 0, 0, 0))
    part = pl.BlockSpec((depth, ny, nz, nb), lambda i: (i, 0, 0, 0))
    low, high = exchange(sends, "domain")
    partial = pl.pallas_call(
        interior_kernel(stage, planes, ny, nz),
        grid=(blocks,),
        in_specs=[whole, part],
        out_specs=part,
        out_shape=jax.ShapeDtypeStruct(block.shape, jnp.float32),
        scratch_shapes=[pltpu.VMEM(block.shape, jnp.float32)],
        name=f"interior_{stage}",
    )(block, potential_wide)
    operands = [low, high, partial]
    in_specs = [edge, edge, part]
    if initial is not None:
        operands.append(initial)
        in_specs.append(part)
    shapes = [jax.ShapeDtypeStruct(block.shape, jnp.bfloat16)]
    out_specs = [part]
    if keep_sends:
        edge_shape = jax.ShapeDtypeStruct((RADIUS, ny, nz, nb), jnp.bfloat16)
        shapes += [edge_shape, edge_shape]
        out_specs += [edge, edge]
    return pl.pallas_call(
        finish_kernel_whole(stage, planes, ny),
        grid=(blocks,),
        in_specs=in_specs,
        out_specs=tuple(out_specs),
        out_shape=tuple(shapes),
        name=f"finish_{stage}",
    )(*operands)


def exchange(sends, axis):
    count = lax.axis_size(axis)
    forward = [(i, (i + 1) % count) for i in range(count)]
    backward = [(target, source) for source, target in forward]
    return lax.ppermute(sends[0], axis, forward), lax.ppermute(sends[1], axis, backward)


def butterfly_sum(values, axis):
    count = lax.axis_size(axis)
    bit = 1
    while bit < count:
        pairs = [(i, i ^ bit) for i in range(count)]
        values = values + lax.ppermute(values, axis, pairs)
        bit *= 2
    return values


def shards(orbitals, potential):
    planes, ny, nz, nb = orbitals.shape
    potential_wide = jnp.broadcast_to(potential[:, :, :, None], (planes, ny, nz, nb))
    cell_count = planes * ny * nz
    cell_weight = 1.0 / (cell_count * lax.axis_size("domain"))
    band = lax.axis_index("band")
    gram = lambda rows, cols: with_layout_constraint(
        jnp.einsum("cb,ck->bk", rows, cols, preferred_element_type=jnp.float32),
        Layout((0, 1)),
    )
    placed = lambda mine, theirs: jnp.where(
        band == 0,
        jnp.concatenate([mine, theirs], axis=1),
        jnp.concatenate([theirs, mine], axis=1),
    )
    planes_sent = (
        lax.slice_in_dim(orbitals, planes - RADIUS, None, axis=0),
        lax.slice_in_dim(orbitals, 0, RADIUS, axis=0),
    )
    first, *first_sent = stencil_stage("first", orbitals, planes_sent, potential_wide)
    filtered, *filtered_sent = stencil_stage(
        "filtered", first, first_sent, potential_wide, orbitals
    )
    own_block = filtered.reshape(cell_count, nb)
    partner = lax.ppermute(own_block, "band", [(0, 1), (1, 0)])
    correlation_piece = placed(gram(own_block, own_block), gram(own_block, partner))
    correlation = butterfly_sum(correlation_piece, "domain") * cell_weight
    (applied_grid,) = stencil_stage(
        "applied", filtered, filtered_sent, potential_wide, keep_sends=False
    )
    applied = applied_grid.reshape(cell_count, nb)
    energy_piece = placed(gram(applied, own_block), gram(applied, partner))
    projected = butterfly_sum(energy_piece, "domain") * cell_weight
    return (filtered, correlation, projected)


def solution(mesh):
    placed = (P("domain", None, None, "band"), P("domain", None, None))
    return jax.shard_map(
        shards,
        mesh=mesh,
        in_specs=placed,
        out_specs=(P("domain", None, None, "band"), P("band", None), P("band", None)),
        check_vma=False,
    )
```

```python
import jax
import jax.numpy as jnp
from jax import lax
from jax.experimental import pallas as pl
from jax.experimental.pallas import tpu as pltpu
from jax.experimental.layout import Layout, with_layout_constraint
from jax.sharding import PartitionSpec as P

RADIUS = 4


stencil_weights = (-205.0 / 72.0, 8.0 / 5.0, -1.0 / 5.0, 8.0 / 315.0, -1.0 / 560.0)
spectrum_centre = 6.0
first_factor = -0.125
second_factor = -1.0 / 7.0
memory_factor = -1.0 / 7.0


def plane_blocks(planes):
    return (planes // RADIUS, RADIUS) if planes % RADIUS == 0 else (1, planes)


def interior_kernel(stage, planes, ny, nz):
    shift = 0.0 if stage == "applied" else spectrum_centre
    blocks, depth = plane_blocks(planes)

    def kernel(own_narrow, pot_t, out, own, pot):
        step = pl.program_id(0)
        nb = out.shape[-1]
        lanes = lax.broadcasted_iota(jnp.int32, (ny, ny * nb), 1)
        rows = lax.broadcasted_iota(jnp.int32, (ny, ny * nb), 0)
        select = (lanes // nb == rows).astype(jnp.float32)

        @pl.when(step == 0)
        def _():
            for x in range(planes):
                own[x] = own_narrow[x].astype(jnp.float32)

        for block in range(blocks):
            @pl.when(step == block)
            def _(block=block):
                for j in range(depth):
                    x = block * depth + j
                    spread = jnp.dot(
                        pot_t[x],
                        select,
                        precision=lax.Precision.HIGHEST,
                        preferred_element_type=jnp.float32,
                    )
                    for y in range(ny):
                        pot[y] = spread[:, y * nb:(y + 1) * nb]

                    def row(y, carry, x=x, j=j):
                        centre = own[x, y]
                        summed = (3.0 * stencil_weights[0]) * centre
                        for k in range(1, RADIUS + 1):
                            beside = own[x, (y + k) % ny] + own[x, (y + ny - k) % ny]
                            beside = beside + (
                                pltpu.roll(centre, k, 0) + pltpu.roll(centre, nz - k, 0)
                            )
                            if x + k < planes:
                                beside = beside + own[x + k, y]
                            if x - k >= 0:
                                beside = beside + own[x - k, y]
                            summed = summed + stencil_weights[k] * beside
                        applied = -0.5 * summed + pot[y] * centre
                        if shift:
                            applied = applied - shift * centre
                        out[j, y] = applied
                        return carry

                    lax.fori_loop(0, ny, row, 0)

    return kernel


def finish_kernel(stage, planes, ny):
    blocks, depth = plane_blocks(planes)

    def kernel(*refs):
        refs = list(refs)
        low, partial = refs[:2]
        high = low
        initial = refs[2] if stage == "filtered" else None
        outs = refs[3:] if stage == "filtered" else refs[2:]
        out = outs[0]
        step = pl.program_id(0)
        for block in range(blocks):
            @pl.when(step == block)
            def _(block=block):
                for j in range(depth):
                    x = block * depth + j

                    def row(y, carry, x=x, j=j):
                        summed = partial[j, y]
                        for k in range(1, RADIUS + 1):
                            outside = []
                            if x + k >= planes:
                                outside.append(high[x + k - planes, y].astype(jnp.float32))
                            if x - k < 0:
                                outside.append(low[x - k + RADIUS, y].astype(jnp.float32))
                            if outside:
                                term = outside[0] if len(outside) == 1 else outside[0] + outside[1]
                                summed = summed + (-0.5 * stencil_weights[k]) * term
                        if stage == "first":
                            result = summed * first_factor
                        elif stage == "filtered":
                            result = summed * second_factor + (
                                memory_factor * initial[j, y].astype(jnp.float32)
                            )
                        else:
                            result = summed
                        result = result.astype(out.dtype)
                        out[j, y] = result
                        if len(outs) == 3:
                            if x >= planes - RADIUS:
                                outs[1][x - planes + RADIUS, y] = result
                            if x < RADIUS:
                                outs[2][x, y] = result
                        return carry

                    lax.fori_loop(0, ny, row, 0)

    return kernel


def stencil_stage(stage, block, sends, potential_wide, initial=None, keep_sends=True):
    planes, ny, nz, nb = block.shape
    blocks, depth = plane_blocks(planes)
    if blocks < 2:
        return stencil_stage_whole(stage, block, sends, potential_wide, initial, keep_sends)
    whole = pl.BlockSpec(block.shape, lambda i: (0, 0, 0, 0))
    edge = pl.BlockSpec((RADIUS, ny, nz, nb), lambda i: (0, 0, 0, 0))
    part = pl.BlockSpec((depth, ny, nz, nb), lambda i: (i, 0, 0, 0))
    low, high = exchange(sends, "domain")
    partial = pl.pallas_call(
        interior_kernel(stage, planes, ny, nz),
        grid=(blocks,),
        in_specs=[whole, pl.BlockSpec(potential_wide.shape, lambda i: (0, 0, 0))],
        out_specs=part,
        out_shape=jax.ShapeDtypeStruct(block.shape, jnp.float32),
        scratch_shapes=[
            pltpu.VMEM(block.shape, jnp.float32),
            pltpu.VMEM((ny, nz, nb), jnp.float32),
        ],
        name=f"interior_{stage}",
    )(block, potential_wide)
    halos = jnp.concatenate([low, high], axis=0)
    halo_block = pl.BlockSpec((RADIUS, ny, nz, nb), lambda i: (jnp.minimum(i, 1), 0, 0, 0))
    operands = [halos, partial]
    in_specs = [halo_block, part]
    if initial is not None:
        operands.append(initial)
        in_specs.append(part)
    shapes = [jax.ShapeDtypeStruct(block.shape, jnp.bfloat16)]
    out_specs = [part]
    if keep_sends:
        edge_shape = jax.ShapeDtypeStruct((RADIUS, ny, nz, nb), jnp.bfloat16)
        shapes += [edge_shape, edge_shape]
        out_specs += [edge, edge]
    return pl.pallas_call(
        finish_kernel(stage, planes, ny),
        grid=(blocks,),
        in_specs=in_specs,
        out_specs=tuple(out_specs),
        out_shape=tuple(shapes),
        name=f"finish_{stage}",
    )(*operands)


def finish_kernel_whole(stage, planes, ny):
    blocks, depth = plane_blocks(planes)

    def kernel(*refs):
        refs = list(refs)
        low, high, partial = refs[:3]
        initial = refs[3] if stage == "filtered" else None
        outs = refs[4:] if stage == "filtered" else refs[3:]
        out = outs[0]
        step = pl.program_id(0)
        for block in range(blocks):
            @pl.when(step == block)
            def _(block=block):
                for j in range(depth):
                    x = block * depth + j

                    def row(y, carry, x=x, j=j):
                        summed = partial[j, y]
                        for k in range(1, RADIUS + 1):
                            outside = []
                            if x + k >= planes:
                                outside.append(high[x + k - planes, y].astype(jnp.float32))
                            if x - k < 0:
                                outside.append(low[x - k + RADIUS, y].astype(jnp.float32))
                            if outside:
                                term = outside[0] if len(outside) == 1 else outside[0] + outside[1]
                                summed = summed + (-0.5 * stencil_weights[k]) * term
                        if stage == "first":
                            result = summed * first_factor
                        elif stage == "filtered":
                            result = summed * second_factor + (
                                memory_factor * initial[j, y].astype(jnp.float32)
                            )
                        else:
                            result = summed
                        result = result.astype(out.dtype)
                        out[j, y] = result
                        if len(outs) == 3:
                            if x >= planes - RADIUS:
                                outs[1][x - planes + RADIUS, y] = result
                            if x < RADIUS:
                                outs[2][x, y] = result
                        return carry

                    lax.fori_loop(0, ny, row, 0)

    return kernel


def stencil_stage_whole(stage, block, sends, potential_wide, initial=None, keep_sends=True):
    planes, ny, nz, nb = block.shape
    blocks, depth = plane_blocks(planes)
    whole = pl.BlockSpec(block.shape, lambda i: (0, 0, 0, 0))
    edge = pl.BlockSpec((RADIUS, ny, nz, nb), lambda i: (0, 0, 0, 0))
    part = pl.BlockSpec((depth, ny, nz, nb), lambda i: (i, 0, 0, 0))
    low, high = exchange(sends, "domain")
    partial = pl.pallas_call(
        interior_kernel(stage, planes, ny, nz),
        grid=(blocks,),
        in_specs=[whole, pl.BlockSpec(potential_wide.shape, lambda i: (0, 0, 0))],
        out_specs=part,
        out_shape=jax.ShapeDtypeStruct(block.shape, jnp.float32),
        scratch_shapes=[
            pltpu.VMEM(block.shape, jnp.float32),
            pltpu.VMEM((ny, nz, nb), jnp.float32),
        ],
        name=f"interior_{stage}",
    )(block, potential_wide)
    operands = [low, high, partial]
    in_specs = [edge, edge, part]
    if initial is not None:
        operands.append(initial)
        in_specs.append(part)
    shapes = [jax.ShapeDtypeStruct(block.shape, jnp.bfloat16)]
    out_specs = [part]
    if keep_sends:
        edge_shape = jax.ShapeDtypeStruct((RADIUS, ny, nz, nb), jnp.bfloat16)
        shapes += [edge_shape, edge_shape]
        out_specs += [edge, edge]
    return pl.pallas_call(
        finish_kernel_whole(stage, planes, ny),
        grid=(blocks,),
        in_specs=in_specs,
        out_specs=tuple(out_specs),
        out_shape=tuple(shapes),
        name=f"finish_{stage}",
    )(*operands)


def exchange(sends, axis):
    count = lax.axis_size(axis)
    forward = [(i, (i + 1) % count) for i in range(count)]
    backward = [(target, source) for source, target in forward]
    return lax.ppermute(sends[0], axis, forward), lax.ppermute(sends[1], axis, backward)


def butterfly_sum(values, axis):
    count = lax.axis_size(axis)
    bit = 1
    while bit < count:
        pairs = [(i, i ^ bit) for i in range(count)]
        values = values + lax.ppermute(values, axis, pairs)
        bit *= 2
    return values


def shards(orbitals, potential):
    planes, ny, nz, nb = orbitals.shape
    potential_wide = jnp.swapaxes(potential, 1, 2)
    cell_count = planes * ny * nz
    cell_weight = 1.0 / (cell_count * lax.axis_size("domain"))
    band = lax.axis_index("band")
    gram = lambda rows, cols: with_layout_constraint(
        jnp.einsum("cb,ck->bk", rows, cols, preferred_element_type=jnp.float32),
        Layout((0, 1)),
    )
    placed = lambda mine, theirs: jnp.where(
        band == 0,
        jnp.concatenate([mine, theirs], axis=1),
        jnp.concatenate([theirs, mine], axis=1),
    )
    planes_sent = (
        lax.slice_in_dim(orbitals, planes - RADIUS, None, axis=0),
        lax.slice_in_dim(orbitals, 0, RADIUS, axis=0),
    )
    first, *first_sent = stencil_stage("first", orbitals, planes_sent, potential_wide)
    filtered, *filtered_sent = stencil_stage(
        "filtered", first, first_sent, potential_wide, orbitals
    )
    own_block = filtered.reshape(cell_count, nb)
    partner = lax.ppermute(own_block, "band", [(0, 1), (1, 0)])
    correlation_piece = placed(gram(own_block, own_block), gram(own_block, partner))
    correlation = butterfly_sum(correlation_piece, "domain") * cell_weight
    (applied_grid,) = stencil_stage(
        "applied", filtered, filtered_sent, potential_wide, keep_sends=False
    )
    applied = applied_grid.reshape(cell_count, nb)
    energy_piece = placed(gram(applied, own_block), gram(applied, partner))
    projected = butterfly_sum(energy_piece, "domain") * cell_weight
    return (filtered, correlation, projected)


def solution(mesh):
    placed = (P("domain", None, None, "band"), P("domain", None, None))
    return jax.shard_map(
        shards,
        mesh=mesh,
        in_specs=placed,
        out_specs=(P("domain", None, None, "band"), P("band", None), P("band", None)),
        check_vma=False,
    )
```

```python
import jax
import jax.numpy as jnp
from jax import lax
from jax.experimental import pallas as pl
from jax.experimental.pallas import tpu as pltpu
from jax.experimental.layout import Layout, with_layout_constraint
from jax.sharding import PartitionSpec as P

RADIUS = 4


stencil_weights = (-205.0 / 72.0, 8.0 / 5.0, -1.0 / 5.0, 8.0 / 315.0, -1.0 / 560.0)
spectrum_centre = 6.0
first_factor = -0.125
second_factor = -1.0 / 7.0
memory_factor = -1.0 / 7.0


def plane_blocks(planes):
    return (planes // RADIUS, RADIUS) if planes % RADIUS == 0 else (1, planes)


def interior_kernel(stage, planes, ny, nz):
    shift = 0.0 if stage == "applied" else spectrum_centre
    blocks, depth = plane_blocks(planes)

    def kernel(own_narrow, pot, out, own):
        step = pl.program_id(0)

        @pl.when(step == 0)
        def _():
            for x in range(planes):
                own[x] = own_narrow[x].astype(jnp.float32)

        for block in range(blocks):
            @pl.when(step == block)
            def _(block=block):
                for j in range(depth):
                    x = block * depth + j

                    def row(y, carry, x=x, j=j):
                        centre = own[x, y]
                        summed = (3.0 * stencil_weights[0]) * centre
                        for k in range(1, RADIUS + 1):
                            beside = own[x, (y + k) % ny] + own[x, (y + ny - k) % ny]
                            beside = beside + (
                                pltpu.roll(centre, k, 0) + pltpu.roll(centre, nz - k, 0)
                            )
                            if x + k < planes:
                                beside = beside + own[x + k, y]
                            if x - k >= 0:
                                beside = beside + own[x - k, y]
                            summed = summed + stencil_weights[k] * beside
                        applied = -0.5 * summed + pot[j, y] * centre
                        if shift:
                            applied = applied - shift * centre
                        out[j, y] = applied
                        return carry

                    lax.fori_loop(0, ny, row, 0)

    return kernel


def finish_kernel(stage, planes, ny):
    blocks, depth = plane_blocks(planes)

    def kernel(*refs):
        refs = list(refs)
        low, partial = refs[:2]
        high = low
        initial = refs[2] if stage == "filtered" else None
        outs = refs[3:] if stage == "filtered" else refs[2:]
        out = outs[0]
        step = pl.program_id(0)
        for block in range(blocks):
            @pl.when(step == block)
            def _(block=block):
                for j in range(depth):
                    x = block * depth + j

                    def row(y, carry, x=x, j=j):
                        summed = partial[j, y]
                        for k in range(1, RADIUS + 1):
                            outside = []
                            if x + k >= planes:
                                outside.append(high[x + k - planes, y].astype(jnp.float32))
                            if x - k < 0:
                                outside.append(low[x - k + RADIUS, y].astype(jnp.float32))
                            if outside:
                                term = outside[0] if len(outside) == 1 else outside[0] + outside[1]
                                summed = summed + (-0.5 * stencil_weights[k]) * term
                        if stage == "first":
                            result = summed * first_factor
                        elif stage == "filtered":
                            result = summed * second_factor + (
                                memory_factor * initial[j, y].astype(jnp.float32)
                            )
                        else:
                            result = summed
                        result = result.astype(out.dtype)
                        out[j, y] = result
                        if len(outs) == 3:
                            if x >= planes - RADIUS:
                                outs[1][x - planes + RADIUS, y] = result
                            if x < RADIUS:
                                outs[2][x, y] = result
                        return carry

                    lax.fori_loop(0, ny, row, 0)

    return kernel


def stencil_stage(stage, block, sends, potential_wide, initial=None, keep_sends=True):
    planes, ny, nz, nb = block.shape
    blocks, depth = plane_blocks(planes)
    if blocks < 2:
        return stencil_stage_whole(stage, block, sends, potential_wide, initial, keep_sends)
    whole = pl.BlockSpec(block.shape, lambda i: (0, 0, 0, 0))
    edge = pl.BlockSpec((RADIUS, ny, nz, nb), lambda i: (0, 0, 0, 0))
    part = pl.BlockSpec((depth, ny, nz, nb), lambda i: (i, 0, 0, 0))
    low, high = exchange(sends, "domain")
    partial = pl.pallas_call(
        interior_kernel(stage, planes, ny, nz),
        grid=(blocks,),
        in_specs=[whole, part],
        out_specs=part,
        out_shape=jax.ShapeDtypeStruct(block.shape, jnp.float32),
        scratch_shapes=[pltpu.VMEM(block.shape, jnp.float32)],
        name=f"interior_{stage}",
    )(block, potential_wide)
    halos = jnp.concatenate([low, high], axis=0)
    halo_block = pl.BlockSpec((RADIUS, ny, nz, nb), lambda i: (jnp.minimum(i, 1), 0, 0, 0))
    operands = [halos, partial]
    in_specs = [halo_block, part]
    if initial is not None:
        operands.append(initial)
        in_specs.append(part)
    shapes = [jax.ShapeDtypeStruct(block.shape, jnp.bfloat16)]
    out_specs = [part]
    if keep_sends:
        edge_shape = jax.ShapeDtypeStruct((RADIUS, ny, nz, nb), jnp.bfloat16)
        shapes += [edge_shape, edge_shape]
        out_specs += [edge, edge]
    return pl.pallas_call(
        finish_kernel(stage, planes, ny),
        grid=(blocks,),
        in_specs=in_specs,
        out_specs=tuple(out_specs),
        out_shape=tuple(shapes),
        name=f"finish_{stage}",
    )(*operands)


def finish_kernel_whole(stage, planes, ny):
    blocks, depth = plane_blocks(planes)

    def kernel(*refs):
        refs = list(refs)
        low, high, partial = refs[:3]
        initial = refs[3] if stage == "filtered" else None
        outs = refs[4:] if stage == "filtered" else refs[3:]
        out = outs[0]
        step = pl.program_id(0)
        for block in range(blocks):
            @pl.when(step == block)
            def _(block=block):
                for j in range(depth):
                    x = block * depth + j

                    def row(y, carry, x=x, j=j):
                        summed = partial[j, y]
                        for k in range(1, RADIUS + 1):
                            outside = []
                            if x + k >= planes:
                                outside.append(high[x + k - planes, y].astype(jnp.float32))
                            if x - k < 0:
                                outside.append(low[x - k + RADIUS, y].astype(jnp.float32))
                            if outside:
                                term = outside[0] if len(outside) == 1 else outside[0] + outside[1]
                                summed = summed + (-0.5 * stencil_weights[k]) * term
                        if stage == "first":
                            result = summed * first_factor
                        elif stage == "filtered":
                            result = summed * second_factor + (
                                memory_factor * initial[j, y].astype(jnp.float32)
                            )
                        else:
                            result = summed
                        result = result.astype(out.dtype)
                        out[j, y] = result
                        if len(outs) == 3:
                            if x >= planes - RADIUS:
                                outs[1][x - planes + RADIUS, y] = result
                            if x < RADIUS:
                                outs[2][x, y] = result
                        return carry

                    lax.fori_loop(0, ny, row, 0)

    return kernel


def stencil_stage_whole(stage, block, sends, potential_wide, initial=None, keep_sends=True):
    planes, ny, nz, nb = block.shape
    blocks, depth = plane_blocks(planes)
    whole = pl.BlockSpec(block.shape, lambda i: (0, 0, 0, 0))
    edge = pl.BlockSpec((RADIUS, ny, nz, nb), lambda i: (0, 0, 0, 0))
    part = pl.BlockSpec((depth, ny, nz, nb), lambda i: (i, 0, 0, 0))
    low, high = exchange(sends, "domain")
    partial = pl.pallas_call(
        interior_kernel(stage, planes, ny, nz),
        grid=(blocks,),
        in_specs=[whole, part],
        out_specs=part,
        out_shape=jax.ShapeDtypeStruct(block.shape, jnp.float32),
        scratch_shapes=[pltpu.VMEM(block.shape, jnp.float32)],
        name=f"interior_{stage}",
    )(block, potential_wide)
    operands = [low, high, partial]
    in_specs = [edge, edge, part]
    if initial is not None:
        operands.append(initial)
        in_specs.append(part)
    shapes = [jax.ShapeDtypeStruct(block.shape, jnp.bfloat16)]
    out_specs = [part]
    if keep_sends:
        edge_shape = jax.ShapeDtypeStruct((RADIUS, ny, nz, nb), jnp.bfloat16)
        shapes += [edge_shape, edge_shape]
        out_specs += [edge, edge]
    return pl.pallas_call(
        finish_kernel_whole(stage, planes, ny),
        grid=(blocks,),
        in_specs=in_specs,
        out_specs=tuple(out_specs),
        out_shape=tuple(shapes),
        name=f"finish_{stage}",
    )(*operands)


def exchange(sends, axis):
    count = lax.axis_size(axis)
    forward = [(i, (i + 1) % count) for i in range(count)]
    backward = [(target, source) for source, target in forward]
    return lax.ppermute(sends[0], axis, forward), lax.ppermute(sends[1], axis, backward)


def edge_copies(block):
    planes = block.shape[0]
    edge = jax.ShapeDtypeStruct((RADIUS,) + block.shape[1:], block.dtype)

    def kernel(source, upper, lower, done):
        copies = [
            pltpu.make_async_copy(source.at[pl.ds(planes - RADIUS, RADIUS)], upper, done.at[0]),
            pltpu.make_async_copy(source.at[pl.ds(0, RADIUS)], lower, done.at[1]),
        ]
        for copy in copies:
            copy.start()
        for copy in copies:
            copy.wait()

    anywhere = pl.BlockSpec(memory_space=pl.ANY)
    return pl.pallas_call(
        kernel,
        in_specs=[anywhere],
        out_specs=(anywhere, anywhere),
        out_shape=(edge, edge),
        scratch_shapes=[pltpu.SemaphoreType.DMA((2,))],
        name="edge_copies",
    )(block)


def butterfly_sum(values, axis):
    count = lax.axis_size(axis)
    bit = 1
    while bit < count:
        pairs = [(i, i ^ bit) for i in range(count)]
        values = values + lax.ppermute(values, axis, pairs)
        bit *= 2
    return values


def shards(orbitals, potential):
    planes, ny, nz, nb = orbitals.shape
    potential_wide = jnp.broadcast_to(potential[:, :, :, None], (planes, ny, nz, nb))
    cell_count = planes * ny * nz
    cell_weight = 1.0 / (cell_count * lax.axis_size("domain"))
    band = lax.axis_index("band")
    gram = lambda rows, cols: with_layout_constraint(
        jnp.einsum("cb,ck->bk", rows, cols, preferred_element_type=jnp.float32),
        Layout((0, 1)),
    )
    placed = lambda mine, theirs: jnp.where(
        band == 0,
        jnp.concatenate([mine, theirs], axis=1),
        jnp.concatenate([theirs, mine], axis=1),
    )
    planes_sent = edge_copies(orbitals)
    first, *first_sent = stencil_stage("first", orbitals, planes_sent, potential_wide)
    filtered, *filtered_sent = stencil_stage(
        "filtered", first, first_sent, potential_wide, orbitals
    )
    own_block = filtered.reshape(cell_count, nb)
    partner = lax.ppermute(own_block, "band", [(0, 1), (1, 0)])
    correlation_piece = placed(gram(own_block, own_block), gram(own_block, partner))
    correlation = butterfly_sum(correlation_piece, "domain") * cell_weight
    (applied_grid,) = stencil_stage(
        "applied", filtered, filtered_sent, potential_wide, keep_sends=False
    )
    applied = applied_grid.reshape(cell_count, nb)
    energy_piece = placed(gram(applied, own_block), gram(applied, partner))
    projected = butterfly_sum(energy_piece, "domain") * cell_weight
    return (filtered, correlation, projected)


def solution(mesh):
    placed = (P("domain", None, None, "band"), P("domain", None, None))
    return jax.shard_map(
        shards,
        mesh=mesh,
        in_specs=placed,
        out_specs=(P("domain", None, None, "band"), P("band", None), P("band", None)),
        check_vma=False,
    )
```

```python
import jax
import jax.numpy as jnp
from jax import lax
from jax.experimental import pallas as pl
from jax.experimental.pallas import tpu as pltpu
from jax.experimental.layout import Layout, with_layout_constraint
from jax.sharding import PartitionSpec as P

RADIUS = 4


stencil_weights = (-205.0 / 72.0, 8.0 / 5.0, -1.0 / 5.0, 8.0 / 315.0, -1.0 / 560.0)
spectrum_centre = 6.0
first_factor = -0.125
second_factor = -1.0 / 7.0
memory_factor = -1.0 / 7.0


def plane_blocks(planes):
    return (planes // RADIUS, RADIUS) if planes % RADIUS == 0 else (1, planes)


def interior_kernel(stage, planes, ny, nz):
    shift = 0.0 if stage == "applied" else spectrum_centre
    blocks, depth = plane_blocks(planes)

    def kernel(own_narrow, pot, out, own):
        step = pl.program_id(0)

        @pl.when(step == 0)
        def _():
            for x in range(planes):
                own[x] = own_narrow[x].astype(jnp.float32)

        for block in range(blocks):
            @pl.when(step == block)
            def _(block=block):
                for j in range(depth):
                    x = block * depth + j

                    def row(y, carry, x=x, j=j):
                        centre = own[x, y]
                        summed = (3.0 * stencil_weights[0]) * centre
                        for k in range(1, RADIUS + 1):
                            beside = own[x, (y + k) % ny] + own[x, (y + ny - k) % ny]
                            beside = beside + (
                                pltpu.roll(centre, k, 0) + pltpu.roll(centre, nz - k, 0)
                            )
                            if x + k < planes:
                                beside = beside + own[x + k, y]
                            if x - k >= 0:
                                beside = beside + own[x - k, y]
                            summed = summed + stencil_weights[k] * beside
                        applied = -0.5 * summed + pot[j, y] * centre
                        if shift:
                            applied = applied - shift * centre
                        out[j, y] = applied
                        return carry

                    lax.fori_loop(0, ny, row, 0)

    return kernel


def finish_kernel(stage, planes, ny):
    blocks, depth = plane_blocks(planes)

    def kernel(*refs):
        refs = list(refs)
        low, partial = refs[:2]
        high = low
        initial = refs[2] if stage == "filtered" else None
        outs = refs[3:] if stage == "filtered" else refs[2:]
        out = outs[0]
        step = pl.program_id(0)
        for block in range(blocks):
            @pl.when(step == block)
            def _(block=block):
                for j in range(depth):
                    x = block * depth + j

                    def row(y, carry, x=x, j=j):
                        summed = partial[j, y]
                        for k in range(1, RADIUS + 1):
                            outside = []
                            if x + k >= planes:
                                outside.append(high[x + k - planes, y].astype(jnp.float32))
                            if x - k < 0:
                                outside.append(low[x - k + RADIUS, y].astype(jnp.float32))
                            if outside:
                                term = outside[0] if len(outside) == 1 else outside[0] + outside[1]
                                summed = summed + (-0.5 * stencil_weights[k]) * term
                        if stage == "first":
                            result = summed * first_factor
                        elif stage == "filtered":
                            result = summed * second_factor + (
                                memory_factor * initial[j, y].astype(jnp.float32)
                            )
                        else:
                            result = summed
                        result = result.astype(out.dtype)
                        out[j, y] = result
                        if len(outs) == 3:
                            if x >= planes - RADIUS:
                                outs[1][x - planes + RADIUS, y] = result
                            if x < RADIUS:
                                outs[2][x, y] = result
                        return carry

                    lax.fori_loop(0, ny, row, 0)

    return kernel


def stencil_stage(stage, block, sends, potential_wide, initial=None, keep_sends=True):
    planes, ny, nz, nb = block.shape
    blocks, depth = plane_blocks(planes)
    if blocks < 2:
        return stencil_stage_whole(stage, block, sends, potential_wide, initial, keep_sends)
    whole = pl.BlockSpec(block.shape, lambda i: (0, 0, 0, 0))
    edge = pl.BlockSpec((RADIUS, ny, nz, nb), lambda i: (0, 0, 0, 0))
    part = pl.BlockSpec((depth, ny, nz, nb), lambda i: (i, 0, 0, 0))
    low, high = exchange(sends, "domain")
    partial = pl.pallas_call(
        interior_kernel(stage, planes, ny, nz),
        grid=(blocks,),
        in_specs=[whole, part],
        out_specs=part,
        out_shape=jax.ShapeDtypeStruct(block.shape, jnp.float32),
        scratch_shapes=[pltpu.VMEM(block.shape, jnp.float32)],
        name=f"interior_{stage}",
    )(block, potential_wide)
    halos = jnp.concatenate([low, high], axis=0)
    halo_block = pl.BlockSpec((RADIUS, ny, nz, nb), lambda i: (jnp.minimum(i, 1), 0, 0, 0))
    operands = [halos, partial]
    in_specs = [halo_block, part]
    if initial is not None:
        operands.append(initial)
        in_specs.append(part)
    shapes = [jax.ShapeDtypeStruct(block.shape, jnp.bfloat16)]
    out_specs = [part]
    if keep_sends:
        edge_shape = jax.ShapeDtypeStruct((RADIUS, ny, nz, nb), jnp.bfloat16)
        shapes += [edge_shape, edge_shape]
        out_specs += [edge, edge]
    return pl.pallas_call(
        finish_kernel(stage, planes, ny),
        grid=(blocks,),
        in_specs=in_specs,
        out_specs=tuple(out_specs),
        out_shape=tuple(shapes),
        name=f"finish_{stage}",
    )(*operands)


def finish_kernel_whole(stage, planes, ny):
    blocks, depth = plane_blocks(planes)

    def kernel(*refs):
        refs = list(refs)
        low, high, partial = refs[:3]
        initial = refs[3] if stage == "filtered" else None
        outs = refs[4:] if stage == "filtered" else refs[3:]
        out = outs[0]
        step = pl.program_id(0)
        for block in range(blocks):
            @pl.when(step == block)
            def _(block=block):
                for j in range(depth):
                    x = block * depth + j

                    def row(y, carry, x=x, j=j):
                        summed = partial[j, y]
                        for k in range(1, RADIUS + 1):
                            outside = []
                            if x + k >= planes:
                                outside.append(high[x + k - planes, y].astype(jnp.float32))
                            if x - k < 0:
                                outside.append(low[x - k + RADIUS, y].astype(jnp.float32))
                            if outside:
                                term = outside[0] if len(outside) == 1 else outside[0] + outside[1]
                                summed = summed + (-0.5 * stencil_weights[k]) * term
                        if stage == "first":
                            result = summed * first_factor
                        elif stage == "filtered":
                            result = summed * second_factor + (
                                memory_factor * initial[j, y].astype(jnp.float32)
                            )
                        else:
                            result = summed
                        result = result.astype(out.dtype)
                        out[j, y] = result
                        if len(outs) == 3:
                            if x >= planes - RADIUS:
                                outs[1][x - planes + RADIUS, y] = result
                            if x < RADIUS:
                                outs[2][x, y] = result
                        return carry

                    lax.fori_loop(0, ny, row, 0)

    return kernel


def stencil_stage_whole(stage, block, sends, potential_wide, initial=None, keep_sends=True):
    planes, ny, nz, nb = block.shape
    blocks, depth = plane_blocks(planes)
    whole = pl.BlockSpec(block.shape, lambda i: (0, 0, 0, 0))
    edge = pl.BlockSpec((RADIUS, ny, nz, nb), lambda i: (0, 0, 0, 0))
    part = pl.BlockSpec((depth, ny, nz, nb), lambda i: (i, 0, 0, 0))
    low, high = exchange(sends, "domain")
    partial = pl.pallas_call(
        interior_kernel(stage, planes, ny, nz),
        grid=(blocks,),
        in_specs=[whole, part],
        out_specs=part,
        out_shape=jax.ShapeDtypeStruct(block.shape, jnp.float32),
        scratch_shapes=[pltpu.VMEM(block.shape, jnp.float32)],
        name=f"interior_{stage}",
    )(block, potential_wide)
    operands = [low, high, partial]
    in_specs = [edge, edge, part]
    if initial is not None:
        operands.append(initial)
        in_specs.append(part)
    shapes = [jax.ShapeDtypeStruct(block.shape, jnp.bfloat16)]
    out_specs = [part]
    if keep_sends:
        edge_shape = jax.ShapeDtypeStruct((RADIUS, ny, nz, nb), jnp.bfloat16)
        shapes += [edge_shape, edge_shape]
        out_specs += [edge, edge]
    return pl.pallas_call(
        finish_kernel_whole(stage, planes, ny),
        grid=(blocks,),
        in_specs=in_specs,
        out_specs=tuple(out_specs),
        out_shape=tuple(shapes),
        name=f"finish_{stage}",
    )(*operands)


def exchange(sends, axis):
    count = lax.axis_size(axis)
    forward = [(i, (i + 1) % count) for i in range(count)]
    backward = [(target, source) for source, target in forward]
    return lax.ppermute(sends[0], axis, forward), lax.ppermute(sends[1], axis, backward)


def butterfly_sum(values, axis):
    count = lax.axis_size(axis)
    bit = 1
    while bit < count:
        pairs = [(i, i ^ bit) for i in range(count)]
        values = values + lax.ppermute(values, axis, pairs)
        bit *= 2
    return values


def shards(orbitals, potential):
    planes, ny, nz, nb = orbitals.shape
    potential_wide = jnp.broadcast_to(potential[:, :, :, None], (planes, ny, nz, nb))
    cell_count = planes * ny * nz
    cell_weight = 1.0 / (cell_count * lax.axis_size("domain"))
    band = lax.axis_index("band")
    gram = lambda rows, cols: with_layout_constraint(
        jnp.einsum("cb,ck->bk", rows, cols, preferred_element_type=jnp.float32),
        Layout((0, 1)),
    )
    placed = lambda mine, theirs: jnp.where(
        band == 0,
        jnp.concatenate([mine, theirs], axis=1),
        jnp.concatenate([theirs, mine], axis=1),
    )
    planes_sent = (
        lax.slice_in_dim(orbitals, planes - RADIUS, None, axis=0),
        lax.slice_in_dim(orbitals, 0, RADIUS, axis=0),
    )
    first, *first_sent = stencil_stage("first", orbitals, planes_sent, potential_wide)
    filtered, *filtered_sent = stencil_stage(
        "filtered", first, first_sent, potential_wide, orbitals
    )
    own_block = filtered.reshape(cell_count, nb)
    partner = lax.ppermute(own_block, "band", [(0, 1), (1, 0)])
    correlation_piece = placed(gram(own_block, own_block), gram(own_block, partner))
    (applied_grid,) = stencil_stage(
        "applied", filtered, filtered_sent, potential_wide, keep_sends=False
    )
    applied = applied_grid.reshape(cell_count, nb)
    energy_piece = placed(gram(applied, own_block), gram(applied, partner))
    summed = butterfly_sum(jnp.stack((correlation_piece, energy_piece)), "domain") * cell_weight
    correlation = summed[0]
    projected = summed[1]
    return (filtered, correlation, projected)


def solution(mesh):
    placed = (P("domain", None, None, "band"), P("domain", None, None))
    return jax.shard_map(
        shards,
        mesh=mesh,
        in_specs=placed,
        out_specs=(P("domain", None, None, "band"), P("band", None), P("band", None)),
        check_vma=False,
    )
```

```python
import jax
import jax.numpy as jnp
from jax import lax
from jax.experimental import pallas as pl
from jax.experimental.pallas import tpu as pltpu
from jax.experimental.layout import Layout, with_layout_constraint
from jax.sharding import PartitionSpec as P

RADIUS = 4


stencil_weights = (-205.0 / 72.0, 8.0 / 5.0, -1.0 / 5.0, 8.0 / 315.0, -1.0 / 560.0)
spectrum_centre = 6.0
first_factor = -0.125
second_factor = -1.0 / 7.0
memory_factor = -1.0 / 7.0


def plane_blocks(planes):
    return (planes // RADIUS, RADIUS) if planes % RADIUS == 0 else (1, planes)


def interior_kernel(stage, planes, ny, nz):
    shift = 0.0 if stage == "applied" else spectrum_centre
    blocks, depth = plane_blocks(planes)

    def kernel(own_narrow, pot, out, own):
        step = pl.program_id(0)

        @pl.when(step == 0)
        def _():
            for x in range(planes):
                own[x] = own_narrow[x].astype(jnp.float32)

        for block in range(blocks):
            @pl.when(step == block)
            def _(block=block):
                for j in range(depth):
                    x = block * depth + j

                    def row(y, carry, x=x, j=j):
                        centre = own[x, y]
                        summed = (3.0 * stencil_weights[0]) * centre
                        for k in range(1, RADIUS + 1):
                            beside = own[x, (y + k) % ny] + own[x, (y + ny - k) % ny]
                            beside = beside + (
                                pltpu.roll(centre, k, 0) + pltpu.roll(centre, nz - k, 0)
                            )
                            if x + k < planes:
                                beside = beside + own[x + k, y]
                            if x - k >= 0:
                                beside = beside + own[x - k, y]
                            summed = summed + stencil_weights[k] * beside
                        applied = -0.5 * summed + pot[j, y] * centre
                        if shift:
                            applied = applied - shift * centre
                        out[j, y] = applied
                        return carry

                    lax.fori_loop(0, ny, row, 0)

    return kernel


def finish_kernel(stage, planes, ny):
    blocks, depth = plane_blocks(planes)

    def kernel(*refs):
        refs = list(refs)
        low, partial = refs[:2]
        high = low
        initial = refs[2] if stage == "filtered" else None
        outs = refs[3:] if stage == "filtered" else refs[2:]
        out = outs[0]
        step = pl.program_id(0)
        for block in range(blocks):
            @pl.when(step == block)
            def _(block=block):
                for j in range(depth):
                    x = block * depth + j

                    def row(y, carry, x=x, j=j):
                        summed = partial[j, y]
                        for k in range(1, RADIUS + 1):
                            outside = []
                            if x + k >= planes:
                                outside.append(high[x + k - planes, y].astype(jnp.float32))
                            if x - k < 0:
                                outside.append(low[x - k + RADIUS, y].astype(jnp.float32))
                            if outside:
                                term = outside[0] if len(outside) == 1 else outside[0] + outside[1]
                                summed = summed + (-0.5 * stencil_weights[k]) * term
                        if stage == "first":
                            result = summed * first_factor
                        elif stage == "filtered":
                            result = summed * second_factor + (
                                memory_factor * initial[j, y].astype(jnp.float32)
                            )
                        else:
                            result = summed
                        result = result.astype(out.dtype)
                        out[j, y] = result
                        if len(outs) == 3:
                            if x >= planes - RADIUS:
                                outs[1][x - planes + RADIUS, y] = result
                            if x < RADIUS:
                                outs[2][x, y] = result
                        return carry

                    lax.fori_loop(0, ny, row, 0)

    return kernel


def stencil_stage(stage, block, sends, potential_wide, initial=None, keep_sends=True):
    planes, ny, nz, nb = block.shape
    blocks, depth = plane_blocks(planes)
    if blocks < 2:
        return stencil_stage_whole(stage, block, sends, potential_wide, initial, keep_sends)
    whole = pl.BlockSpec(block.shape, lambda i: (0, 0, 0, 0))
    edge = pl.BlockSpec((RADIUS, ny, nz, nb), lambda i: (0, 0, 0, 0))
    part = pl.BlockSpec((depth, ny, nz, nb), lambda i: (i, 0, 0, 0))
    low, high = exchange(sends, "domain")
    partial = pl.pallas_call(
        interior_kernel(stage, planes, ny, nz),
        grid=(blocks,),
        in_specs=[whole, part],
        out_specs=part,
        out_shape=jax.ShapeDtypeStruct(block.shape, jnp.float32),
        scratch_shapes=[pltpu.VMEM(block.shape, jnp.float32)],
        name=f"interior_{stage}",
    )(block, potential_wide)
    halos = jnp.concatenate([low, high], axis=0)
    halo_block = pl.BlockSpec((RADIUS, ny, nz, nb), lambda i: (jnp.minimum(i, 1), 0, 0, 0))
    operands = [halos, partial]
    in_specs = [halo_block, part]
    if initial is not None:
        operands.append(initial)
        in_specs.append(part)
    shapes = [jax.ShapeDtypeStruct(block.shape, jnp.bfloat16)]
    out_specs = [part]
    if keep_sends:
        edge_shape = jax.ShapeDtypeStruct((RADIUS, ny, nz, nb), jnp.bfloat16)
        shapes += [edge_shape, edge_shape]
        out_specs += [edge, edge]
    return pl.pallas_call(
        finish_kernel(stage, planes, ny),
        grid=(blocks,),
        in_specs=in_specs,
        out_specs=tuple(out_specs),
        out_shape=tuple(shapes),
        name=f"finish_{stage}",
    )(*operands)


def finish_kernel_whole(stage, planes, ny):
    blocks, depth = plane_blocks(planes)

    def kernel(*refs):
        refs = list(refs)
        low, high, partial = refs[:3]
        initial = refs[3] if stage == "filtered" else None
        outs = refs[4:] if stage == "filtered" else refs[3:]
        out = outs[0]
        step = pl.program_id(0)
        for block in range(blocks):
            @pl.when(step == block)
            def _(block=block):
                for j in range(depth):
                    x = block * depth + j

                    def row(y, carry, x=x, j=j):
                        summed = partial[j, y]
                        for k in range(1, RADIUS + 1):
                            outside = []
                            if x + k >= planes:
                                outside.append(high[x + k - planes, y].astype(jnp.float32))
                            if x - k < 0:
                                outside.append(low[x - k + RADIUS, y].astype(jnp.float32))
                            if outside:
                                term = outside[0] if len(outside) == 1 else outside[0] + outside[1]
                                summed = summed + (-0.5 * stencil_weights[k]) * term
                        if stage == "first":
                            result = summed * first_factor
                        elif stage == "filtered":
                            result = summed * second_factor + (
                                memory_factor * initial[j, y].astype(jnp.float32)
                            )
                        else:
                            result = summed
                        result = result.astype(out.dtype)
                        out[j, y] = result
                        if len(outs) == 3:
                            if x >= planes - RADIUS:
                                outs[1][x - planes + RADIUS, y] = result
                            if x < RADIUS:
                                outs[2][x, y] = result
                        return carry

                    lax.fori_loop(0, ny, row, 0)

    return kernel


def stencil_stage_whole(stage, block, sends, potential_wide, initial=None, keep_sends=True):
    planes, ny, nz, nb = block.shape
    blocks, depth = plane_blocks(planes)
    whole = pl.BlockSpec(block.shape, lambda i: (0, 0, 0, 0))
    edge = pl.BlockSpec((RADIUS, ny, nz, nb), lambda i: (0, 0, 0, 0))
    part = pl.BlockSpec((depth, ny, nz, nb), lambda i: (i, 0, 0, 0))
    low, high = exchange(sends, "domain")
    partial = pl.pallas_call(
        interior_kernel(stage, planes, ny, nz),
        grid=(blocks,),
        in_specs=[whole, part],
        out_specs=part,
        out_shape=jax.ShapeDtypeStruct(block.shape, jnp.float32),
        scratch_shapes=[pltpu.VMEM(block.shape, jnp.float32)],
        name=f"interior_{stage}",
    )(block, potential_wide)
    operands = [low, high, partial]
    in_specs = [edge, edge, part]
    if initial is not None:
        operands.append(initial)
        in_specs.append(part)
    shapes = [jax.ShapeDtypeStruct(block.shape, jnp.bfloat16)]
    out_specs = [part]
    if keep_sends:
        edge_shape = jax.ShapeDtypeStruct((RADIUS, ny, nz, nb), jnp.bfloat16)
        shapes += [edge_shape, edge_shape]
        out_specs += [edge, edge]
    return pl.pallas_call(
        finish_kernel_whole(stage, planes, ny),
        grid=(blocks,),
        in_specs=in_specs,
        out_specs=tuple(out_specs),
        out_shape=tuple(shapes),
        name=f"finish_{stage}",
    )(*operands)


def exchange(sends, axis):
    count = lax.axis_size(axis)
    forward = [(i, (i + 1) % count) for i in range(count)]
    backward = [(target, source) for source, target in forward]
    return lax.ppermute(sends[0], axis, forward), lax.ppermute(sends[1], axis, backward)


def butterfly_sum(values, axis):
    count = lax.axis_size(axis)
    bit = 1
    while bit < count:
        pairs = [(i, i ^ bit) for i in range(count)]
        values = values + lax.ppermute(values, axis, pairs)
        bit *= 2
    return values


def split_sum(values, axis):
    half = values.shape[0] // 2
    return jnp.concatenate(
        [butterfly_sum(values[:half], axis), butterfly_sum(values[half:], axis)], axis=0
    )


def shards(orbitals, potential):
    planes, ny, nz, nb = orbitals.shape
    potential_wide = jnp.broadcast_to(potential[:, :, :, None], (planes, ny, nz, nb))
    cell_count = planes * ny * nz
    cell_weight = 1.0 / (cell_count * lax.axis_size("domain"))
    band = lax.axis_index("band")
    gram = lambda rows, cols: with_layout_constraint(
        jnp.einsum("cb,ck->bk", rows, cols, preferred_element_type=jnp.float32),
        Layout((0, 1)),
    )
    placed = lambda mine, theirs: jnp.where(
        band == 0,
        jnp.concatenate([mine, theirs], axis=1),
        jnp.concatenate([theirs, mine], axis=1),
    )
    planes_sent = (
        lax.slice_in_dim(orbitals, planes - RADIUS, None, axis=0),
        lax.slice_in_dim(orbitals, 0, RADIUS, axis=0),
    )
    first, *first_sent = stencil_stage("first", orbitals, planes_sent, potential_wide)
    filtered, *filtered_sent = stencil_stage(
        "filtered", first, first_sent, potential_wide, orbitals
    )
    own_block = filtered.reshape(cell_count, nb)
    partner = lax.ppermute(own_block, "band", [(0, 1), (1, 0)])
    correlation_piece = placed(gram(own_block, own_block), gram(own_block, partner))
    correlation = split_sum(correlation_piece, "domain") * cell_weight
    (applied_grid,) = stencil_stage(
        "applied", filtered, filtered_sent, potential_wide, keep_sends=False
    )
    applied = applied_grid.reshape(cell_count, nb)
    energy_piece = placed(gram(applied, own_block), gram(applied, partner))
    projected = split_sum(energy_piece, "domain") * cell_weight
    return (filtered, correlation, projected)


def solution(mesh):
    placed = (P("domain", None, None, "band"), P("domain", None, None))
    return jax.shard_map(
        shards,
        mesh=mesh,
        in_specs=placed,
        out_specs=(P("domain", None, None, "band"), P("band", None), P("band", None)),
        check_vma=False,
    )
```

```python
import jax
import jax.numpy as jnp
from jax import lax
from jax.experimental import pallas as pl
from jax.experimental.pallas import tpu as pltpu
from jax.experimental.layout import Layout, with_layout_constraint
from jax.sharding import PartitionSpec as P

RADIUS = 4


stencil_weights = (-205.0 / 72.0, 8.0 / 5.0, -1.0 / 5.0, 8.0 / 315.0, -1.0 / 560.0)
spectrum_centre = 6.0
first_factor = -0.125
second_factor = -1.0 / 7.0
memory_factor = -1.0 / 7.0


def plane_blocks(planes):
    return (planes // RADIUS, RADIUS) if planes % RADIUS == 0 else (1, planes)


def interior_kernel(stage, planes, ny, nz):
    shift = 0.0 if stage == "applied" else spectrum_centre
    blocks, depth = plane_blocks(planes)

    def kernel(own_narrow, pot, out, own):
        step = pl.program_id(0)

        @pl.when(step == 0)
        def _():
            for x in range(planes):
                own[x] = own_narrow[x].astype(jnp.float32)

        for block in range(blocks):
            @pl.when(step == block)
            def _(block=block):
                for j in range(depth):
                    x = block * depth + j

                    def row(y, carry, x=x, j=j):
                        centre = own[x, y]
                        summed = (3.0 * stencil_weights[0]) * centre
                        for k in range(1, RADIUS + 1):
                            beside = own[x, (y + k) % ny] + own[x, (y + ny - k) % ny]
                            beside = beside + (
                                pltpu.roll(centre, k, 0) + pltpu.roll(centre, nz - k, 0)
                            )
                            if x + k < planes:
                                beside = beside + own[x + k, y]
                            if x - k >= 0:
                                beside = beside + own[x - k, y]
                            summed = summed + stencil_weights[k] * beside
                        applied = -0.5 * summed + pot[j, y] * centre
                        if shift:
                            applied = applied - shift * centre
                        out[j, y] = applied
                        return carry

                    lax.fori_loop(0, ny, row, 0)

    return kernel


def finish_kernel(stage, planes, ny):
    blocks, depth = plane_blocks(planes)

    def kernel(*refs):
        refs = list(refs)
        low, partial = refs[:2]
        high = low
        initial = refs[2] if stage == "filtered" else None
        outs = refs[3:] if stage == "filtered" else refs[2:]
        out = outs[0]
        step = pl.program_id(0)
        for block in range(blocks):
            @pl.when(step == block)
            def _(block=block):
                for j in range(depth):
                    x = block * depth + j

                    def row(y, carry, x=x, j=j):
                        summed = partial[j, y]
                        for k in range(1, RADIUS + 1):
                            outside = []
                            if x + k >= planes:
                                outside.append(high[x + k - planes, y].astype(jnp.float32))
                            if x - k < 0:
                                outside.append(low[x - k + RADIUS, y].astype(jnp.float32))
                            if outside:
                                term = outside[0] if len(outside) == 1 else outside[0] + outside[1]
                                summed = summed + (-0.5 * stencil_weights[k]) * term
                        if stage == "first":
                            result = summed * first_factor
                        elif stage == "filtered":
                            result = summed * second_factor + (
                                memory_factor * initial[j, y].astype(jnp.float32)
                            )
                        else:
                            result = summed
                        result = result.astype(out.dtype)
                        out[j, y] = result
                        if len(outs) == 3:
                            if x >= planes - RADIUS:
                                outs[1][x - planes + RADIUS, y] = result
                            if x < RADIUS:
                                outs[2][x, y] = result
                        return carry

                    lax.fori_loop(0, ny, row, 0)

    return kernel


def stencil_stage(stage, block, sends, potential_wide, initial=None, keep_sends=True):
    planes, ny, nz, nb = block.shape
    blocks, depth = plane_blocks(planes)
    if blocks < 2:
        return stencil_stage_whole(stage, block, sends, potential_wide, initial, keep_sends)
    whole = pl.BlockSpec(block.shape, lambda i: (0, 0, 0, 0))
    edge = pl.BlockSpec((RADIUS, ny, nz, nb), lambda i: (0, 0, 0, 0))
    part = pl.BlockSpec((depth, ny, nz, nb), lambda i: (i, 0, 0, 0))
    low, high = exchange(sends, "domain")
    partial = pl.pallas_call(
        interior_kernel(stage, planes, ny, nz),
        grid=(blocks,),
        in_specs=[whole, part],
        out_specs=part,
        out_shape=jax.ShapeDtypeStruct(block.shape, jnp.float32),
        scratch_shapes=[pltpu.VMEM(block.shape, jnp.float32)],
        name=f"interior_{stage}",
    )(block, potential_wide)
    halos = jnp.concatenate([low, high], axis=0)
    halo_block = pl.BlockSpec((RADIUS, ny, nz, nb), lambda i: (jnp.minimum(i, 1), 0, 0, 0))
    operands = [halos, partial]
    in_specs = [halo_block, part]
    if initial is not None:
        operands.append(initial)
        in_specs.append(part)
    shapes = [jax.ShapeDtypeStruct(block.shape, jnp.bfloat16)]
    out_specs = [part]
    if keep_sends:
        edge_shape = jax.ShapeDtypeStruct((RADIUS, ny, nz, nb), jnp.bfloat16)
        shapes += [edge_shape, edge_shape]
        out_specs += [edge, edge]
    return pl.pallas_call(
        finish_kernel(stage, planes, ny),
        grid=(blocks,),
        in_specs=in_specs,
        out_specs=tuple(out_specs),
        out_shape=tuple(shapes),
        name=f"finish_{stage}",
    )(*operands)


def finish_kernel_whole(stage, planes, ny):
    blocks, depth = plane_blocks(planes)

    def kernel(*refs):
        refs = list(refs)
        low, high, partial = refs[:3]
        initial = refs[3] if stage == "filtered" else None
        outs = refs[4:] if stage == "filtered" else refs[3:]
        out = outs[0]
        step = pl.program_id(0)
        for block in range(blocks):
            @pl.when(step == block)
            def _(block=block):
                for j in range(depth):
                    x = block * depth + j

                    def row(y, carry, x=x, j=j):
                        summed = partial[j, y]
                        for k in range(1, RADIUS + 1):
                            outside = []
                            if x + k >= planes:
                                outside.append(high[x + k - planes, y].astype(jnp.float32))
                            if x - k < 0:
                                outside.append(low[x - k + RADIUS, y].astype(jnp.float32))
                            if outside:
                                term = outside[0] if len(outside) == 1 else outside[0] + outside[1]
                                summed = summed + (-0.5 * stencil_weights[k]) * term
                        if stage == "first":
                            result = summed * first_factor
                        elif stage == "filtered":
                            result = summed * second_factor + (
                                memory_factor * initial[j, y].astype(jnp.float32)
                            )
                        else:
                            result = summed
                        result = result.astype(out.dtype)
                        out[j, y] = result
                        if len(outs) == 3:
                            if x >= planes - RADIUS:
                                outs[1][x - planes + RADIUS, y] = result
                            if x < RADIUS:
                                outs[2][x, y] = result
                        return carry

                    lax.fori_loop(0, ny, row, 0)

    return kernel


def stencil_stage_whole(stage, block, sends, potential_wide, initial=None, keep_sends=True):
    planes, ny, nz, nb = block.shape
    blocks, depth = plane_blocks(planes)
    whole = pl.BlockSpec(block.shape, lambda i: (0, 0, 0, 0))
    edge = pl.BlockSpec((RADIUS, ny, nz, nb), lambda i: (0, 0, 0, 0))
    part = pl.BlockSpec((depth, ny, nz, nb), lambda i: (i, 0, 0, 0))
    low, high = exchange(sends, "domain")
    partial = pl.pallas_call(
        interior_kernel(stage, planes, ny, nz),
        grid=(blocks,),
        in_specs=[whole, part],
        out_specs=part,
        out_shape=jax.ShapeDtypeStruct(block.shape, jnp.float32),
        scratch_shapes=[pltpu.VMEM(block.shape, jnp.float32)],
        name=f"interior_{stage}",
    )(block, potential_wide)
    operands = [low, high, partial]
    in_specs = [edge, edge, part]
    if initial is not None:
        operands.append(initial)
        in_specs.append(part)
    shapes = [jax.ShapeDtypeStruct(block.shape, jnp.bfloat16)]
    out_specs = [part]
    if keep_sends:
        edge_shape = jax.ShapeDtypeStruct((RADIUS, ny, nz, nb), jnp.bfloat16)
        shapes += [edge_shape, edge_shape]
        out_specs += [edge, edge]
    return pl.pallas_call(
        finish_kernel_whole(stage, planes, ny),
        grid=(blocks,),
        in_specs=in_specs,
        out_specs=tuple(out_specs),
        out_shape=tuple(shapes),
        name=f"finish_{stage}",
    )(*operands)


def exchange(sends, axis):
    count = lax.axis_size(axis)
    forward = [(i, (i + 1) % count) for i in range(count)]
    backward = [(target, source) for source, target in forward]
    return lax.ppermute(sends[0], axis, forward), lax.ppermute(sends[1], axis, backward)


def butterfly_sum(values, axis):
    count = lax.axis_size(axis)
    bit = 1
    while bit < count:
        pairs = [(i, i ^ bit) for i in range(count)]
        values = values + lax.ppermute(values, axis, pairs)
        bit *= 2
    return values


def shards(orbitals, potential):
    planes, ny, nz, nb = orbitals.shape
    potential_wide = jnp.broadcast_to(potential[:, :, :, None], (planes, ny, nz, nb))
    cell_count = planes * ny * nz
    cell_weight = 1.0 / (cell_count * lax.axis_size("domain"))
    band = lax.axis_index("band")
    gram = lambda rows, cols: with_layout_constraint(
        jnp.einsum("cb,ck->bk", rows, cols, preferred_element_type=jnp.float32),
        Layout((0, 1)),
    )
    placed = lambda mine, theirs: jnp.where(
        band == 0,
        jnp.concatenate([mine, theirs], axis=1),
        jnp.concatenate([theirs, mine], axis=1),
    )
    planes_sent = (
        lax.slice_in_dim(orbitals, planes - RADIUS, None, axis=0),
        lax.slice_in_dim(orbitals, 0, RADIUS, axis=0),
    )
    first, *first_sent = stencil_stage("first", orbitals, planes_sent, potential_wide)
    filtered, *filtered_sent = stencil_stage(
        "filtered", first, first_sent, potential_wide, orbitals
    )
    own_block = filtered.reshape(cell_count, nb)
    swap = [(0, 1), (1, 0)]
    halves = [half.reshape(-1, nb) for half in (filtered_sent[1], filtered_sent[0])]
    partner_halves = [lax.ppermute(half, "band", swap) for half in halves]
    split_rows = lambda block: (block[: cell_count // 2], block[cell_count // 2 :])
    cross = lambda block: sum(
        gram(rows, cols) for rows, cols in zip(split_rows(block), partner_halves)
    )
    correlation_piece = placed(gram(own_block, own_block), cross(own_block))
    correlation = butterfly_sum(correlation_piece, "domain") * cell_weight
    (applied_grid,) = stencil_stage(
        "applied", filtered, filtered_sent, potential_wide, keep_sends=False
    )
    applied = applied_grid.reshape(cell_count, nb)
    energy_piece = placed(gram(applied, own_block), cross(applied))
    projected = butterfly_sum(energy_piece, "domain") * cell_weight
    return (filtered, correlation, projected)


def solution(mesh):
    placed = (P("domain", None, None, "band"), P("domain", None, None))
    return jax.shard_map(
        shards,
        mesh=mesh,
        in_specs=placed,
        out_specs=(P("domain", None, None, "band"), P("band", None), P("band", None)),
        check_vma=False,
    )
```

```python
import jax
import jax.numpy as jnp
from jax import lax
from jax.experimental import pallas as pl
from jax.experimental.pallas import tpu as pltpu
from jax.experimental.layout import Layout, with_layout_constraint
from jax.sharding import PartitionSpec as P

RADIUS = 4


stencil_weights = (-205.0 / 72.0, 8.0 / 5.0, -1.0 / 5.0, 8.0 / 315.0, -1.0 / 560.0)
spectrum_centre = 6.0
first_factor = -0.125
second_factor = -1.0 / 7.0
memory_factor = -1.0 / 7.0


def plane_blocks(planes):
    return (planes // RADIUS, RADIUS) if planes % RADIUS == 0 else (1, planes)


def interior_kernel(stage, planes, ny, nz):
    shift = 0.0 if stage == "applied" else spectrum_centre
    blocks, depth = plane_blocks(planes)

    def kernel(own_narrow, pot, out, own):
        step = pl.program_id(0)

        @pl.when(step == 0)
        def _():
            for x in range(planes):
                own[x] = own_narrow[x].astype(jnp.float32)

        for block in range(blocks):
            @pl.when(step == block)
            def _(block=block):
                for j in range(depth):
                    x = block * depth + j

                    def row(y, carry, x=x, j=j):
                        centre = own[x, y]
                        summed = (3.0 * stencil_weights[0]) * centre
                        for k in range(1, RADIUS + 1):
                            beside = own[x, (y + k) % ny] + own[x, (y + ny - k) % ny]
                            beside = beside + (
                                pltpu.roll(centre, k, 0) + pltpu.roll(centre, nz - k, 0)
                            )
                            if x + k < planes:
                                beside = beside + own[x + k, y]
                            if x - k >= 0:
                                beside = beside + own[x - k, y]
                            summed = summed + stencil_weights[k] * beside
                        applied = -0.5 * summed + pot[j, y] * centre
                        if shift:
                            applied = applied - shift * centre
                        out[j, y] = applied
                        return carry

                    lax.fori_loop(0, ny, row, 0)

    return kernel


def finish_kernel(stage, planes, ny, blocks, depth):

    def kernel(*refs):
        refs = list(refs)
        low, partial = refs[:2]
        high = low
        initial = refs[2] if stage == "filtered" else None
        outs = refs[3:] if stage == "filtered" else refs[2:]
        out = outs[0]
        step = pl.program_id(0)
        for block in range(blocks):
            @pl.when(step == block)
            def _(block=block):
                for j in range(depth):
                    x = block * depth + j

                    def row(y, carry, x=x, j=j):
                        summed = partial[j, y]
                        for k in range(1, RADIUS + 1):
                            outside = []
                            if x + k >= planes:
                                outside.append(high[x + k - planes, y].astype(jnp.float32))
                            if x - k < 0:
                                outside.append(low[x - k + RADIUS, y].astype(jnp.float32))
                            if outside:
                                term = outside[0] if len(outside) == 1 else outside[0] + outside[1]
                                summed = summed + (-0.5 * stencil_weights[k]) * term
                        if stage == "first":
                            result = summed * first_factor
                        elif stage == "filtered":
                            result = summed * second_factor + (
                                memory_factor * initial[j, y].astype(jnp.float32)
                            )
                        else:
                            result = summed
                        result = result.astype(out.dtype)
                        out[j, y] = result
                        if len(outs) == 3:
                            if x >= planes - RADIUS:
                                outs[1][x - planes + RADIUS, y] = result
                            if x < RADIUS:
                                outs[2][x, y] = result
                        return carry

                    lax.fori_loop(0, ny, row, 0)

    return kernel


def stencil_stage(stage, block, sends, potential_wide, initial=None, keep_sends=True):
    planes, ny, nz, nb = block.shape
    blocks, depth = plane_blocks(planes)
    if blocks < 2:
        return stencil_stage_whole(stage, block, sends, potential_wide, initial, keep_sends)
    whole = pl.BlockSpec(block.shape, lambda i: (0, 0, 0, 0))
    edge = pl.BlockSpec((RADIUS, ny, nz, nb), lambda i: (0, 0, 0, 0))
    part = pl.BlockSpec((depth, ny, nz, nb), lambda i: (i, 0, 0, 0))
    low, high = exchange(sends, "domain")
    partial = pl.pallas_call(
        interior_kernel(stage, planes, ny, nz),
        grid=(blocks,),
        in_specs=[whole, part],
        out_specs=part,
        out_shape=jax.ShapeDtypeStruct(block.shape, jnp.float32),
        scratch_shapes=[pltpu.VMEM(block.shape, jnp.float32)],
        name=f"interior_{stage}",
    )(block, potential_wide)
    fine = RADIUS // 2 if RADIUS % 2 == 0 else RADIUS
    fine_blocks = planes // fine
    fine_part = pl.BlockSpec((fine, ny, nz, nb), lambda i: (i, 0, 0, 0))
    halos = jnp.concatenate([low, high], axis=0)
    halo_block = pl.BlockSpec(
        (RADIUS, ny, nz, nb), lambda i: (jnp.where(i * fine < RADIUS, 0, 1), 0, 0, 0)
    )
    operands = [halos, partial]
    in_specs = [halo_block, fine_part]
    if initial is not None:
        operands.append(initial)
        in_specs.append(fine_part)
    shapes = [jax.ShapeDtypeStruct(block.shape, jnp.bfloat16)]
    out_specs = [fine_part]
    if keep_sends:
        edge_shape = jax.ShapeDtypeStruct((RADIUS, ny, nz, nb), jnp.bfloat16)
        shapes += [edge_shape, edge_shape]
        out_specs += [edge, edge]
    return pl.pallas_call(
        finish_kernel(stage, planes, ny, fine_blocks, fine),
        grid=(fine_blocks,),
        in_specs=in_specs,
        out_specs=tuple(out_specs),
        out_shape=tuple(shapes),
        name=f"finish_{stage}",
    )(*operands)


def finish_kernel_whole(stage, planes, ny):
    blocks, depth = plane_blocks(planes)

    def kernel(*refs):
        refs = list(refs)
        low, high, partial = refs[:3]
        initial = refs[3] if stage == "filtered" else None
        outs = refs[4:] if stage == "filtered" else refs[3:]
        out = outs[0]
        step = pl.program_id(0)
        for block in range(blocks):
            @pl.when(step == block)
            def _(block=block):
                for j in range(depth):
                    x = block * depth + j

                    def row(y, carry, x=x, j=j):
                        summed = partial[j, y]
                        for k in range(1, RADIUS + 1):
                            outside = []
                            if x + k >= planes:
                                outside.append(high[x + k - planes, y].astype(jnp.float32))
                            if x - k < 0:
                                outside.append(low[x - k + RADIUS, y].astype(jnp.float32))
                            if outside:
                                term = outside[0] if len(outside) == 1 else outside[0] + outside[1]
                                summed = summed + (-0.5 * stencil_weights[k]) * term
                        if stage == "first":
                            result = summed * first_factor
                        elif stage == "filtered":
                            result = summed * second_factor + (
                                memory_factor * initial[j, y].astype(jnp.float32)
                            )
                        else:
                            result = summed
                        result = result.astype(out.dtype)
                        out[j, y] = result
                        if len(outs) == 3:
                            if x >= planes - RADIUS:
                                outs[1][x - planes + RADIUS, y] = result
                            if x < RADIUS:
                                outs[2][x, y] = result
                        return carry

                    lax.fori_loop(0, ny, row, 0)

    return kernel


def stencil_stage_whole(stage, block, sends, potential_wide, initial=None, keep_sends=True):
    planes, ny, nz, nb = block.shape
    blocks, depth = plane_blocks(planes)
    whole = pl.BlockSpec(block.shape, lambda i: (0, 0, 0, 0))
    edge = pl.BlockSpec((RADIUS, ny, nz, nb), lambda i: (0, 0, 0, 0))
    part = pl.BlockSpec((depth, ny, nz, nb), lambda i: (i, 0, 0, 0))
    low, high = exchange(sends, "domain")
    partial = pl.pallas_call(
        interior_kernel(stage, planes, ny, nz),
        grid=(blocks,),
        in_specs=[whole, part],
        out_specs=part,
        out_shape=jax.ShapeDtypeStruct(block.shape, jnp.float32),
        scratch_shapes=[pltpu.VMEM(block.shape, jnp.float32)],
        name=f"interior_{stage}",
    )(block, potential_wide)
    operands = [low, high, partial]
    in_specs = [edge, edge, part]
    if initial is not None:
        operands.append(initial)
        in_specs.append(part)
    shapes = [jax.ShapeDtypeStruct(block.shape, jnp.bfloat16)]
    out_specs = [part]
    if keep_sends:
        edge_shape = jax.ShapeDtypeStruct((RADIUS, ny, nz, nb), jnp.bfloat16)
        shapes += [edge_shape, edge_shape]
        out_specs += [edge, edge]
    return pl.pallas_call(
        finish_kernel_whole(stage, planes, ny),
        grid=(blocks,),
        in_specs=in_specs,
        out_specs=tuple(out_specs),
        out_shape=tuple(shapes),
        name=f"finish_{stage}",
    )(*operands)


def exchange(sends, axis):
    count = lax.axis_size(axis)
    forward = [(i, (i + 1) % count) for i in range(count)]
    backward = [(target, source) for source, target in forward]
    return lax.ppermute(sends[0], axis, forward), lax.ppermute(sends[1], axis, backward)


def butterfly_sum(values, axis):
    count = lax.axis_size(axis)
    bit = 1
    while bit < count:
        pairs = [(i, i ^ bit) for i in range(count)]
        values = values + lax.ppermute(values, axis, pairs)
        bit *= 2
    return values


def shards(orbitals, potential):
    planes, ny, nz, nb = orbitals.shape
    potential_wide = jnp.broadcast_to(potential[:, :, :, None], (planes, ny, nz, nb))
    cell_count = planes * ny * nz
    cell_weight = 1.0 / (cell_count * lax.axis_size("domain"))
    band = lax.axis_index("band")
    gram = lambda rows, cols: with_layout_constraint(
        jnp.einsum("cb,ck->bk", rows, cols, preferred_element_type=jnp.float32),
        Layout((0, 1)),
    )
    placed = lambda mine, theirs: jnp.where(
        band == 0,
        jnp.concatenate([mine, theirs], axis=1),
        jnp.concatenate([theirs, mine], axis=1),
    )
    planes_sent = (
        lax.slice_in_dim(orbitals, planes - RADIUS, None, axis=0),
        lax.slice_in_dim(orbitals, 0, RADIUS, axis=0),
    )
    first, *first_sent = stencil_stage("first", orbitals, planes_sent, potential_wide)
    filtered, *filtered_sent = stencil_stage(
        "filtered", first, first_sent, potential_wide, orbitals
    )
    own_block = filtered.reshape(cell_count, nb)
    partner = lax.ppermute(own_block, "band", [(0, 1), (1, 0)])
    correlation_piece = placed(gram(own_block, own_block), gram(own_block, partner))
    correlation = butterfly_sum(correlation_piece, "domain") * cell_weight
    (applied_grid,) = stencil_stage(
        "applied", filtered, filtered_sent, potential_wide, keep_sends=False
    )
    applied = applied_grid.reshape(cell_count, nb)
    energy_piece = placed(gram(applied, own_block), gram(applied, partner))
    projected = butterfly_sum(energy_piece, "domain") * cell_weight
    return (filtered, correlation, projected)


def solution(mesh):
    placed = (P("domain", None, None, "band"), P("domain", None, None))
    return jax.shard_map(
        shards,
        mesh=mesh,
        in_specs=placed,
        out_specs=(P("domain", None, None, "band"), P("band", None), P("band", None)),
        check_vma=False,
    )
```

```python
import jax
import jax.numpy as jnp
from jax import lax
from jax.experimental import pallas as pl
from jax.experimental.pallas import tpu as pltpu
from jax.experimental.layout import Layout, with_layout_constraint
from jax.sharding import PartitionSpec as P

RADIUS = 4


stencil_weights = (-205.0 / 72.0, 8.0 / 5.0, -1.0 / 5.0, 8.0 / 315.0, -1.0 / 560.0)
spectrum_centre = 6.0
first_factor = -0.125
second_factor = -1.0 / 7.0
memory_factor = -1.0 / 7.0


def plane_blocks(planes):
    return (planes // RADIUS, RADIUS) if planes % RADIUS == 0 else (1, planes)


def interior_kernel(stage, planes, ny, nz):
    shift = 0.0 if stage == "applied" else spectrum_centre
    blocks, depth = plane_blocks(planes)

    def kernel(own_narrow, pot, out, own):
        step = pl.program_id(0)

        @pl.when(step == 0)
        def _():
            for x in range(planes):
                own[x] = own_narrow[x].astype(jnp.float32)

        for block in range(blocks):
            @pl.when(step == block)
            def _(block=block):
                for j in range(depth):
                    x = block * depth + j

                    def row(y, carry, x=x, j=j):
                        centre = own[x, y]
                        summed = (3.0 * stencil_weights[0]) * centre
                        for k in range(1, RADIUS + 1):
                            beside = own[x, (y + k) % ny] + own[x, (y + ny - k) % ny]
                            beside = beside + (
                                pltpu.roll(centre, k, 0) + pltpu.roll(centre, nz - k, 0)
                            )
                            if x + k < planes:
                                beside = beside + own[x + k, y]
                            if x - k >= 0:
                                beside = beside + own[x - k, y]
                            summed = summed + stencil_weights[k] * beside
                        applied = -0.5 * summed + pot[j, y] * centre
                        if shift:
                            applied = applied - shift * centre
                        out[j, y] = applied
                        return carry

                    lax.fori_loop(0, ny, row, 0)

    return kernel


def finish_kernel(stage, planes, ny):
    blocks, depth = plane_blocks(planes)

    def kernel(*refs):
        refs = list(refs)
        low, partial = refs[:2]
        high = low
        initial = refs[2] if stage == "filtered" else None
        outs = refs[3:] if stage == "filtered" else refs[2:]
        out = outs[0]
        step = pl.program_id(0)
        for block in range(blocks):
            @pl.when(step == block)
            def _(block=block):
                for j in range(depth):
                    x = block * depth + j

                    def row(y, carry, x=x, j=j):
                        summed = partial[j, y]
                        for k in range(1, RADIUS + 1):
                            outside = []
                            if x + k >= planes:
                                outside.append(high[x + k - planes, y].astype(jnp.float32))
                            if x - k < 0:
                                outside.append(low[x - k + RADIUS, y].astype(jnp.float32))
                            if outside:
                                term = outside[0] if len(outside) == 1 else outside[0] + outside[1]
                                summed = summed + (-0.5 * stencil_weights[k]) * term
                        if stage == "first":
                            result = summed * first_factor
                        elif stage == "filtered":
                            result = summed * second_factor + (
                                memory_factor * initial[j, y].astype(jnp.float32)
                            )
                        else:
                            result = summed
                        result = result.astype(out.dtype)
                        out[j, y] = result
                        if len(outs) == 3:
                            if x >= planes - RADIUS:
                                outs[1][x - planes + RADIUS, y] = result
                            if x < RADIUS:
                                outs[2][x, y] = result
                        return carry

                    lax.fori_loop(0, ny, row, 0)

    return kernel


def stencil_stage(stage, block, sends, potential_wide, initial=None, keep_sends=True):
    planes, ny, nz, nb = block.shape
    blocks, depth = plane_blocks(planes)
    if blocks < 2:
        return stencil_stage_whole(stage, block, sends, potential_wide, initial, keep_sends)
    whole = pl.BlockSpec(block.shape, lambda i: (0, 0, 0, 0))
    edge = pl.BlockSpec((RADIUS, ny, nz, nb), lambda i: (0, 0, 0, 0))
    part = pl.BlockSpec((depth, ny, nz, nb), lambda i: (i, 0, 0, 0))
    low, high = exchange(sends, "domain")
    partial = pl.pallas_call(
        interior_kernel(stage, planes, ny, nz),
        grid=(blocks,),
        in_specs=[whole, part],
        out_specs=part,
        out_shape=jax.ShapeDtypeStruct(block.shape, jnp.float32),
        scratch_shapes=[pltpu.VMEM(block.shape, jnp.float32)],
        name=f"interior_{stage}",
    )(block, potential_wide)
    halos = jnp.concatenate([low, high], axis=0)
    halo_block = pl.BlockSpec((RADIUS, ny, nz, nb), lambda i: (jnp.minimum(i, 1), 0, 0, 0))
    operands = [halos, partial]
    in_specs = [halo_block, part]
    if initial is not None:
        operands.append(initial)
        in_specs.append(part)
    shapes = [jax.ShapeDtypeStruct(block.shape, jnp.bfloat16)]
    out_specs = [part]
    if keep_sends:
        edge_shape = jax.ShapeDtypeStruct((RADIUS, ny, nz, nb), jnp.bfloat16)
        shapes += [edge_shape, edge_shape]
        out_specs += [edge, edge]
    return pl.pallas_call(
        finish_kernel(stage, planes, ny),
        grid=(blocks,),
        in_specs=in_specs,
        out_specs=tuple(out_specs),
        out_shape=tuple(shapes),
        name=f"finish_{stage}",
    )(*operands)


def finish_kernel_whole(stage, planes, ny):
    blocks, depth = plane_blocks(planes)

    def kernel(*refs):
        refs = list(refs)
        low, high, partial = refs[:3]
        initial = refs[3] if stage == "filtered" else None
        outs = refs[4:] if stage == "filtered" else refs[3:]
        out = outs[0]
        step = pl.program_id(0)
        for block in range(blocks):
            @pl.when(step == block)
            def _(block=block):
                for j in range(depth):
                    x = block * depth + j

                    def row(y, carry, x=x, j=j):
                        summed = partial[j, y]
                        for k in range(1, RADIUS + 1):
                            outside = []
                            if x + k >= planes:
                                outside.append(high[x + k - planes, y].astype(jnp.float32))
                            if x - k < 0:
                                outside.append(low[x - k + RADIUS, y].astype(jnp.float32))
                            if outside:
                                term = outside[0] if len(outside) == 1 else outside[0] + outside[1]
                                summed = summed + (-0.5 * stencil_weights[k]) * term
                        if stage == "first":
                            result = summed * first_factor
                        elif stage == "filtered":
                            result = summed * second_factor + (
                                memory_factor * initial[j, y].astype(jnp.float32)
                            )
                        else:
                            result = summed
                        result = result.astype(out.dtype)
                        out[j, y] = result
                        if len(outs) == 3:
                            if x >= planes - RADIUS:
                                outs[1][x - planes + RADIUS, y] = result
                            if x < RADIUS:
                                outs[2][x, y] = result
                        return carry

                    lax.fori_loop(0, ny, row, 0)

    return kernel


def stencil_stage_whole(stage, block, sends, potential_wide, initial=None, keep_sends=True):
    planes, ny, nz, nb = block.shape
    blocks, depth = plane_blocks(planes)
    whole = pl.BlockSpec(block.shape, lambda i: (0, 0, 0, 0))
    edge = pl.BlockSpec((RADIUS, ny, nz, nb), lambda i: (0, 0, 0, 0))
    part = pl.BlockSpec((depth, ny, nz, nb), lambda i: (i, 0, 0, 0))
    low, high = exchange(sends, "domain")
    partial = pl.pallas_call(
        interior_kernel(stage, planes, ny, nz),
        grid=(blocks,),
        in_specs=[whole, part],
        out_specs=part,
        out_shape=jax.ShapeDtypeStruct(block.shape, jnp.float32),
        scratch_shapes=[pltpu.VMEM(block.shape, jnp.float32)],
        name=f"interior_{stage}",
    )(block, potential_wide)
    operands = [low, high, partial]
    in_specs = [edge, edge, part]
    if initial is not None:
        operands.append(initial)
        in_specs.append(part)
    shapes = [jax.ShapeDtypeStruct(block.shape, jnp.bfloat16)]
    out_specs = [part]
    if keep_sends:
        edge_shape = jax.ShapeDtypeStruct((RADIUS, ny, nz, nb), jnp.bfloat16)
        shapes += [edge_shape, edge_shape]
        out_specs += [edge, edge]
    return pl.pallas_call(
        finish_kernel_whole(stage, planes, ny),
        grid=(blocks,),
        in_specs=in_specs,
        out_specs=tuple(out_specs),
        out_shape=tuple(shapes),
        name=f"finish_{stage}",
    )(*operands)


def exchange(sends, axis):
    count = lax.axis_size(axis)
    forward = [(i, (i + 1) % count) for i in range(count)]
    backward = [(target, source) for source, target in forward]
    return lax.ppermute(sends[0], axis, forward), lax.ppermute(sends[1], axis, backward)


def butterfly_sum(values, axis):
    count = lax.axis_size(axis)
    bit = count // 2
    while bit >= 1:
        pairs = [(i, i ^ bit) for i in range(count)]
        values = values + lax.ppermute(values, axis, pairs)
        bit //= 2
    return values


def shards(orbitals, potential):
    planes, ny, nz, nb = orbitals.shape
    potential_wide = jnp.broadcast_to(potential[:, :, :, None], (planes, ny, nz, nb))
    cell_count = planes * ny * nz
    cell_weight = 1.0 / (cell_count * lax.axis_size("domain"))
    band = lax.axis_index("band")
    gram = lambda rows, cols: with_layout_constraint(
        jnp.einsum("cb,ck->bk", rows, cols, preferred_element_type=jnp.float32),
        Layout((0, 1)),
    )
    placed = lambda mine, theirs: jnp.where(
        band == 0,
        jnp.concatenate([mine, theirs], axis=1),
        jnp.concatenate([theirs, mine], axis=1),
    )
    planes_sent = (
        lax.slice_in_dim(orbitals, planes - RADIUS, None, axis=0),
        lax.slice_in_dim(orbitals, 0, RADIUS, axis=0),
    )
    first, *first_sent = stencil_stage("first", orbitals, planes_sent, potential_wide)
    filtered, *filtered_sent = stencil_stage(
        "filtered", first, first_sent, potential_wide, orbitals
    )
    own_block = filtered.reshape(cell_count, nb)
    partner = lax.ppermute(own_block, "band", [(0, 1), (1, 0)])
    correlation_piece = placed(gram(own_block, own_block), gram(own_block, partner))
    correlation = butterfly_sum(correlation_piece, "domain") * cell_weight
    (applied_grid,) = stencil_stage(
        "applied", filtered, filtered_sent, potential_wide, keep_sends=False
    )
    applied = applied_grid.reshape(cell_count, nb)
    energy_piece = placed(gram(applied, own_block), gram(applied, partner))
    projected = butterfly_sum(energy_piece, "domain") * cell_weight
    return (filtered, correlation, projected)


def solution(mesh):
    placed = (P("domain", None, None, "band"), P("domain", None, None))
    return jax.shard_map(
        shards,
        mesh=mesh,
        in_specs=placed,
        out_specs=(P("domain", None, None, "band"), P("band", None), P("band", None)),
        check_vma=False,
    )
```

```python
import jax
import jax.numpy as jnp
from jax import lax
from jax.experimental import pallas as pl
from jax.experimental.pallas import tpu as pltpu
from jax.experimental.layout import Layout, with_layout_constraint
from jax.sharding import PartitionSpec as P

RADIUS = 4


stencil_weights = (-205.0 / 72.0, 8.0 / 5.0, -1.0 / 5.0, 8.0 / 315.0, -1.0 / 560.0)
spectrum_centre = 6.0
first_factor = -0.125
second_factor = -1.0 / 7.0
memory_factor = -1.0 / 7.0


def plane_blocks(planes):
    return (planes // RADIUS, RADIUS) if planes % RADIUS == 0 else (1, planes)


def interior_kernel(stage, planes, ny, nz):
    shift = 0.0 if stage == "applied" else spectrum_centre
    blocks, depth = plane_blocks(planes)

    def kernel(own_narrow, pot, out, own):
        step = pl.program_id(0)

        @pl.when(step == 0)
        def _():
            for x in range(planes):
                own[x] = own_narrow[x].astype(jnp.float32)

        for block in range(blocks):
            @pl.when(step == block)
            def _(block=block):
                for j in range(depth):
                    x = block * depth + j

                    def row(y, carry, x=x, j=j):
                        centre = own[x, y]
                        summed = (3.0 * stencil_weights[0]) * centre
                        for k in range(1, RADIUS + 1):
                            beside = own[x, (y + k) % ny] + own[x, (y + ny - k) % ny]
                            beside = beside + (
                                pltpu.roll(centre, k, 0) + pltpu.roll(centre, nz - k, 0)
                            )
                            if x + k < planes:
                                beside = beside + own[x + k, y]
                            if x - k >= 0:
                                beside = beside + own[x - k, y]
                            summed = summed + stencil_weights[k] * beside
                        applied = -0.5 * summed + pot[j, y] * centre
                        if shift:
                            applied = applied - shift * centre
                        out[j, y] = applied
                        return carry

                    lax.fori_loop(0, ny, row, 0)

    return kernel


def finish_kernel(stage, planes, ny):
    blocks, depth = plane_blocks(planes)

    def kernel(*refs):
        refs = list(refs)
        low, partial = refs[:2]
        high = low
        initial = refs[2] if stage == "filtered" else None
        outs = refs[3:] if stage == "filtered" else refs[2:]
        out = outs[0]
        step = pl.program_id(0)
        for block in range(blocks):
            @pl.when(step == block)
            def _(block=block):
                for j in range(depth):
                    x = block * depth + j

                    def row(y, carry, x=x, j=j):
                        summed = partial[j, y]
                        for k in range(1, RADIUS + 1):
                            outside = []
                            if x + k >= planes:
                                outside.append(high[x + k - planes, y].astype(jnp.float32))
                            if x - k < 0:
                                outside.append(low[x - k + RADIUS, y].astype(jnp.float32))
                            if outside:
                                term = outside[0] if len(outside) == 1 else outside[0] + outside[1]
                                summed = summed + (-0.5 * stencil_weights[k]) * term
                        if stage == "first":
                            result = summed * first_factor
                        elif stage == "filtered":
                            result = summed * second_factor + (
                                memory_factor * initial[j, y].astype(jnp.float32)
                            )
                        else:
                            result = summed
                        result = result.astype(out.dtype)
                        out[j, y] = result
                        if len(outs) == 3:
                            if x >= planes - RADIUS:
                                outs[1][x - planes + RADIUS, y] = result
                            if x < RADIUS:
                                outs[2][x, y] = result
                        return carry

                    lax.fori_loop(0, ny, row, 0)

    return kernel


def stencil_stage(stage, block, sends, potential_wide, initial=None, keep_sends=True):
    planes, ny, nz, nb = block.shape
    blocks, depth = plane_blocks(planes)
    if blocks < 2:
        return stencil_stage_whole(stage, block, sends, potential_wide, initial, keep_sends)
    whole = pl.BlockSpec(block.shape, lambda i: (0, 0, 0, 0))
    edge = pl.BlockSpec((RADIUS, ny, nz, nb), lambda i: (0, 0, 0, 0))
    part = pl.BlockSpec((depth, ny, nz, nb), lambda i: (i, 0, 0, 0))
    low, high = exchange(sends, "domain")
    partial = pl.pallas_call(
        interior_kernel(stage, planes, ny, nz),
        grid=(blocks,),
        in_specs=[whole, part],
        out_specs=part,
        out_shape=jax.ShapeDtypeStruct(block.shape, jnp.float32),
        scratch_shapes=[pltpu.VMEM(block.shape, jnp.float32)],
        name=f"interior_{stage}",
    )(block, potential_wide)
    halos = jnp.concatenate([low, high], axis=0)
    halo_block = pl.BlockSpec((RADIUS, ny, nz, nb), lambda i: (jnp.minimum(i, 1), 0, 0, 0))
    operands = [halos, partial]
    in_specs = [halo_block, part]
    if initial is not None:
        operands.append(initial)
        in_specs.append(part)
    shapes = [jax.ShapeDtypeStruct(block.shape, jnp.bfloat16)]
    out_specs = [part]
    if keep_sends:
        edge_shape = jax.ShapeDtypeStruct((RADIUS, ny, nz, nb), jnp.bfloat16)
        shapes += [edge_shape, edge_shape]
        out_specs += [edge, edge]
    return pl.pallas_call(
        finish_kernel(stage, planes, ny),
        grid=(blocks,),
        in_specs=in_specs,
        out_specs=tuple(out_specs),
        out_shape=tuple(shapes),
        name=f"finish_{stage}",
    )(*operands)


def finish_kernel_whole(stage, planes, ny):
    blocks, depth = plane_blocks(planes)

    def kernel(*refs):
        refs = list(refs)
        low, high, partial = refs[:3]
        initial = refs[3] if stage == "filtered" else None
        outs = refs[4:] if stage == "filtered" else refs[3:]
        out = outs[0]
        step = pl.program_id(0)
        for block in range(blocks):
            @pl.when(step == block)
            def _(block=block):
                for j in range(depth):
                    x = block * depth + j

                    def row(y, carry, x=x, j=j):
                        summed = partial[j, y]
                        for k in range(1, RADIUS + 1):
                            outside = []
                            if x + k >= planes:
                                outside.append(high[x + k - planes, y].astype(jnp.float32))
                            if x - k < 0:
                                outside.append(low[x - k + RADIUS, y].astype(jnp.float32))
                            if outside:
                                term = outside[0] if len(outside) == 1 else outside[0] + outside[1]
                                summed = summed + (-0.5 * stencil_weights[k]) * term
                        if stage == "first":
                            result = summed * first_factor
                        elif stage == "filtered":
                            result = summed * second_factor + (
                                memory_factor * initial[j, y].astype(jnp.float32)
                            )
                        else:
                            result = summed
                        result = result.astype(out.dtype)
                        out[j, y] = result
                        if len(outs) == 3:
                            if x >= planes - RADIUS:
                                outs[1][x - planes + RADIUS, y] = result
                            if x < RADIUS:
                                outs[2][x, y] = result
                        return carry

                    lax.fori_loop(0, ny, row, 0)

    return kernel


def stencil_stage_whole(stage, block, sends, potential_wide, initial=None, keep_sends=True):
    planes, ny, nz, nb = block.shape
    blocks, depth = plane_blocks(planes)
    whole = pl.BlockSpec(block.shape, lambda i: (0, 0, 0, 0))
    edge = pl.BlockSpec((RADIUS, ny, nz, nb), lambda i: (0, 0, 0, 0))
    part = pl.BlockSpec((depth, ny, nz, nb), lambda i: (i, 0, 0, 0))
    low, high = exchange(sends, "domain")
    partial = pl.pallas_call(
        interior_kernel(stage, planes, ny, nz),
        grid=(blocks,),
        in_specs=[whole, part],
        out_specs=part,
        out_shape=jax.ShapeDtypeStruct(block.shape, jnp.float32),
        scratch_shapes=[pltpu.VMEM(block.shape, jnp.float32)],
        name=f"interior_{stage}",
    )(block, potential_wide)
    operands = [low, high, partial]
    in_specs = [edge, edge, part]
    if initial is not None:
        operands.append(initial)
        in_specs.append(part)
    shapes = [jax.ShapeDtypeStruct(block.shape, jnp.bfloat16)]
    out_specs = [part]
    if keep_sends:
        edge_shape = jax.ShapeDtypeStruct((RADIUS, ny, nz, nb), jnp.bfloat16)
        shapes += [edge_shape, edge_shape]
        out_specs += [edge, edge]
    return pl.pallas_call(
        finish_kernel_whole(stage, planes, ny),
        grid=(blocks,),
        in_specs=in_specs,
        out_specs=tuple(out_specs),
        out_shape=tuple(shapes),
        name=f"finish_{stage}",
    )(*operands)


def exchange(sends, axis):
    count = lax.axis_size(axis)
    forward = [(i, (i + 1) % count) for i in range(count)]
    backward = [(target, source) for source, target in forward]
    return lax.ppermute(sends[0], axis, forward), lax.ppermute(sends[1], axis, backward)


def butterfly_sum(values, axis):
    count = lax.axis_size(axis)
    index = lax.axis_index(axis)
    pairs_of = lambda bit: [(i, i ^ bit) for i in range(count)]
    half = values.shape[0] // 2
    upper = index % 2
    keep = lax.dynamic_slice_in_dim(values, upper * half, half, axis=0)
    send = lax.dynamic_slice_in_dim(values, (1 - upper) * half, half, axis=0)
    values = keep + lax.ppermute(send, axis, pairs_of(1))
    bit = count // 2
    while bit >= 2:
        values = values + lax.ppermute(values, axis, pairs_of(bit))
        bit //= 2
    other = lax.ppermute(values, axis, pairs_of(1))
    return jnp.where(
        upper == 0,
        jnp.concatenate([values, other], axis=0),
        jnp.concatenate([other, values], axis=0),
    )


def shards(orbitals, potential):
    planes, ny, nz, nb = orbitals.shape
    potential_wide = jnp.broadcast_to(potential[:, :, :, None], (planes, ny, nz, nb))
    cell_count = planes * ny * nz
    cell_weight = 1.0 / (cell_count * lax.axis_size("domain"))
    band = lax.axis_index("band")
    gram = lambda rows, cols: with_layout_constraint(
        jnp.einsum("cb,ck->bk", rows, cols, preferred_element_type=jnp.float32),
        Layout((0, 1)),
    )
    placed = lambda mine, theirs: jnp.where(
        band == 0,
        jnp.concatenate([mine, theirs], axis=1),
        jnp.concatenate([theirs, mine], axis=1),
    )
    planes_sent = (
        lax.slice_in_dim(orbitals, planes - RADIUS, None, axis=0),
        lax.slice_in_dim(orbitals, 0, RADIUS, axis=0),
    )
    first, *first_sent = stencil_stage("first", orbitals, planes_sent, potential_wide)
    filtered, *filtered_sent = stencil_stage(
        "filtered", first, first_sent, potential_wide, orbitals
    )
    own_block = filtered.reshape(cell_count, nb)
    partner = lax.ppermute(own_block, "band", [(0, 1), (1, 0)])
    correlation_piece = placed(gram(own_block, own_block), gram(own_block, partner))
    correlation = butterfly_sum(correlation_piece, "domain") * cell_weight
    (applied_grid,) = stencil_stage(
        "applied", filtered, filtered_sent, potential_wide, keep_sends=False
    )
    applied = applied_grid.reshape(cell_count, nb)
    energy_piece = placed(gram(applied, own_block), gram(applied, partner))
    projected = butterfly_sum(energy_piece, "domain") * cell_weight
    return (filtered, correlation, projected)


def solution(mesh):
    placed = (P("domain", None, None, "band"), P("domain", None, None))
    return jax.shard_map(
        shards,
        mesh=mesh,
        in_specs=placed,
        out_specs=(P("domain", None, None, "band"), P("band", None), P("band", None)),
        check_vma=False,
    )
```

```python
import jax
import jax.numpy as jnp
from jax import lax
from jax.experimental import pallas as pl
from jax.experimental.pallas import tpu as pltpu
from jax.experimental.layout import Layout, with_layout_constraint
from jax.sharding import PartitionSpec as P

RADIUS = 4


stencil_weights = (-205.0 / 72.0, 8.0 / 5.0, -1.0 / 5.0, 8.0 / 315.0, -1.0 / 560.0)
spectrum_centre = 6.0
first_factor = -0.125
second_factor = -1.0 / 7.0
memory_factor = -1.0 / 7.0


def plane_blocks(planes):
    return (planes // RADIUS, RADIUS) if planes % RADIUS == 0 else (1, planes)


def interior_kernel(stage, planes, ny, nz):
    shift = 0.0 if stage == "applied" else spectrum_centre
    blocks, depth = plane_blocks(planes)

    def kernel(own_narrow, pot, out, own):
        step = pl.program_id(0)

        @pl.when(step == 0)
        def _():
            for x in range(planes):
                own[x] = own_narrow[x].astype(jnp.float32)

        for block in range(blocks):
            @pl.when(step == block)
            def _(block=block):
                for j in range(depth):
                    x = block * depth + j

                    def row(y, carry, x=x, j=j):
                        centre = own[x, y]
                        summed = (3.0 * stencil_weights[0]) * centre
                        for k in range(1, RADIUS + 1):
                            beside = own[x, (y + k) % ny] + own[x, (y + ny - k) % ny]
                            beside = beside + (
                                pltpu.roll(centre, k, 0) + pltpu.roll(centre, nz - k, 0)
                            )
                            if x + k < planes:
                                beside = beside + own[x + k, y]
                            if x - k >= 0:
                                beside = beside + own[x - k, y]
                            summed = summed + stencil_weights[k] * beside
                        applied = -0.5 * summed + pot[j, y] * centre
                        if shift:
                            applied = applied - shift * centre
                        out[j, y] = applied
                        return carry

                    lax.fori_loop(0, ny, row, 0)

    return kernel


def finish_kernel(stage, planes, ny):
    blocks, depth = plane_blocks(planes)

    def kernel(*refs):
        refs = list(refs)
        low, partial = refs[:2]
        high = low
        initial = refs[2] if stage == "filtered" else None
        outs = refs[3:] if stage == "filtered" else refs[2:]
        out = outs[0]
        step = pl.program_id(0)
        for block in range(blocks):
            @pl.when(step == block)
            def _(block=block):
                for j in range(depth):
                    x = block * depth + j

                    def row(y, carry, x=x, j=j):
                        summed = partial[j, y]
                        for k in range(1, RADIUS + 1):
                            outside = []
                            if x + k >= planes:
                                outside.append(high[x + k - planes, y].astype(jnp.float32))
                            if x - k < 0:
                                outside.append(low[x - k + RADIUS, y].astype(jnp.float32))
                            if outside:
                                term = outside[0] if len(outside) == 1 else outside[0] + outside[1]
                                summed = summed + (-0.5 * stencil_weights[k]) * term
                        if stage == "first":
                            result = summed * first_factor
                        elif stage == "filtered":
                            result = summed * second_factor + (
                                memory_factor * initial[j, y].astype(jnp.float32)
                            )
                        else:
                            result = summed
                        result = result.astype(out.dtype)
                        out[j, y] = result
                        if len(outs) == 3:
                            if x >= planes - RADIUS:
                                outs[1][x - planes + RADIUS, y] = result
                            if x < RADIUS:
                                outs[2][x, y] = result
                        return carry

                    lax.fori_loop(0, ny, row, 0)

    return kernel


def stencil_stage(stage, block, sends, potential_wide, initial=None, keep_sends=True):
    planes, ny, nz, nb = block.shape
    blocks, depth = plane_blocks(planes)
    if blocks < 2:
        return stencil_stage_whole(stage, block, sends, potential_wide, initial, keep_sends)
    whole = pl.BlockSpec(block.shape, lambda i: (0, 0, 0, 0))
    edge = pl.BlockSpec((RADIUS, ny, nz, nb), lambda i: (0, 0, 0, 0))
    part = pl.BlockSpec((depth, ny, nz, nb), lambda i: (i, 0, 0, 0))
    low, high = exchange(sends, "domain")
    partial = pl.pallas_call(
        interior_kernel(stage, planes, ny, nz),
        grid=(blocks,),
        in_specs=[whole, part],
        out_specs=part,
        out_shape=jax.ShapeDtypeStruct(block.shape, jnp.float32),
        scratch_shapes=[pltpu.VMEM(block.shape, jnp.float32)],
        name=f"interior_{stage}",
    )(block, potential_wide)
    halos = jnp.concatenate([low, high], axis=0)
    halo_block = pl.BlockSpec((RADIUS, ny, nz, nb), lambda i: (jnp.minimum(i, 1), 0, 0, 0))
    operands = [halos, partial]
    in_specs = [halo_block, part]
    if initial is not None:
        operands.append(initial)
        in_specs.append(part)
    shapes = [jax.ShapeDtypeStruct(block.shape, jnp.bfloat16)]
    out_specs = [part]
    if keep_sends:
        edge_shape = jax.ShapeDtypeStruct((RADIUS, ny, nz, nb), jnp.bfloat16)
        shapes += [edge_shape, edge_shape]
        out_specs += [edge, edge]
    return pl.pallas_call(
        finish_kernel(stage, planes, ny),
        grid=(blocks,),
        in_specs=in_specs,
        out_specs=tuple(out_specs),
        out_shape=tuple(shapes),
        name=f"finish_{stage}",
    )(*operands)


def finish_kernel_whole(stage, planes, ny):
    blocks, depth = plane_blocks(planes)

    def kernel(*refs):
        refs = list(refs)
        low, high, partial = refs[:3]
        initial = refs[3] if stage == "filtered" else None
        outs = refs[4:] if stage == "filtered" else refs[3:]
        out = outs[0]
        step = pl.program_id(0)
        for block in range(blocks):
            @pl.when(step == block)
            def _(block=block):
                for j in range(depth):
                    x = block * depth + j

                    def row(y, carry, x=x, j=j):
                        summed = partial[j, y]
                        for k in range(1, RADIUS + 1):
                            outside = []
                            if x + k >= planes:
                                outside.append(high[x + k - planes, y].astype(jnp.float32))
                            if x - k < 0:
                                outside.append(low[x - k + RADIUS, y].astype(jnp.float32))
                            if outside:
                                term = outside[0] if len(outside) == 1 else outside[0] + outside[1]
                                summed = summed + (-0.5 * stencil_weights[k]) * term
                        if stage == "first":
                            result = summed * first_factor
                        elif stage == "filtered":
                            result = summed * second_factor + (
                                memory_factor * initial[j, y].astype(jnp.float32)
                            )
                        else:
                            result = summed
                        result = result.astype(out.dtype)
                        out[j, y] = result
                        if len(outs) == 3:
                            if x >= planes - RADIUS:
                                outs[1][x - planes + RADIUS, y] = result
                            if x < RADIUS:
                                outs[2][x, y] = result
                        return carry

                    lax.fori_loop(0, ny, row, 0)

    return kernel


def stencil_stage_whole(stage, block, sends, potential_wide, initial=None, keep_sends=True):
    planes, ny, nz, nb = block.shape
    blocks, depth = plane_blocks(planes)
    whole = pl.BlockSpec(block.shape, lambda i: (0, 0, 0, 0))
    edge = pl.BlockSpec((RADIUS, ny, nz, nb), lambda i: (0, 0, 0, 0))
    part = pl.BlockSpec((depth, ny, nz, nb), lambda i: (i, 0, 0, 0))
    low, high = exchange(sends, "domain")
    partial = pl.pallas_call(
        interior_kernel(stage, planes, ny, nz),
        grid=(blocks,),
        in_specs=[whole, part],
        out_specs=part,
        out_shape=jax.ShapeDtypeStruct(block.shape, jnp.float32),
        scratch_shapes=[pltpu.VMEM(block.shape, jnp.float32)],
        name=f"interior_{stage}",
    )(block, potential_wide)
    operands = [low, high, partial]
    in_specs = [edge, edge, part]
    if initial is not None:
        operands.append(initial)
        in_specs.append(part)
    shapes = [jax.ShapeDtypeStruct(block.shape, jnp.bfloat16)]
    out_specs = [part]
    if keep_sends:
        edge_shape = jax.ShapeDtypeStruct((RADIUS, ny, nz, nb), jnp.bfloat16)
        shapes += [edge_shape, edge_shape]
        out_specs += [edge, edge]
    return pl.pallas_call(
        finish_kernel_whole(stage, planes, ny),
        grid=(blocks,),
        in_specs=in_specs,
        out_specs=tuple(out_specs),
        out_shape=tuple(shapes),
        name=f"finish_{stage}",
    )(*operands)


def exchange(sends, axis):
    count = lax.axis_size(axis)
    forward = [(i, (i + 1) % count) for i in range(count)]
    backward = [(target, source) for source, target in forward]
    return lax.ppermute(sends[0], axis, forward), lax.ppermute(sends[1], axis, backward)


def butterfly_sum(values, axis):
    count = lax.axis_size(axis)
    index = lax.axis_index(axis)
    pairs_of = lambda bit: [(i, i ^ bit) for i in range(count)]
    scattered = [1, count // 2] if count >= 4 else [1]
    for bit in scattered:
        half = values.shape[0] // 2
        upper = (index // bit) % 2
        keep = lax.dynamic_slice_in_dim(values, upper * half, half, axis=0)
        send = lax.dynamic_slice_in_dim(values, (1 - upper) * half, half, axis=0)
        values = keep + lax.ppermute(send, axis, pairs_of(bit))
    bit = count // 4
    while bit >= 2:
        values = values + lax.ppermute(values, axis, pairs_of(bit))
        bit //= 2
    for bit in reversed(scattered):
        upper = (index // bit) % 2
        other = lax.ppermute(values, axis, pairs_of(bit))
        values = jnp.where(
            upper == 0,
            jnp.concatenate([values, other], axis=0),
            jnp.concatenate([other, values], axis=0),
        )
    return values


def shards(orbitals, potential):
    planes, ny, nz, nb = orbitals.shape
    potential_wide = jnp.broadcast_to(potential[:, :, :, None], (planes, ny, nz, nb))
    cell_count = planes * ny * nz
    cell_weight = 1.0 / (cell_count * lax.axis_size("domain"))
    band = lax.axis_index("band")
    gram = lambda rows, cols: with_layout_constraint(
        jnp.einsum("cb,ck->bk", rows, cols, preferred_element_type=jnp.float32),
        Layout((0, 1)),
    )
    placed = lambda mine, theirs: jnp.where(
        band == 0,
        jnp.concatenate([mine, theirs], axis=1),
        jnp.concatenate([theirs, mine], axis=1),
    )
    planes_sent = (
        lax.slice_in_dim(orbitals, planes - RADIUS, None, axis=0),
        lax.slice_in_dim(orbitals, 0, RADIUS, axis=0),
    )
    first, *first_sent = stencil_stage("first", orbitals, planes_sent, potential_wide)
    filtered, *filtered_sent = stencil_stage(
        "filtered", first, first_sent, potential_wide, orbitals
    )
    own_block = filtered.reshape(cell_count, nb)
    partner = lax.ppermute(own_block, "band", [(0, 1), (1, 0)])
    correlation_piece = placed(gram(own_block, own_block), gram(own_block, partner))
    correlation = butterfly_sum(correlation_piece, "domain") * cell_weight
    (applied_grid,) = stencil_stage(
        "applied", filtered, filtered_sent, potential_wide, keep_sends=False
    )
    applied = applied_grid.reshape(cell_count, nb)
    energy_piece = placed(gram(applied, own_block), gram(applied, partner))
    projected = butterfly_sum(energy_piece, "domain") * cell_weight
    return (filtered, correlation, projected)


def solution(mesh):
    placed = (P("domain", None, None, "band"), P("domain", None, None))
    return jax.shard_map(
        shards,
        mesh=mesh,
        in_specs=placed,
        out_specs=(P("domain", None, None, "band"), P("band", None), P("band", None)),
        check_vma=False,
    )
```

```python
import jax
import jax.numpy as jnp
from jax import lax
from jax.experimental import pallas as pl
from jax.experimental.pallas import tpu as pltpu
from jax.experimental.layout import Layout, with_layout_constraint
from jax.sharding import PartitionSpec as P

RADIUS = 4


stencil_weights = (-205.0 / 72.0, 8.0 / 5.0, -1.0 / 5.0, 8.0 / 315.0, -1.0 / 560.0)
spectrum_centre = 6.0
first_factor = -0.125
second_factor = -1.0 / 7.0
memory_factor = -1.0 / 7.0


def plane_blocks(planes):
    return (planes // RADIUS, RADIUS) if planes % RADIUS == 0 else (1, planes)


def interior_kernel(stage, planes, ny, nz):
    shift = 0.0 if stage == "applied" else spectrum_centre
    blocks, depth = plane_blocks(planes)

    def kernel(own_narrow, pot, out, own):
        step = pl.program_id(0)

        @pl.when(step == 0)
        def _():
            for x in range(planes):
                own[x] = own_narrow[x].astype(jnp.float32)

        for block in range(blocks):
            @pl.when(step == block)
            def _(block=block):
                for j in range(depth):
                    x = block * depth + j

                    def row(y, carry, x=x, j=j):
                        centre = own[x, y]
                        summed = (3.0 * stencil_weights[0]) * centre
                        for k in range(1, RADIUS + 1):
                            beside = own[x, (y + k) % ny] + own[x, (y + ny - k) % ny]
                            beside = beside + (
                                pltpu.roll(centre, k, 0) + pltpu.roll(centre, nz - k, 0)
                            )
                            if x + k < planes:
                                beside = beside + own[x + k, y]
                            if x - k >= 0:
                                beside = beside + own[x - k, y]
                            summed = summed + stencil_weights[k] * beside
                        applied = -0.5 * summed + pot[j, y] * centre
                        if shift:
                            applied = applied - shift * centre
                        out[j, y] = applied
                        return carry

                    lax.fori_loop(0, ny, row, 0)

    return kernel


def finish_kernel(stage, planes, ny):
    blocks, depth = plane_blocks(planes)

    def kernel(*refs):
        refs = list(refs)
        low, partial = refs[:2]
        high = low
        initial = refs[2] if stage == "filtered" else None
        outs = refs[3:] if stage == "filtered" else refs[2:]
        out = outs[0]
        step = pl.program_id(0)
        for block in range(blocks):
            @pl.when(step == block)
            def _(block=block):
                for j in range(depth):
                    x = block * depth + j

                    def row(y, carry, x=x, j=j):
                        summed = partial[j, y]
                        for k in range(1, RADIUS + 1):
                            outside = []
                            if x + k >= planes:
                                outside.append(high[x + k - planes, y].astype(jnp.float32))
                            if x - k < 0:
                                outside.append(low[x - k + RADIUS, y].astype(jnp.float32))
                            if outside:
                                term = outside[0] if len(outside) == 1 else outside[0] + outside[1]
                                summed = summed + (-0.5 * stencil_weights[k]) * term
                        if stage == "first":
                            result = summed * first_factor
                        elif stage == "filtered":
                            result = summed * second_factor + (
                                memory_factor * initial[j, y].astype(jnp.float32)
                            )
                        else:
                            result = summed
                        result = result.astype(out.dtype)
                        out[j, y] = result
                        if len(outs) == 3:
                            if x >= planes - RADIUS:
                                outs[1][x - planes + RADIUS, y] = result
                            if x < RADIUS:
                                outs[2][x, y] = result
                        return carry

                    lax.fori_loop(0, ny, row, 0)

    return kernel


def stencil_stage(stage, block, sends, potential_wide, initial=None, keep_sends=True):
    planes, ny, nz, nb = block.shape
    blocks, depth = plane_blocks(planes)
    if blocks < 2:
        return stencil_stage_whole(stage, block, sends, potential_wide, initial, keep_sends)
    whole = pl.BlockSpec(block.shape, lambda i: (0, 0, 0, 0))
    edge = pl.BlockSpec((RADIUS, ny, nz, nb), lambda i: (0, 0, 0, 0))
    part = pl.BlockSpec((depth, ny, nz, nb), lambda i: (i, 0, 0, 0))
    low, high = exchange(sends, "domain")
    partial = pl.pallas_call(
        interior_kernel(stage, planes, ny, nz),
        grid=(blocks,),
        in_specs=[whole, part],
        out_specs=part,
        out_shape=jax.ShapeDtypeStruct(block.shape, jnp.float32),
        scratch_shapes=[pltpu.VMEM(block.shape, jnp.float32)],
        name=f"interior_{stage}",
    )(block, potential_wide)
    halos = jnp.concatenate([low, high], axis=0)
    halo_block = pl.BlockSpec((RADIUS, ny, nz, nb), lambda i: (jnp.minimum(i, 1), 0, 0, 0))
    operands = [halos, partial]
    in_specs = [halo_block, part]
    if initial is not None:
        operands.append(initial)
        in_specs.append(part)
    shapes = [jax.ShapeDtypeStruct(block.shape, jnp.bfloat16)]
    out_specs = [part]
    if keep_sends:
        edge_shape = jax.ShapeDtypeStruct((RADIUS, ny, nz, nb), jnp.bfloat16)
        shapes += [edge_shape, edge_shape]
        out_specs += [edge, edge]
    return pl.pallas_call(
        finish_kernel(stage, planes, ny),
        grid=(blocks,),
        in_specs=in_specs,
        out_specs=tuple(out_specs),
        out_shape=tuple(shapes),
        name=f"finish_{stage}",
    )(*operands)


def finish_kernel_whole(stage, planes, ny):
    blocks, depth = plane_blocks(planes)

    def kernel(*refs):
        refs = list(refs)
        low, high, partial = refs[:3]
        initial = refs[3] if stage == "filtered" else None
        outs = refs[4:] if stage == "filtered" else refs[3:]
        out = outs[0]
        step = pl.program_id(0)
        for block in range(blocks):
            @pl.when(step == block)
            def _(block=block):
                for j in range(depth):
                    x = block * depth + j

                    def row(y, carry, x=x, j=j):
                        summed = partial[j, y]
                        for k in range(1, RADIUS + 1):
                            outside = []
                            if x + k >= planes:
                                outside.append(high[x + k - planes, y].astype(jnp.float32))
                            if x - k < 0:
                                outside.append(low[x - k + RADIUS, y].astype(jnp.float32))
                            if outside:
                                term = outside[0] if len(outside) == 1 else outside[0] + outside[1]
                                summed = summed + (-0.5 * stencil_weights[k]) * term
                        if stage == "first":
                            result = summed * first_factor
                        elif stage == "filtered":
                            result = summed * second_factor + (
                                memory_factor * initial[j, y].astype(jnp.float32)
                            )
                        else:
                            result = summed
                        result = result.astype(out.dtype)
                        out[j, y] = result
                        if len(outs) == 3:
                            if x >= planes - RADIUS:
                                outs[1][x - planes + RADIUS, y] = result
                            if x < RADIUS:
                                outs[2][x, y] = result
                        return carry

                    lax.fori_loop(0, ny, row, 0)

    return kernel


def stencil_stage_whole(stage, block, sends, potential_wide, initial=None, keep_sends=True):
    planes, ny, nz, nb = block.shape
    blocks, depth = plane_blocks(planes)
    whole = pl.BlockSpec(block.shape, lambda i: (0, 0, 0, 0))
    edge = pl.BlockSpec((RADIUS, ny, nz, nb), lambda i: (0, 0, 0, 0))
    part = pl.BlockSpec((depth, ny, nz, nb), lambda i: (i, 0, 0, 0))
    low, high = exchange(sends, "domain")
    partial = pl.pallas_call(
        interior_kernel(stage, planes, ny, nz),
        grid=(blocks,),
        in_specs=[whole, part],
        out_specs=part,
        out_shape=jax.ShapeDtypeStruct(block.shape, jnp.float32),
        scratch_shapes=[pltpu.VMEM(block.shape, jnp.float32)],
        name=f"interior_{stage}",
    )(block, potential_wide)
    operands = [low, high, partial]
    in_specs = [edge, edge, part]
    if initial is not None:
        operands.append(initial)
        in_specs.append(part)
    shapes = [jax.ShapeDtypeStruct(block.shape, jnp.bfloat16)]
    out_specs = [part]
    if keep_sends:
        edge_shape = jax.ShapeDtypeStruct((RADIUS, ny, nz, nb), jnp.bfloat16)
        shapes += [edge_shape, edge_shape]
        out_specs += [edge, edge]
    return pl.pallas_call(
        finish_kernel_whole(stage, planes, ny),
        grid=(blocks,),
        in_specs=in_specs,
        out_specs=tuple(out_specs),
        out_shape=tuple(shapes),
        name=f"finish_{stage}",
    )(*operands)


def exchange(sends, axis):
    count = lax.axis_size(axis)
    forward = [(i, (i + 1) % count) for i in range(count)]
    backward = [(target, source) for source, target in forward]
    return lax.ppermute(sends[0], axis, forward), lax.ppermute(sends[1], axis, backward)


def butterfly_sum(values, axis, far_first=True):
    count = lax.axis_size(axis)
    index = lax.axis_index(axis)
    pairs_of = lambda bit: [(i, i ^ bit) for i in range(count)]
    half = values.shape[0] // 2
    upper = index % 2
    keep = lax.dynamic_slice_in_dim(values, upper * half, half, axis=0)
    send = lax.dynamic_slice_in_dim(values, (1 - upper) * half, half, axis=0)
    values = keep + lax.ppermute(send, axis, pairs_of(1))
    bits = []
    bit = count // 2
    while bit >= 2:
        bits.append(bit)
        bit //= 2
    for bit in bits if far_first else reversed(bits):
        values = values + lax.ppermute(values, axis, pairs_of(bit))
    other = lax.ppermute(values, axis, pairs_of(1))
    return jnp.where(
        upper == 0,
        jnp.concatenate([values, other], axis=0),
        jnp.concatenate([other, values], axis=0),
    )


def shards(orbitals, potential):
    planes, ny, nz, nb = orbitals.shape
    potential_wide = jnp.broadcast_to(potential[:, :, :, None], (planes, ny, nz, nb))
    cell_count = planes * ny * nz
    cell_weight = 1.0 / (cell_count * lax.axis_size("domain"))
    band = lax.axis_index("band")
    gram = lambda rows, cols: with_layout_constraint(
        jnp.einsum("cb,ck->bk", rows, cols, preferred_element_type=jnp.float32),
        Layout((0, 1)),
    )
    placed = lambda mine, theirs: jnp.where(
        band == 0,
        jnp.concatenate([mine, theirs], axis=1),
        jnp.concatenate([theirs, mine], axis=1),
    )
    planes_sent = (
        lax.slice_in_dim(orbitals, planes - RADIUS, None, axis=0),
        lax.slice_in_dim(orbitals, 0, RADIUS, axis=0),
    )
    first, *first_sent = stencil_stage("first", orbitals, planes_sent, potential_wide)
    filtered, *filtered_sent = stencil_stage(
        "filtered", first, first_sent, potential_wide, orbitals
    )
    own_block = filtered.reshape(cell_count, nb)
    partner = lax.ppermute(own_block, "band", [(0, 1), (1, 0)])
    correlation_piece = placed(gram(own_block, own_block), gram(own_block, partner))
    correlation = butterfly_sum(correlation_piece, "domain", far_first=False) * cell_weight
    (applied_grid,) = stencil_stage(
        "applied", filtered, filtered_sent, potential_wide, keep_sends=False
    )
    applied = applied_grid.reshape(cell_count, nb)
    energy_piece = placed(gram(applied, own_block), gram(applied, partner))
    projected = butterfly_sum(energy_piece, "domain") * cell_weight
    return (filtered, correlation, projected)


def solution(mesh):
    placed = (P("domain", None, None, "band"), P("domain", None, None))
    return jax.shard_map(
        shards,
        mesh=mesh,
        in_specs=placed,
        out_specs=(P("domain", None, None, "band"), P("band", None), P("band", None)),
        check_vma=False,
    )
```

```python
import jax
import jax.numpy as jnp
from jax import lax
from jax.experimental import pallas as pl
from jax.experimental.pallas import tpu as pltpu
from jax.experimental.layout import Layout, with_layout_constraint
from jax.sharding import PartitionSpec as P

RADIUS = 4


stencil_weights = (-205.0 / 72.0, 8.0 / 5.0, -1.0 / 5.0, 8.0 / 315.0, -1.0 / 560.0)
spectrum_centre = 6.0
first_factor = -0.125
second_factor = -1.0 / 7.0
memory_factor = -1.0 / 7.0


def plane_blocks(planes):
    return (planes // RADIUS, RADIUS) if planes % RADIUS == 0 else (1, planes)


def interior_kernel(stage, planes, ny, nz):
    shift = 0.0 if stage == "applied" else spectrum_centre
    blocks, depth = plane_blocks(planes)

    def kernel(own_narrow, pot, out, own):
        step = pl.program_id(0)

        @pl.when(step == 0)
        def _():
            for x in range(planes):
                own[x] = own_narrow[x].astype(jnp.float32)

        for block in range(blocks):
            @pl.when(step == block)
            def _(block=block):
                for j in range(depth):
                    x = block * depth + j

                    def row(y, carry, x=x, j=j):
                        centre = own[x, y]
                        summed = (3.0 * stencil_weights[0]) * centre
                        for k in range(1, RADIUS + 1):
                            beside = own[x, (y + k) % ny] + own[x, (y + ny - k) % ny]
                            beside = beside + (
                                pltpu.roll(centre, k, 0) + pltpu.roll(centre, nz - k, 0)
                            )
                            if x + k < planes:
                                beside = beside + own[x + k, y]
                            if x - k >= 0:
                                beside = beside + own[x - k, y]
                            summed = summed + stencil_weights[k] * beside
                        applied = -0.5 * summed + pot[j, y] * centre
                        if shift:
                            applied = applied - shift * centre
                        out[j, y] = applied
                        return carry

                    lax.fori_loop(0, ny, row, 0)

    return kernel


def finish_kernel(stage, planes, ny):
    blocks, depth = plane_blocks(planes)

    def kernel(*refs):
        refs = list(refs)
        low, partial = refs[:2]
        high = low
        initial = refs[2] if stage == "filtered" else None
        outs = refs[3:] if stage == "filtered" else refs[2:]
        out = outs[0]
        step = pl.program_id(0)
        for block in range(blocks):
            @pl.when(step == block)
            def _(block=block):
                for j in range(depth):
                    x = block * depth + j

                    def row(y, carry, x=x, j=j):
                        summed = partial[j, y]
                        for k in range(1, RADIUS + 1):
                            outside = []
                            if x + k >= planes:
                                outside.append(high[x + k - planes, y].astype(jnp.float32))
                            if x - k < 0:
                                outside.append(low[x - k + RADIUS, y].astype(jnp.float32))
                            if outside:
                                term = outside[0] if len(outside) == 1 else outside[0] + outside[1]
                                summed = summed + (-0.5 * stencil_weights[k]) * term
                        if stage == "first":
                            result = summed * first_factor
                        elif stage == "filtered":
                            result = summed * second_factor + (
                                memory_factor * initial[j, y].astype(jnp.float32)
                            )
                        else:
                            result = summed
                        result = result.astype(out.dtype)
                        out[j, y] = result
                        if len(outs) == 3:
                            if x >= planes - RADIUS:
                                outs[1][x - planes + RADIUS, y] = result
                            if x < RADIUS:
                                outs[2][x, y] = result
                        return carry

                    lax.fori_loop(0, ny, row, 0)

    return kernel


def stencil_stage(stage, block, sends, potential_wide, initial=None, keep_sends=True):
    planes, ny, nz, nb = block.shape
    blocks, depth = plane_blocks(planes)
    if blocks < 2:
        return stencil_stage_whole(stage, block, sends, potential_wide, initial, keep_sends)
    whole = pl.BlockSpec(block.shape, lambda i: (0, 0, 0, 0))
    edge = pl.BlockSpec((RADIUS, ny, nz, nb), lambda i: (0, 0, 0, 0))
    part = pl.BlockSpec((depth, ny, nz, nb), lambda i: (i, 0, 0, 0))
    low, high = exchange(sends, "domain")
    partial = pl.pallas_call(
        interior_kernel(stage, planes, ny, nz),
        grid=(blocks,),
        in_specs=[whole, part],
        out_specs=part,
        out_shape=jax.ShapeDtypeStruct(block.shape, jnp.float32),
        scratch_shapes=[pltpu.VMEM(block.shape, jnp.float32)],
        name=f"interior_{stage}",
    )(block, potential_wide)
    halos = jnp.concatenate([low, high], axis=0)
    halo_block = pl.BlockSpec((RADIUS, ny, nz, nb), lambda i: (jnp.minimum(i, 1), 0, 0, 0))
    operands = [halos, partial]
    in_specs = [halo_block, part]
    if initial is not None:
        operands.append(initial)
        in_specs.append(part)
    shapes = [jax.ShapeDtypeStruct(block.shape, jnp.bfloat16)]
    out_specs = [part]
    if keep_sends:
        edge_shape = jax.ShapeDtypeStruct((RADIUS, ny, nz, nb), jnp.bfloat16)
        shapes += [edge_shape, edge_shape]
        out_specs += [edge, edge]
    return pl.pallas_call(
        finish_kernel(stage, planes, ny),
        grid=(blocks,),
        in_specs=in_specs,
        out_specs=tuple(out_specs),
        out_shape=tuple(shapes),
        name=f"finish_{stage}",
    )(*operands)


def finish_kernel_whole(stage, planes, ny):
    blocks, depth = plane_blocks(planes)

    def kernel(*refs):
        refs = list(refs)
        low, high, partial = refs[:3]
        initial = refs[3] if stage == "filtered" else None
        outs = refs[4:] if stage == "filtered" else refs[3:]
        out = outs[0]
        step = pl.program_id(0)
        for block in range(blocks):
            @pl.when(step == block)
            def _(block=block):
                for j in range(depth):
                    x = block * depth + j

                    def row(y, carry, x=x, j=j):
                        summed = partial[j, y]
                        for k in range(1, RADIUS + 1):
                            outside = []
                            if x + k >= planes:
                                outside.append(high[x + k - planes, y].astype(jnp.float32))
                            if x - k < 0:
                                outside.append(low[x - k + RADIUS, y].astype(jnp.float32))
                            if outside:
                                term = outside[0] if len(outside) == 1 else outside[0] + outside[1]
                                summed = summed + (-0.5 * stencil_weights[k]) * term
                        if stage == "first":
                            result = summed * first_factor
                        elif stage == "filtered":
                            result = summed * second_factor + (
                                memory_factor * initial[j, y].astype(jnp.float32)
                            )
                        else:
                            result = summed
                        result = result.astype(out.dtype)
                        out[j, y] = result
                        if len(outs) == 3:
                            if x >= planes - RADIUS:
                                outs[1][x - planes + RADIUS, y] = result
                            if x < RADIUS:
                                outs[2][x, y] = result
                        return carry

                    lax.fori_loop(0, ny, row, 0)

    return kernel


def stencil_stage_whole(stage, block, sends, potential_wide, initial=None, keep_sends=True):
    planes, ny, nz, nb = block.shape
    blocks, depth = plane_blocks(planes)
    whole = pl.BlockSpec(block.shape, lambda i: (0, 0, 0, 0))
    edge = pl.BlockSpec((RADIUS, ny, nz, nb), lambda i: (0, 0, 0, 0))
    part = pl.BlockSpec((depth, ny, nz, nb), lambda i: (i, 0, 0, 0))
    low, high = exchange(sends, "domain")
    partial = pl.pallas_call(
        interior_kernel(stage, planes, ny, nz),
        grid=(blocks,),
        in_specs=[whole, part],
        out_specs=part,
        out_shape=jax.ShapeDtypeStruct(block.shape, jnp.float32),
        scratch_shapes=[pltpu.VMEM(block.shape, jnp.float32)],
        name=f"interior_{stage}",
    )(block, potential_wide)
    operands = [low, high, partial]
    in_specs = [edge, edge, part]
    if initial is not None:
        operands.append(initial)
        in_specs.append(part)
    shapes = [jax.ShapeDtypeStruct(block.shape, jnp.bfloat16)]
    out_specs = [part]
    if keep_sends:
        edge_shape = jax.ShapeDtypeStruct((RADIUS, ny, nz, nb), jnp.bfloat16)
        shapes += [edge_shape, edge_shape]
        out_specs += [edge, edge]
    return pl.pallas_call(
        finish_kernel_whole(stage, planes, ny),
        grid=(blocks,),
        in_specs=in_specs,
        out_specs=tuple(out_specs),
        out_shape=tuple(shapes),
        name=f"finish_{stage}",
    )(*operands)


def exchange(sends, axis):
    count = lax.axis_size(axis)
    forward = [(i, (i + 1) % count) for i in range(count)]
    backward = [(target, source) for source, target in forward]
    return lax.ppermute(sends[0], axis, forward), lax.ppermute(sends[1], axis, backward)


def butterfly_sum(values, axis):
    count = lax.axis_size(axis)
    index = lax.axis_index(axis)
    pairs_of = lambda bit: [(i, i ^ bit) for i in range(count)]
    half = values.shape[0] // 2
    upper = index % 2
    keep = lax.dynamic_slice_in_dim(values, upper * half, half, axis=0)
    send = lax.dynamic_slice_in_dim(values, (1 - upper) * half, half, axis=0)
    values = keep + lax.ppermute(send, axis, pairs_of(1))
    bits = []
    bit = count // 2
    while bit >= 2:
        bits.append(bit)
        bit //= 2
    for bit in bits[:1] + bits[1:][::-1]:
        values = values + lax.ppermute(values, axis, pairs_of(bit))
    other = lax.ppermute(values, axis, pairs_of(1))
    return jnp.where(
        upper == 0,
        jnp.concatenate([values, other], axis=0),
        jnp.concatenate([other, values], axis=0),
    )


def shards(orbitals, potential):
    planes, ny, nz, nb = orbitals.shape
    potential_wide = jnp.broadcast_to(potential[:, :, :, None], (planes, ny, nz, nb))
    cell_count = planes * ny * nz
    cell_weight = 1.0 / (cell_count * lax.axis_size("domain"))
    band = lax.axis_index("band")
    gram = lambda rows, cols: with_layout_constraint(
        jnp.einsum("cb,ck->bk", rows, cols, preferred_element_type=jnp.float32),
        Layout((0, 1)),
    )
    placed = lambda mine, theirs: jnp.where(
        band == 0,
        jnp.concatenate([mine, theirs], axis=1),
        jnp.concatenate([theirs, mine], axis=1),
    )
    planes_sent = (
        lax.slice_in_dim(orbitals, planes - RADIUS, None, axis=0),
        lax.slice_in_dim(orbitals, 0, RADIUS, axis=0),
    )
    first, *first_sent = stencil_stage("first", orbitals, planes_sent, potential_wide)
    filtered, *filtered_sent = stencil_stage(
        "filtered", first, first_sent, potential_wide, orbitals
    )
    own_block = filtered.reshape(cell_count, nb)
    partner = lax.ppermute(own_block, "band", [(0, 1), (1, 0)])
    correlation_piece = placed(gram(own_block, own_block), gram(own_block, partner))
    correlation = butterfly_sum(correlation_piece, "domain") * cell_weight
    (applied_grid,) = stencil_stage(
        "applied", filtered, filtered_sent, potential_wide, keep_sends=False
    )
    applied = applied_grid.reshape(cell_count, nb)
    energy_piece = placed(gram(applied, own_block), gram(applied, partner))
    projected = butterfly_sum(energy_piece, "domain") * cell_weight
    return (filtered, correlation, projected)


def solution(mesh):
    placed = (P("domain", None, None, "band"), P("domain", None, None))
    return jax.shard_map(
        shards,
        mesh=mesh,
        in_specs=placed,
        out_specs=(P("domain", None, None, "band"), P("band", None), P("band", None)),
        check_vma=False,
    )
```
